32 devices in a mesh: section: 4 (over z), dp: 2 (over core), seq: 4 (over y, x).
Axes of the slice: x: 2, y: 2, z: 4, core: 2. Of those that a mesh axis runs over, the one named last changes fastest.
Arguments:
- qkv: bfloat16 [4, 4, 256, 6144], P('section', 'dp', 'seq'), may hold values from -5 to 5
- stream_lengths: int32 [4, 4], P('section'), may hold values from 1 to 192, 256 in all within a row
- doc_lengths: int32 [4, 4, 8], P('section'), may hold values from 1 to 128, 256 in all within a row
- hand_over: int32 [4, 2], P('section'), may hold values from 0 to 1
Outputs:
- handoff: bfloat16 [4, 4, 256, 4096], P('section', 'dp', 'seq')
The draws below stay inside these ranges and needn't reach their ends.
Inputs may be any that keep to these rules, and one draw needn't show every extreme that they name: `stream_lengths`: each entry is the length of one row; the 4 entries of one section, taken together, sum to 256, and in each section one entry is exactly the most.
All inputs are finite; a program needn't handle non-finite values.
Results may differ from the reference program's by a relative error of at most 0.0013.
Values may be sent and summed in bfloat16 or wider, within the bound.
No kernel may reach another device: no remote copies, remote signals or barrier semaphores. Data moves between devices by JAX's collectives and lax.ppermute only.
A program may use at most 64 MiB of HBM per device.

```python
import math
import jax
import jax.numpy as jnp
import numpy as np
from jax import lax

H = 32
HD = 128
KV_HEADS = 8
D = 4096
NDOC = 8
SECTIONS = 4
ROWS = 4
LEN = 256
N_DP = 2


def draw_qkv(key, part):
    key_value_width = KV_HEADS * HD
    shape = (SECTIONS, ROWS, LEN, D + 2 * key_value_width)
    key_base = jax.random.fold_in(jax.random.fold_in(key, 11), 0)
    values = jnp.clip(jax.random.normal(key_base, shape, jnp.float32), -5.0, 5.0)
    return values.astype(jnp.bfloat16)


def touch_ends(array, own_key, least, high):
    extent = array.shape
    spot = [jax.random.randint(jax.random.fold_in(own_key, axis), (), 0, extent[axis]) for axis in range(len(extent))]
    array = array.at[tuple(spot)].set(least)
    longest = extent.index(max(extent))
    spot[longest] = (spot[longest] + 1) % extent[longest]
    return array.at[tuple(spot)].set(high)


def split_up(amount, total, reach, lean):
    weights = [(1 << 20) // math.isqrt(grade ** lean) + 1 for grade in range(2, amount + 1)]
    surplus, counts = total - reach - (amount - 1), [1] * (amount - 1)
    while surplus > 0:
        movable = [i for i in range(amount - 1) if counts[i] < reach]
        whole, remaining = sum([weights[i] for i in movable]), surplus
        for i in movable:
            more = min(reach - counts[i], max(1, remaining * weights[i] // whole), surplus)
            counts[i] = counts[i] + more
            surplus = surplus - more
    return np.array([reach] + counts)


def uneven(rng, amount, total, most, slope):
    if amount == 2:
        one = jax.random.randint(rng, (), max(1, total - most), min(most, total - 1) + 1)
        return jnp.stack([one, total - one])
    sizes = jnp.asarray(split_up(amount, total, most, slope), jnp.int32)
    pairs = (amount - 1) // 2
    donor, sink = sizes[1:1 + 2 * pairs:2], sizes[2:2 + 2 * pairs:2]
    slack = jnp.minimum(donor - 1, most - sink)
    shifted = jax.random.randint(jax.random.fold_in(rng, 1), (pairs,), 0, 1 << 20) % (slack + 1)
    sizes = sizes.at[1:1 + 2 * pairs:2].set(donor - shifted).at[2:2 + 2 * pairs:2].set(sink + shifted)
    return sizes[jax.random.permutation(jax.random.fold_in(rng, 2), amount)]


def setup_inputs(seed: int = 0) -> dict:
    seeds = jax.random.split(jax.random.key(seed), 5)
    qkv = draw_qkv(jax.random.fold_in(seeds[4], 71), 0)
    stream_lengths = jax.vmap(lambda own: uneven(own, ROWS, ROWS * LEN // 4, 3 * LEN // 4, 1))(jax.random.split(seeds[1], SECTIONS)).reshape((SECTIONS, ROWS)).astype(jnp.int32)
    doc_lengths = jax.vmap(lambda own: uneven(own, NDOC, LEN, LEN // 2, 1))(jax.random.split(seeds[2], SECTIONS * ROWS)).reshape((SECTIONS, ROWS, NDOC)).astype(jnp.int32)
    hand_over = touch_ends(jax.random.randint(seeds[3], (SECTIONS, N_DP), 0, 2), jax.random.fold_in(seeds[3], 1), 0, 1).astype(jnp.int32)
    return {"qkv": qkv, "stream_lengths": stream_lengths, "doc_lengths": doc_lengths, "hand_over": hand_over}


def attend_row(row_data, doc_ends, unpadded_length):
    group_size = H // KV_HEADS
    key_value_width = KV_HEADS * HD
    queries = row_data[:, :D].astype(jnp.float32).reshape(LEN, KV_HEADS, group_size, HD)
    key_rows = row_data[:, D:D + key_value_width].astype(jnp.float32).reshape(LEN, KV_HEADS, HD)
    value_rows = row_data[:, D + key_value_width:].astype(jnp.float32).reshape(LEN, KV_HEADS, HD)
    positions = jnp.arange(LEN).astype(jnp.int32)
    doc_index = jnp.sum((positions[:, None] >= doc_ends[None, :]).astype(jnp.int32), axis=1)
    allowed = (positions[:, None] >= positions[None, :]) & (doc_index[:, None] == doc_index[None, :])
    scores = jnp.einsum("qkgd,skd->kgqs", queries, key_rows) * (HD ** -0.5)
    masked = jnp.where(allowed, scores, -jnp.inf)
    row_top = jnp.max(masked, axis=-1, keepdims=True)
    weights = jnp.where(allowed, jnp.exp(scores - row_top), 0.0)
    row_total = jnp.sum(weights, axis=-1)
    rounded = weights.astype(jnp.bfloat16).astype(jnp.float32)
    summed = jnp.einsum("kgqs,skd->qkgd", rounded, value_rows)
    result = summed / jnp.transpose(row_total, (2, 0, 1))[..., None]
    valid = (positions < unpadded_length).astype(jnp.float32)
    result = result * valid[:, None, None, None]
    return result.reshape(LEN, D).astype(jnp.bfloat16)


def reference(qkv, stream_lengths, doc_lengths, hand_over):
    doc_ends = jnp.cumsum(doc_lengths, axis=-1).astype(jnp.int32)
    flat_rows = qkv.reshape(SECTIONS * ROWS, LEN, qkv.shape[-1])
    flat_ends = doc_ends.reshape(SECTIONS * ROWS, NDOC)
    flat_lengths = stream_lengths.reshape(SECTIONS * ROWS)
    attention_output = lax.map(lambda item: attend_row(item[0], item[1], item[2]), (flat_rows, flat_ends, flat_lengths))
    attention_output = attention_output.reshape(SECTIONS, ROWS, LEN, D)
    row_numbers = jnp.arange(ROWS).astype(jnp.int32)
    replica = row_numbers // 2
    slot_index = row_numbers % 2
    partner = jnp.bitwise_xor(replica, 1)
    own_pick = hand_over[:, replica]
    partner_pick = hand_over[:, partner]
    sender_replica = jnp.where(slot_index[None, :] == 0, 2 * replica[None, :] + 1 - own_pick, 2 * partner[None, :] + partner_pick).astype(jnp.int32)
    balanced_rows = jnp.take_along_axis(attention_output, sender_replica[:, :, None, None], axis=1)
    return jnp.roll(balanced_rows, 1, axis=0)
```

```python
import jax
import jax.numpy as jnp
from jax import lax
from jax.sharding import PartitionSpec as P

H = 32
HD = 128
KV_HEADS = 8
D = 4096
RPR = 2


def swapped(block, axis, distance):
    count = lax.axis_size(axis)
    route = []
    for low in range(count):
        high = low | 1 << distance
        if high != low and high < count:
            route += [(low, high), (high, low)]
    return lax.ppermute(block, axis, route)


def passed_along(value, axis, steps):
    count = lax.axis_size(axis)
    pairs = [(source, (source + steps) % count) for source in range(count)]
    return lax.ppermute(value, axis, pairs)


def doc_of(positions, ends):
    return jnp.sum((positions[:, None] >= ends[None, :]).astype(jnp.int32), axis=1)


def attend_row(query_rows, key_rows, value_rows, query_pos, key_pos, ends, length):
    seg_len = query_rows.shape[0]
    key_len = key_rows.shape[0]
    group_size = H // KV_HEADS
    query_doc = doc_of(query_pos, ends)
    key_doc = doc_of(key_pos, ends)
    allowed = (key_pos[None, :] <= query_pos[:, None]) & (key_doc[None, :] == query_doc[:, None])
    queries = query_rows.reshape(seg_len, KV_HEADS, group_size, HD)
    keys = key_rows.reshape(key_len, KV_HEADS, HD)
    values = value_rows.reshape(key_len, KV_HEADS, HD)
    scores = (
        jnp.einsum("qkgd,skd->kgqs", queries, keys, preferred_element_type=jnp.float32)
        * HD ** (-0.5)
    )
    row_top = jnp.max(jnp.where(allowed, scores, -jnp.inf), axis=-1, keepdims=True)
    weights = jnp.where(allowed, jnp.exp(scores - row_top), 0.0)
    row_total = jnp.sum(weights, axis=-1)
    rounded = weights.astype(jnp.bfloat16)
    summed = jnp.einsum("kgqs,skd->qkgd", rounded, values, preferred_element_type=jnp.float32)
    result = summed / jnp.transpose(row_total, (2, 0, 1))[..., None]
    valid = (query_pos < length).astype(jnp.float32)
    result = result * valid[:, None, None, None]
    return result.reshape(seg_len, D).astype(jnp.bfloat16)


def shards(qkv, stream_lengths, doc_lengths, hand_over):
    seq_count = lax.axis_size("seq")
    seq_index = lax.axis_index("seq")
    replica = lax.axis_index("dp")
    partner = jnp.bitwise_xor(replica, 1)
    handed = lax.dynamic_index_in_dim(hand_over[0], replica, 0, keepdims=False)
    partner_handed = lax.dynamic_index_in_dim(hand_over[0], partner, 0, keepdims=False)
    own_rows = qkv[0]
    seg_len = own_rows.shape[1]
    doc_ends = jnp.cumsum(doc_lengths[0], axis=1)
    lengths_all = stream_lengths[0]
    given = lax.dynamic_index_in_dim(own_rows, handed, 0, keepdims=True)
    kept = lax.dynamic_index_in_dim(own_rows, 1 - handed, 0, keepdims=True)
    received = swapped(given, "dp", 0)
    rows = jnp.concatenate([kept, received], axis=0)
    row_ids = [2 * replica + 1 - handed, 2 * partner + partner_handed]

    kv_local = rows[..., D:]
    pieces = [kv_local]
    chunk_ids = [seq_index]
    for shift in range(1, seq_count):
        pieces.append(passed_along(kv_local, "seq", shift))
        chunk_ids.append((seq_index - shift) % seq_count)
    kv_all = jnp.concatenate(pieces, axis=1)
    local = jnp.arange(seg_len, dtype=jnp.int32)
    key_pos = jnp.concatenate([chunk * seg_len + local for chunk in chunk_ids])
    query_pos = seq_index * seg_len + local
    key_value_width = KV_HEADS * HD

    results = []
    for slot in range(RPR):
        ends = lax.dynamic_index_in_dim(doc_ends, row_ids[slot], 0, keepdims=False)
        length = lax.dynamic_index_in_dim(lengths_all, row_ids[slot], 0, keepdims=False)
        results.append(
            attend_row(
                rows[slot, :, :D],
                kv_all[slot, :, :key_value_width],
                kv_all[slot, :, key_value_width:],
                query_pos,
                key_pos,
                ends,
                length,
            )
        )
    out = jnp.stack(results, axis=0)
    out = passed_along(out, "section", 1)
    return out.reshape(1, RPR, seg_len, D)


def solution(mesh):
    return jax.shard_map(
        shards,
        mesh=mesh,
        in_specs=(
            P("section", "dp", "seq", None),
            P("section", None),
            P("section", None, None),
            P("section", None),
        ),
        out_specs=P("section", "dp", "seq", None),
        check_vma=False,
    )
```

```python
import jax
import jax.numpy as jnp
from jax import lax
from jax.sharding import PartitionSpec as P

H = 32
HD = 128
KV_HEADS = 8
D = 4096
RPR = 2


def swapped(block, axis, distance):
    count = lax.axis_size(axis)
    route = []
    for low in range(count):
        high = low | 1 << distance
        if high != low and high < count:
            route += [(low, high), (high, low)]
    return lax.ppermute(block, axis, route)


def passed_along(value, axis, steps):
    count = lax.axis_size(axis)
    pairs = [(source, (source + steps) % count) for source in range(count)]
    return lax.ppermute(value, axis, pairs)


def doc_of(positions, ends):
    return jnp.sum((positions[:, None] >= ends[None, :]).astype(jnp.int32), axis=1)


def attend_row(query_rows, key_rows, value_rows, query_pos, key_pos, ends, length):
    seg_len = query_rows.shape[0]
    key_len = key_rows.shape[0]
    group_size = H // KV_HEADS
    query_doc = doc_of(query_pos, ends)
    key_doc = doc_of(key_pos, ends)
    allowed = (key_pos[None, :] <= query_pos[:, None]) & (key_doc[None, :] == query_doc[:, None])
    queries = query_rows.reshape(seg_len, KV_HEADS, group_size, HD)
    keys = key_rows.reshape(key_len, KV_HEADS, HD)
    values = value_rows.reshape(key_len, KV_HEADS, HD)
    scores = (
        jnp.einsum("qkgd,skd->kgqs", queries, keys, preferred_element_type=jnp.float32)
        * HD ** (-0.5)
    )
    row_top = jnp.max(jnp.where(allowed, scores, -jnp.inf), axis=-1, keepdims=True)
    weights = jnp.where(allowed, jnp.exp(scores - row_top), 0.0)
    row_total = jnp.sum(weights, axis=-1)
    rounded = weights.astype(jnp.bfloat16)
    summed = jnp.einsum("kgqs,skd->qkgd", rounded, values, preferred_element_type=jnp.float32)
    result = summed / jnp.transpose(row_total, (2, 0, 1))[..., None]
    valid = (query_pos < length).astype(jnp.float32)
    result = result * valid[:, None, None, None]
    return result.reshape(seg_len, D).astype(jnp.bfloat16)


def shards(qkv, stream_lengths, doc_lengths, hand_over):
    seq_count = lax.axis_size("seq")
    seq_index = lax.axis_index("seq")
    replica = lax.axis_index("dp")
    partner = jnp.bitwise_xor(replica, 1)
    handed = lax.dynamic_index_in_dim(hand_over[0], replica, 0, keepdims=False)
    partner_handed = lax.dynamic_index_in_dim(hand_over[0], partner, 0, keepdims=False)
    own_rows = qkv[0]
    seg_len = own_rows.shape[1]
    length_all = seg_len * seq_count
    doc_ends = jnp.cumsum(doc_lengths[0], axis=1)
    lengths_all = stream_lengths[0]
    given = lax.dynamic_index_in_dim(own_rows, handed, 0, keepdims=False)
    kept = lax.dynamic_index_in_dim(own_rows, 1 - handed, 0, keepdims=False)
    received = swapped(given, "dp", 0)
    row_ids = [2 * replica + 1 - handed, 2 * partner + partner_handed]
    reach = min(seq_count - 1, -(-(length_all // 2 - 1) // seg_len))
    local = jnp.arange(seg_len, dtype=jnp.int32)
    query_pos = seq_index * seg_len + local
    key_value_width = KV_HEADS * HD
    far = jnp.int32(4 * length_all)

    outs = []
    for slot, row in enumerate([kept, received]):
        kv_local = row[:, D:]
        pieces = [kv_local]
        key_pos = [query_pos]
        for shift in range(1, reach + 1):
            pairs = [(source, source + shift) for source in range(seq_count - shift)]
            pieces.append(lax.ppermute(kv_local, "seq", pairs))
            chunk = seq_index - shift
            key_pos.append(jnp.where(chunk >= 0, chunk * seg_len + local, far))
        kv_all = jnp.concatenate(pieces, axis=0)
        key_pos = jnp.concatenate(key_pos)
        ends = lax.dynamic_index_in_dim(doc_ends, row_ids[slot], 0, keepdims=False)
        length = lax.dynamic_index_in_dim(lengths_all, row_ids[slot], 0, keepdims=False)
        result = attend_row(
            row[:, :D],
            kv_all[:, :key_value_width],
            kv_all[:, key_value_width:],
            query_pos,
            key_pos,
            ends,
            length,
        )
        outs.append(passed_along(result, "section", 1))
    out = jnp.stack(outs, axis=0)
    return out.reshape(1, RPR, seg_len, D)


def solution(mesh):
    return jax.shard_map(
        shards,
        mesh=mesh,
        in_specs=(
            P("section", "dp", "seq", None),
            P("section", None),
            P("section", None, None),
            P("section", None),
        ),
        out_specs=P("section", "dp", "seq", None),
        check_vma=False,
    )
```

```python
import jax
import jax.numpy as jnp
from jax import lax
from jax.sharding import PartitionSpec as P

H = 32
HD = 128
KV_HEADS = 8
D = 4096
RPR = 2


def swapped(block, axis, distance):
    count = lax.axis_size(axis)
    route = []
    for low in range(count):
        high = low | 1 << distance
        if high != low and high < count:
            route += [(low, high), (high, low)]
    return lax.ppermute(block, axis, route)


def passed_along(value, axis, steps):
    count = lax.axis_size(axis)
    pairs = [(source, (source + steps) % count) for source in range(count)]
    return lax.ppermute(value, axis, pairs)


def doc_of(positions, ends):
    return jnp.sum((positions[:, None] >= ends[None, :]).astype(jnp.int32), axis=1)


def attend_row(query_rows, key_rows, value_rows, query_pos, key_pos, ends, length):
    seg_len = query_rows.shape[0]
    key_len = key_rows.shape[0]
    group_size = H // KV_HEADS
    query_doc = doc_of(query_pos, ends)
    key_doc = doc_of(key_pos, ends)
    allowed = (key_pos[None, :] <= query_pos[:, None]) & (key_doc[None, :] == query_doc[:, None])
    queries = query_rows.reshape(seg_len, KV_HEADS, group_size, HD)
    keys = key_rows.reshape(key_len, KV_HEADS, HD)
    values = value_rows.reshape(key_len, KV_HEADS, HD)
    scores = (
        jnp.einsum("qkgd,skd->kgqs", queries, keys, preferred_element_type=jnp.float32)
        * HD ** (-0.5)
    )
    row_top = jnp.max(jnp.where(allowed, scores, -jnp.inf), axis=-1, keepdims=True)
    weights = jnp.where(allowed, jnp.exp(scores - row_top), 0.0)
    row_total = jnp.sum(weights, axis=-1)
    rounded = weights.astype(jnp.bfloat16)
    summed = jnp.einsum("kgqs,skd->qkgd", rounded, values, preferred_element_type=jnp.float32)
    result = summed / jnp.transpose(row_total, (2, 0, 1))[..., None]
    valid = (query_pos < length).astype(jnp.float32)
    result = result * valid[:, None, None, None]
    return result.reshape(seg_len, D).astype(jnp.bfloat16)


def gathered(block, seq_index, seq_count, reach):
    if seq_count == 4 and reach == 2:
        over_x = lax.ppermute(block, "seq", [(0, 1), (2, 3)])
        over_y = lax.ppermute(block, "seq", [(0, 2), (1, 3)])
        relayed = lax.ppermute(over_y, "seq", [(3, 2)])
        odd = seq_index % 2 == 1
        return [
            (over_x, jnp.where(odd, seq_index - 1, -1)),
            (over_y, seq_index - 2),
            (relayed, jnp.where(seq_index == 2, 1, -1)),
        ]
    pieces = []
    for shift in range(1, reach + 1):
        pairs = [(source, source + shift) for source in range(seq_count - shift)]
        pieces.append((lax.ppermute(block, "seq", pairs), seq_index - shift))
    return pieces


def shards(qkv, stream_lengths, doc_lengths, hand_over):
    seq_count = lax.axis_size("seq")
    seq_index = lax.axis_index("seq")
    replica = lax.axis_index("dp")
    partner = jnp.bitwise_xor(replica, 1)
    handed = lax.dynamic_index_in_dim(hand_over[0], replica, 0, keepdims=False)
    own_rows = qkv[0]
    seg_len = own_rows.shape[1]
    length_all = seg_len * seq_count
    doc_ends = jnp.cumsum(doc_lengths[0], axis=1)
    lengths_all = stream_lengths[0]
    reach = min(seq_count - 1, -(-(length_all // 2 - 1) // seg_len))
    local = jnp.arange(seg_len, dtype=jnp.int32)
    query_pos = seq_index * seg_len + local
    key_value_width = KV_HEADS * HD
    far = jnp.int32(4 * length_all)

    outs = []
    for own_index in [1 - handed, handed]:
        row = lax.dynamic_index_in_dim(own_rows, own_index, 0, keepdims=False)
        kv_local = row[:, D:]
        pieces = [kv_local]
        key_pos = [query_pos]
        for piece, chunk in gathered(kv_local, seq_index, seq_count, reach):
            pieces.append(piece)
            key_pos.append(jnp.where(chunk >= 0, chunk * seg_len + local, far))
        kv_all = jnp.concatenate(pieces, axis=0)
        key_pos = jnp.concatenate(key_pos)
        row_id = 2 * replica + own_index
        ends = lax.dynamic_index_in_dim(doc_ends, row_id, 0, keepdims=False)
        length = lax.dynamic_index_in_dim(lengths_all, row_id, 0, keepdims=False)
        outs.append(
            attend_row(
                row[:, :D],
                kv_all[:, :key_value_width],
                kv_all[:, key_value_width:],
                query_pos,
                key_pos,
                ends,
                length,
            )
        )
    kept_out, given_out = outs
    sent = [passed_along(kept_out, "section", 1)]
    received = swapped(given_out, "dp", 0)
    sent.append(passed_along(received, "section", 1))
    out = jnp.stack(sent, axis=0)
    return out.reshape(1, RPR, seg_len, D)


def solution(mesh):
    return jax.shard_map(
        shards,
        mesh=mesh,
        in_specs=(
            P("section", "dp", "seq", None),
            P("section", None),
            P("section", None, None),
            P("section", None),
        ),
        out_specs=P("section", "dp", "seq", None),
        check_vma=False,
    )
```

```python
import jax
import jax.numpy as jnp
from jax import lax
from jax.sharding import PartitionSpec as P

H = 32
HD = 128
KV_HEADS = 8
D = 4096
RPR = 2


def swapped(block, axis, distance):
    count = lax.axis_size(axis)
    route = []
    for low in range(count):
        high = low | 1 << distance
        if high != low and high < count:
            route += [(low, high), (high, low)]
    return lax.ppermute(block, axis, route)


def passed_along(value, axis, steps):
    count = lax.axis_size(axis)
    pairs = [(source, (source + steps) % count) for source in range(count)]
    return lax.ppermute(value, axis, pairs)


def doc_of(positions, ends):
    return jnp.sum((positions[:, None] >= ends[None, :]).astype(jnp.int32), axis=1)


def attend_row(query_rows, key_rows, value_rows, query_pos, key_pos, ends, length):
    seg_len = query_rows.shape[0]
    key_len = key_rows.shape[0]
    group_size = H // KV_HEADS
    query_doc = doc_of(query_pos, ends)
    key_doc = doc_of(key_pos, ends)
    allowed = (key_pos[None, :] <= query_pos[:, None]) & (key_doc[None, :] == query_doc[:, None])
    queries = query_rows.reshape(seg_len, KV_HEADS, group_size, HD)
    keys = key_rows.reshape(key_len, KV_HEADS, HD)
    values = value_rows.reshape(key_len, KV_HEADS, HD)
    scores = (
        jnp.einsum("qkgd,skd->kgqs", queries, keys, preferred_element_type=jnp.float32)
        * HD ** (-0.5)
    )
    row_top = jnp.max(jnp.where(allowed, scores, -jnp.inf), axis=-1, keepdims=True)
    weights = jnp.where(allowed, jnp.exp(scores - row_top), 0.0)
    row_total = jnp.sum(weights, axis=-1)
    rounded = weights.astype(jnp.bfloat16)
    summed = jnp.einsum("kgqs,skd->qkgd", rounded, values, preferred_element_type=jnp.float32)
    result = summed / jnp.transpose(row_total, (2, 0, 1))[..., None]
    valid = (query_pos < length).astype(jnp.float32)
    result = result * valid[:, None, None, None]
    return result.reshape(seg_len, D).astype(jnp.bfloat16)


def gathered(block, seq_index, seq_count, reach):
    if seq_count == 4 and reach == 2:
        over_x = lax.ppermute(block, "seq", [(0, 1), (2, 3)])
        over_y = lax.ppermute(block, "seq", [(0, 2), (1, 3)])
        relayed = lax.ppermute(over_y, "seq", [(3, 2)])
        odd = seq_index % 2 == 1
        return [
            (over_x, jnp.where(odd, seq_index - 1, -1)),
            (over_y, seq_index - 2),
            (relayed, jnp.where(seq_index == 2, 1, -1)),
        ]
    pieces = []
    for shift in range(1, reach + 1):
        pairs = [(source, source + shift) for source in range(seq_count - shift)]
        pieces.append((lax.ppermute(block, "seq", pairs), seq_index - shift))
    return pieces


def shards(qkv, stream_lengths, doc_lengths, hand_over):
    seq_count = lax.axis_size("seq")
    seq_index = lax.axis_index("seq")
    replica = lax.axis_index("dp")
    partner = jnp.bitwise_xor(replica, 1)
    handed = lax.dynamic_index_in_dim(hand_over[0], replica, 0, keepdims=False)
    own_rows = qkv[0]
    seg_len = own_rows.shape[1]
    length_all = seg_len * seq_count
    doc_ends = jnp.cumsum(doc_lengths[0], axis=1)
    lengths_all = stream_lengths[0]
    reach = min(seq_count - 1, -(-(length_all // 2 - 1) // seg_len))
    local = jnp.arange(seg_len, dtype=jnp.int32)
    query_pos = seq_index * seg_len + local
    key_value_width = KV_HEADS * HD
    far = jnp.int32(4 * length_all)

    def prepare(own_index):
        row = lax.dynamic_index_in_dim(own_rows, own_index, 0, keepdims=False)
        kv_local = row[:, D:]
        return row, kv_local

    def attend_own(row, kv_local, pieces_and_chunks, own_index):
        pieces = [kv_local]
        key_pos = [query_pos]
        for piece, chunk in pieces_and_chunks:
            pieces.append(piece)
            key_pos.append(jnp.where(chunk >= 0, chunk * seg_len + local, far))
        kv_all = jnp.concatenate(pieces, axis=0)
        key_pos = jnp.concatenate(key_pos)
        row_id = 2 * replica + own_index
        ends = lax.dynamic_index_in_dim(doc_ends, row_id, 0, keepdims=False)
        length = lax.dynamic_index_in_dim(lengths_all, row_id, 0, keepdims=False)
        return attend_row(
            row[:, :D],
            kv_all[:, :key_value_width],
            kv_all[:, key_value_width:],
            query_pos,
            key_pos,
            ends,
            length,
        )

    kept_row, kept_kv = prepare(1 - handed)
    given_row, given_kv = prepare(handed)
    kept_pieces = gathered(kept_kv, seq_index, seq_count, reach)
    given_kv = lax.optimization_barrier((given_kv, kept_pieces[0][0], kept_pieces[1][0]))[0]
    given_pieces = gathered(given_kv, seq_index, seq_count, reach)
    kept_out = attend_own(kept_row, kept_kv, kept_pieces, 1 - handed)
    sent = [passed_along(kept_out, "section", 1)]
    given_row = lax.optimization_barrier((given_row, kept_out))[0]
    given_out = attend_own(given_row, given_kv, given_pieces, handed)
    sections = lax.axis_size("section")
    replicas = lax.axis_size("dp")
    pairs = []
    for section in range(sections):
        for rep in range(replicas):
            pairs.append(
                (section * replicas + rep, (section + 1) % sections * replicas + (rep ^ 1))
            )
    sent.append(lax.ppermute(given_out, ("section", "dp"), pairs))
    out = jnp.stack(sent, axis=0)
    return out.reshape(1, RPR, seg_len, D)


def solution(mesh):
    return jax.shard_map(
        shards,
        mesh=mesh,
        in_specs=(
            P("section", "dp", "seq", None),
            P("section", None),
            P("section", None, None),
            P("section", None),
        ),
        out_specs=P("section", "dp", "seq", None),
        check_vma=False,
    )
```

```python
import jax
import jax.numpy as jnp
from jax import lax
from jax.sharding import PartitionSpec as P

H = 32
HD = 128
KV_HEADS = 8
D = 4096
RPR = 2


def swapped(block, axis, distance):
    count = lax.axis_size(axis)
    route = []
    for low in range(count):
        high = low | 1 << distance
        if high != low and high < count:
            route += [(low, high), (high, low)]
    return lax.ppermute(block, axis, route)


def passed_along(value, axis, steps):
    count = lax.axis_size(axis)
    pairs = [(source, (source + steps) % count) for source in range(count)]
    return lax.ppermute(value, axis, pairs)


def doc_of(positions, ends):
    return jnp.sum((positions[:, None] >= ends[None, :]).astype(jnp.int32), axis=1)


def attend_row(query_rows, key_rows, value_rows, query_pos, key_pos, ends, length):
    seg_len = query_rows.shape[0]
    key_len = key_rows.shape[0]
    group_size = H // KV_HEADS
    query_doc = doc_of(query_pos, ends)
    key_doc = doc_of(key_pos, ends)
    allowed = (key_pos[None, :] <= query_pos[:, None]) & (key_doc[None, :] == query_doc[:, None])
    queries = query_rows.reshape(seg_len, KV_HEADS, group_size, HD)
    keys = key_rows.reshape(key_len, KV_HEADS, HD)
    values = value_rows.reshape(key_len, KV_HEADS, HD)
    scores = (
        jnp.einsum("qkgd,skd->kgqs", queries, keys, preferred_element_type=jnp.float32)
        * HD ** (-0.5)
    )
    row_top = jnp.max(jnp.where(allowed, scores, -jnp.inf), axis=-1, keepdims=True)
    weights = jnp.where(allowed, jnp.exp(scores - row_top), 0.0)
    row_total = jnp.sum(weights, axis=-1)
    rounded = weights.astype(jnp.bfloat16)
    summed = jnp.einsum("kgqs,skd->qkgd", rounded, values, preferred_element_type=jnp.float32)
    result = summed / jnp.transpose(row_total, (2, 0, 1))[..., None]
    valid = (query_pos < length).astype(jnp.float32)
    result = result * valid[:, None, None, None]
    return result.reshape(seg_len, D).astype(jnp.bfloat16)


def gathered(block, seq_index, seq_count, reach):
    if seq_count == 4 and reach == 2:
        over_y = lax.ppermute(block, "seq", [(j, j ^ 2) for j in range(4)])
        odd = seq_index % 2 == 1
        onward = jnp.where(odd, over_y, block)
        over_x = lax.ppermute(onward, "seq", [(j, j ^ 1) for j in range(4)])
        return [
            (over_y, jnp.bitwise_xor(seq_index, 2)),
            (over_x, jnp.where(odd, seq_index - 1, jnp.bitwise_xor(seq_index, 3))),
        ]
    pieces = []
    for shift in range(1, reach + 1):
        pairs = [(source, source + shift) for source in range(seq_count - shift)]
        pieces.append((lax.ppermute(block, "seq", pairs), seq_index - shift))
    return pieces


def shards(qkv, stream_lengths, doc_lengths, hand_over):
    seq_count = lax.axis_size("seq")
    seq_index = lax.axis_index("seq")
    replica = lax.axis_index("dp")
    partner = jnp.bitwise_xor(replica, 1)
    handed = lax.dynamic_index_in_dim(hand_over[0], replica, 0, keepdims=False)
    own_rows = qkv[0]
    seg_len = own_rows.shape[1]
    length_all = seg_len * seq_count
    doc_ends = jnp.cumsum(doc_lengths[0], axis=1)
    lengths_all = stream_lengths[0]
    reach = min(seq_count - 1, -(-(length_all // 2 - 1) // seg_len))
    local = jnp.arange(seg_len, dtype=jnp.int32)
    query_pos = seq_index * seg_len + local
    key_value_width = KV_HEADS * HD
    far = jnp.int32(4 * length_all)

    def prepare(own_index):
        row = lax.dynamic_index_in_dim(own_rows, own_index, 0, keepdims=False)
        kv_local = row[:, D:]
        return row, kv_local

    def attend_own(row, kv_local, pieces_and_chunks, own_index):
        pieces = [kv_local]
        key_pos = [query_pos]
        for piece, chunk in pieces_and_chunks:
            pieces.append(piece)
            key_pos.append(jnp.where(chunk >= 0, chunk * seg_len + local, far))
        kv_all = jnp.concatenate(pieces, axis=0)
        key_pos = jnp.concatenate(key_pos)
        row_id = 2 * replica + own_index
        ends = lax.dynamic_index_in_dim(doc_ends, row_id, 0, keepdims=False)
        length = lax.dynamic_index_in_dim(lengths_all, row_id, 0, keepdims=False)
        return attend_row(
            row[:, :D],
            kv_all[:, :key_value_width],
            kv_all[:, key_value_width:],
            query_pos,
            key_pos,
            ends,
            length,
        )

    kept_row, kept_kv = prepare(1 - handed)
    given_row, given_kv = prepare(handed)
    kept_pieces = gathered(kept_kv, seq_index, seq_count, reach)
    given_kv = lax.optimization_barrier((given_kv, kept_pieces[0][0]))[0]
    given_pieces = gathered(given_kv, seq_index, seq_count, reach)
    kept_out = attend_own(kept_row, kept_kv, kept_pieces, 1 - handed)
    sent = [passed_along(kept_out, "section", 1)]
    given_row = lax.optimization_barrier((given_row, kept_out))[0]
    given_out = attend_own(given_row, given_kv, given_pieces, handed)
    sections = lax.axis_size("section")
    replicas = lax.axis_size("dp")
    pairs = []
    for section in range(sections):
        for rep in range(replicas):
            pairs.append(
                (section * replicas + rep, (section + 1) % sections * replicas + (rep ^ 1))
            )
    sent.append(lax.ppermute(given_out, ("section", "dp"), pairs))
    out = jnp.stack(sent, axis=0)
    return out.reshape(1, RPR, seg_len, D)


def solution(mesh):
    return jax.shard_map(
        shards,
        mesh=mesh,
        in_specs=(
            P("section", "dp", "seq", None),
            P("section", None),
            P("section", None, None),
            P("section", None),
        ),
        out_specs=P("section", "dp", "seq", None),
        check_vma=False,
    )
```

```python
import jax
import jax.numpy as jnp
from jax import lax
from jax.sharding import PartitionSpec as P

H = 32
HD = 128
KV_HEADS = 8
D = 4096
RPR = 2


def swapped(block, axis, distance):
    count = lax.axis_size(axis)
    route = []
    for low in range(count):
        high = low | 1 << distance
        if high != low and high < count:
            route += [(low, high), (high, low)]
    return lax.ppermute(block, axis, route)


def passed_along(value, axis, steps):
    count = lax.axis_size(axis)
    pairs = [(source, (source + steps) % count) for source in range(count)]
    return lax.ppermute(value, axis, pairs)


def doc_of(positions, ends):
    return jnp.sum((positions[:, None] >= ends[None, :]).astype(jnp.int32), axis=1)


def attend_row(query_rows, key_rows, value_rows, query_pos, key_pos, ends, length):
    seg_len = query_rows.shape[0]
    key_len = key_rows.shape[0]
    group_size = H // KV_HEADS
    query_doc = doc_of(query_pos, ends)
    key_doc = doc_of(key_pos, ends)
    allowed = (key_pos[None, :] <= query_pos[:, None]) & (key_doc[None, :] == query_doc[:, None])
    queries = query_rows.reshape(seg_len, KV_HEADS, group_size, HD)
    keys = key_rows.reshape(key_len, KV_HEADS, HD)
    values = value_rows.reshape(key_len, KV_HEADS, HD)
    scores = (
        jnp.einsum("qkgd,skd->kgqs", queries, keys, preferred_element_type=jnp.float32)
        * HD ** (-0.5)
    )
    row_top = jnp.max(jnp.where(allowed, scores, -jnp.inf), axis=-1, keepdims=True)
    weights = jnp.where(allowed, jnp.exp(scores - row_top), 0.0)
    row_total = jnp.sum(weights, axis=-1)
    rounded = weights.astype(jnp.bfloat16)
    summed = jnp.einsum("kgqs,skd->qkgd", rounded, values, preferred_element_type=jnp.float32)
    result = summed / jnp.transpose(row_total, (2, 0, 1))[..., None]
    valid = (query_pos < length).astype(jnp.float32)
    result = result * valid[:, None, None, None]
    return result.reshape(seg_len, D).astype(jnp.bfloat16)


def gathered(block, seq_index, seq_count, reach):
    if seq_count == 4 and reach == 2:
        over_y = lax.ppermute(block, "seq", [(j, j ^ 2) for j in range(4)])
        odd = seq_index % 2 == 1
        onward = jnp.where(odd, over_y, block)
        over_x = lax.ppermute(onward, "seq", [(j, j ^ 1) for j in range(4)])
        return [
            (over_y, jnp.bitwise_xor(seq_index, 2)),
            (over_x, jnp.where(odd, seq_index - 1, jnp.bitwise_xor(seq_index, 3))),
        ]
    pieces = []
    for shift in range(1, reach + 1):
        pairs = [(source, source + shift) for source in range(seq_count - shift)]
        pieces.append((lax.ppermute(block, "seq", pairs), seq_index - shift))
    return pieces


def shards(qkv, stream_lengths, doc_lengths, hand_over):
    seq_count = lax.axis_size("seq")
    seq_index = lax.axis_index("seq")
    replica = lax.axis_index("dp")
    partner = jnp.bitwise_xor(replica, 1)
    own_rows = qkv[0]
    seg_len = own_rows.shape[1]
    length_all = seg_len * seq_count
    doc_ends = jnp.cumsum(doc_lengths[0], axis=1)
    lengths_all = stream_lengths[0]
    reach = min(seq_count - 1, -(-(length_all // 2 - 1) // seg_len))
    local = jnp.arange(seg_len, dtype=jnp.int32)
    query_pos = seq_index * seg_len + local
    key_value_width = KV_HEADS * HD
    far = jnp.int32(4 * length_all)

    def attend_own(row, kv_local, pieces_and_chunks, own_index):
        pieces = [kv_local]
        key_pos = [query_pos]
        for piece, chunk in pieces_and_chunks:
            pieces.append(piece)
            key_pos.append(jnp.where(chunk >= 0, chunk * seg_len + local, far))
        kv_all = jnp.concatenate(pieces, axis=0)
        key_pos = jnp.concatenate(key_pos)
        row_id = 2 * replica + own_index
        ends = lax.dynamic_index_in_dim(doc_ends, row_id, 0, keepdims=False)
        length = lax.dynamic_index_in_dim(lengths_all, row_id, 0, keepdims=False)
        return attend_row(
            row[:, :D],
            kv_all[:, :key_value_width],
            kv_all[:, key_value_width:],
            query_pos,
            key_pos,
            ends,
            length,
        )

    first_row, second_row = own_rows[0], own_rows[1]
    first_kv = first_row[:, D:]
    first_pieces = gathered(first_kv, seq_index, seq_count, reach)
    second_kv = lax.optimization_barrier((second_row[:, D:], first_pieces[0][0]))[0]
    second_pieces = gathered(second_kv, seq_index, seq_count, reach)
    first_out = attend_own(first_row, first_kv, first_pieces, 0)
    first_next = passed_along(first_out, "section", 1)
    second_row = lax.optimization_barrier((second_row, first_out))[0]
    second_out = attend_own(second_row, second_kv, second_pieces, 1)
    second_next = passed_along(second_out, "section", 1)

    previous_hand = passed_along(hand_over[0], "section", 1)
    own_hand = lax.dynamic_index_in_dim(previous_hand, replica, 0, keepdims=False)
    partner_hand = lax.dynamic_index_in_dim(previous_hand, partner, 0, keepdims=False)
    partner_first = swapped(first_next, "dp", 0)
    partner_second = swapped(second_next, "dp", 0)
    sent = [
        jnp.where(own_hand == 1, first_next, second_next),
        jnp.where(partner_hand == 0, partner_first, partner_second),
    ]
    out = jnp.stack(sent, axis=0)
    return out.reshape(1, RPR, seg_len, D)


def solution(mesh):
    return jax.shard_map(
        shards,
        mesh=mesh,
        in_specs=(
            P("section", "dp", "seq", None),
            P("section", None),
            P("section", None, None),
            P("section", None),
        ),
        out_specs=P("section", "dp", "seq", None),
        check_vma=False,
    )
```

```python
import jax
import jax.numpy as jnp
from jax import lax
from jax.sharding import PartitionSpec as P

H = 32
HD = 128
KV_HEADS = 8
D = 4096
RPR = 2


def swapped(block, axis, distance):
    count = lax.axis_size(axis)
    route = []
    for low in range(count):
        high = low | 1 << distance
        if high != low and high < count:
            route += [(low, high), (high, low)]
    return lax.ppermute(block, axis, route)


def passed_along(value, axis, steps):
    count = lax.axis_size(axis)
    pairs = [(source, (source + steps) % count) for source in range(count)]
    return lax.ppermute(value, axis, pairs)


def doc_of(positions, ends):
    return jnp.sum((positions[:, None] >= ends[None, :]).astype(jnp.int32), axis=1)


def attend_row(query_rows, key_rows, value_rows, query_pos, key_pos, ends, length):
    seg_len = query_rows.shape[0]
    key_len = key_rows.shape[0]
    group_size = H // KV_HEADS
    query_doc = doc_of(query_pos, ends)
    key_doc = doc_of(key_pos, ends)
    allowed = (key_pos[None, :] <= query_pos[:, None]) & (key_doc[None, :] == query_doc[:, None])
    queries = query_rows.reshape(seg_len, KV_HEADS, group_size, HD)
    keys = key_rows.reshape(key_len, KV_HEADS, HD)
    values = value_rows.reshape(key_len, KV_HEADS, HD)
    scores = (
        jnp.einsum("qkgd,skd->kgqs", queries, keys, preferred_element_type=jnp.float32)
        * HD ** (-0.5)
    )
    row_top = jnp.max(jnp.where(allowed, scores, -jnp.inf), axis=-1, keepdims=True)
    weights = jnp.where(allowed, jnp.exp(scores - row_top), 0.0)
    row_total = jnp.sum(weights, axis=-1)
    rounded = weights.astype(jnp.bfloat16)
    summed = jnp.einsum("kgqs,skd->qkgd", rounded, values, preferred_element_type=jnp.float32)
    result = summed / jnp.transpose(row_total, (2, 0, 1))[..., None]
    valid = (query_pos < length).astype(jnp.float32)
    result = result * valid[:, None, None, None]
    return result.reshape(seg_len, D).astype(jnp.bfloat16)


def gathered(block, seq_index, seq_count, reach):
    if seq_count == 4 and reach == 2:
        over_y = lax.ppermute(block, "seq", [(j, j ^ 2) for j in range(4)])
        odd = seq_index % 2 == 1
        onward = jnp.where(odd, over_y, block)
        over_x = lax.ppermute(onward, "seq", [(j, j ^ 1) for j in range(4)])
        return [
            (over_y, jnp.bitwise_xor(seq_index, 2)),
            (over_x, jnp.where(odd, seq_index - 1, jnp.bitwise_xor(seq_index, 3))),
        ]
    pieces = []
    for shift in range(1, reach + 1):
        pairs = [(source, source + shift) for source in range(seq_count - shift)]
        pieces.append((lax.ppermute(block, "seq", pairs), seq_index - shift))
    return pieces


def shards(qkv, stream_lengths, doc_lengths, hand_over):
    seq_count = lax.axis_size("seq")
    seq_index = lax.axis_index("seq")
    replica = lax.axis_index("dp")
    partner = jnp.bitwise_xor(replica, 1)
    own_rows = qkv[0]
    seg_len = own_rows.shape[1]
    length_all = seg_len * seq_count
    doc_ends = jnp.cumsum(doc_lengths[0], axis=1)
    lengths_all = stream_lengths[0]
    reach = min(seq_count - 1, -(-(length_all // 2 - 1) // seg_len))
    local = jnp.arange(seg_len, dtype=jnp.int32)
    query_pos = seq_index * seg_len + local
    key_value_width = KV_HEADS * HD
    far = jnp.int32(4 * length_all)

    def attend_own(row, kv_local, pieces_and_chunks, own_index):
        pieces = [kv_local]
        key_pos = [query_pos]
        for piece, chunk in pieces_and_chunks:
            pieces.append(piece)
            key_pos.append(jnp.where(chunk >= 0, chunk * seg_len + local, far))
        kv_all = jnp.concatenate(pieces, axis=0)
        key_pos = jnp.concatenate(key_pos)
        row_id = 2 * replica + own_index
        ends = lax.dynamic_index_in_dim(doc_ends, row_id, 0, keepdims=False)
        length = lax.dynamic_index_in_dim(lengths_all, row_id, 0, keepdims=False)
        return attend_row(
            row[:, :D],
            kv_all[:, :key_value_width],
            kv_all[:, key_value_width:],
            query_pos,
            key_pos,
            ends,
            length,
        )

    first_row, second_row = own_rows[0], own_rows[1]
    first_kv = first_row[:, D:]
    first_pieces = gathered(first_kv, seq_index, seq_count, reach)
    second_kv = lax.optimization_barrier((second_row[:, D:], first_pieces[0][0]))[0]
    second_pieces = gathered(second_kv, seq_index, seq_count, reach)
    first_out = attend_own(first_row, first_kv, first_pieces, 0)
    first_next = passed_along(first_out, "section", 1)
    previous_hand = passed_along(hand_over[0], "section", 1)
    second_row, _, previous_hand = lax.optimization_barrier((second_row, first_out, previous_hand))
    second_out = attend_own(second_row, second_kv, second_pieces, 1)
    second_next = passed_along(second_out, "section", 1)

    own_hand = lax.dynamic_index_in_dim(previous_hand, replica, 0, keepdims=False)
    partner_hand = lax.dynamic_index_in_dim(previous_hand, partner, 0, keepdims=False)
    partner_first = swapped(first_next, "dp", 0)
    partner_second = swapped(second_next, "dp", 0)
    sent = [
        jnp.where(own_hand == 1, first_next, second_next),
        jnp.where(partner_hand == 0, partner_first, partner_second),
    ]
    out = jnp.stack(sent, axis=0)
    return out.reshape(1, RPR, seg_len, D)


def solution(mesh):
    return jax.shard_map(
        shards,
        mesh=mesh,
        in_specs=(
            P("section", "dp", "seq", None),
            P("section", None),
            P("section", None, None),
            P("section", None),
        ),
        out_specs=P("section", "dp", "seq", None),
        check_vma=False,
    )
```

```python
import jax
import jax.numpy as jnp
from jax import lax
from jax.sharding import PartitionSpec as P

H = 32
HD = 128
KV_HEADS = 8
D = 4096
RPR = 2


def swapped(block, axis, distance):
    count = lax.axis_size(axis)
    route = []
    for low in range(count):
        high = low | 1 << distance
        if high != low and high < count:
            route += [(low, high), (high, low)]
    return lax.ppermute(block, axis, route)


def passed_along(value, axis, steps):
    count = lax.axis_size(axis)
    pairs = [(source, (source + steps) % count) for source in range(count)]
    return lax.ppermute(value, axis, pairs)


def doc_of(positions, ends):
    return jnp.sum((positions[:, None] >= ends[None, :]).astype(jnp.int32), axis=1)


def attend_row(query_rows, key_rows, value_rows, query_pos, key_pos, ends, length):
    seg_len = query_rows.shape[0]
    key_len = key_rows.shape[0]
    group_size = H // KV_HEADS
    query_doc = doc_of(query_pos, ends)
    key_doc = doc_of(key_pos, ends)
    allowed = (key_pos[None, :] <= query_pos[:, None]) & (key_doc[None, :] == query_doc[:, None])
    kv_heads = key_rows.shape[1] // HD
    queries = query_rows.reshape(seg_len, kv_heads, group_size, HD)
    keys = key_rows.reshape(key_len, kv_heads, HD)
    values = value_rows.reshape(key_len, kv_heads, HD)
    scores = (
        jnp.einsum("qkgd,skd->kgqs", queries, keys, preferred_element_type=jnp.float32)
        * HD ** (-0.5)
    )
    row_top = jnp.max(jnp.where(allowed, scores, -jnp.inf), axis=-1, keepdims=True)
    weights = jnp.where(allowed, jnp.exp(scores - row_top), 0.0)
    row_total = jnp.sum(weights, axis=-1)
    rounded = weights.astype(jnp.bfloat16)
    summed = jnp.einsum("kgqs,skd->qkgd", rounded, values, preferred_element_type=jnp.float32)
    result = summed / jnp.transpose(row_total, (2, 0, 1))[..., None]
    valid = (query_pos < length).astype(jnp.float32)
    result = result * valid[:, None, None, None]
    return result.reshape(seg_len, kv_heads * group_size * HD).astype(jnp.bfloat16)


def gathered(block, seq_index, seq_count, reach):
    if seq_count == 4 and reach == 2:
        over_y = lax.ppermute(block, "seq", [(j, j ^ 2) for j in range(4)])
        odd = seq_index % 2 == 1
        onward = jnp.where(odd, over_y, block)
        over_x = lax.ppermute(onward, "seq", [(j, j ^ 1) for j in range(4)])
        return [
            (over_y, jnp.bitwise_xor(seq_index, 2)),
            (over_x, jnp.where(odd, seq_index - 1, jnp.bitwise_xor(seq_index, 3))),
        ]
    pieces = []
    for shift in range(1, reach + 1):
        pairs = [(source, source + shift) for source in range(seq_count - shift)]
        pieces.append((lax.ppermute(block, "seq", pairs), seq_index - shift))
    return pieces


def shards(qkv, stream_lengths, doc_lengths, hand_over):
    seq_count = lax.axis_size("seq")
    seq_index = lax.axis_index("seq")
    replica = lax.axis_index("dp")
    partner = jnp.bitwise_xor(replica, 1)
    own_rows = qkv[0]
    seg_len = own_rows.shape[1]
    length_all = seg_len * seq_count
    doc_ends = jnp.cumsum(doc_lengths[0], axis=1)
    lengths_all = stream_lengths[0]
    reach = min(seq_count - 1, -(-(length_all // 2 - 1) // seg_len))
    local = jnp.arange(seg_len, dtype=jnp.int32)
    query_pos = seq_index * seg_len + local
    key_value_width = KV_HEADS * HD
    far = jnp.int32(4 * length_all)

    groups = 2
    group_kv = KV_HEADS // groups
    group_q = group_kv * (H // KV_HEADS) * HD
    group_width = group_kv * HD

    def attend_piece(query_rows, kv_local, pieces_and_chunks, own_index):
        pieces = [kv_local]
        key_pos = [query_pos]
        for piece, chunk in pieces_and_chunks:
            pieces.append(piece)
            key_pos.append(jnp.where(chunk >= 0, chunk * seg_len + local, far))
        kv_all = jnp.concatenate(pieces, axis=0)
        key_pos = jnp.concatenate(key_pos)
        row_id = 2 * replica + own_index
        ends = lax.dynamic_index_in_dim(doc_ends, row_id, 0, keepdims=False)
        length = lax.dynamic_index_in_dim(lengths_all, row_id, 0, keepdims=False)
        return attend_row(
            query_rows,
            kv_all[:, :group_width],
            kv_all[:, group_width:],
            query_pos,
            key_pos,
            ends,
            length,
        )

    previous_hand = passed_along(hand_over[0], "section", 1)
    arrived = {}
    last_first = None
    last_out = None
    for own_index in range(RPR):
        row = own_rows[own_index]
        for group in range(groups):
            keys = row[:, D + group * group_width : D + (group + 1) * group_width]
            values = row[:, D + key_value_width + group * group_width :][:, :group_width]
            kv_local = jnp.concatenate([keys, values], axis=1)
            queries = row[:, group * group_q : (group + 1) * group_q]
            if last_first is not None:
                kv_local = lax.optimization_barrier((kv_local, last_first))[0]
            pieces = gathered(kv_local, seq_index, seq_count, reach)
            if last_out is not None:
                queries, _, previous_hand = lax.optimization_barrier((queries, last_out, previous_hand))
            out = attend_piece(queries, kv_local, pieces, own_index)
            arrived[own_index, group] = passed_along(out, "section", 1)
            last_first = pieces[0][0]
            last_out = out

    own_hand = lax.dynamic_index_in_dim(previous_hand, replica, 0, keepdims=False)
    partner_hand = lax.dynamic_index_in_dim(previous_hand, partner, 0, keepdims=False)
    partner_arrived = {key: swapped(value, "dp", 0) for key, value in arrived.items()}

    def whole(parts, own_index):
        return jnp.concatenate([parts[own_index, group] for group in range(groups)], axis=1)

    sent = [
        jnp.where(own_hand == 1, whole(arrived, 0), whole(arrived, 1)),
        jnp.where(partner_hand == 0, whole(partner_arrived, 0), whole(partner_arrived, 1)),
    ]
    out = jnp.stack(sent, axis=0)
    return out.reshape(1, RPR, seg_len, D)


def solution(mesh):
    return jax.shard_map(
        shards,
        mesh=mesh,
        in_specs=(
            P("section", "dp", "seq", None),
            P("section", None),
            P("section", None, None),
            P("section", None),
        ),
        out_specs=P("section", "dp", "seq", None),
        check_vma=False,
    )
```

```python
import jax
import jax.numpy as jnp
from jax import lax
from jax.sharding import PartitionSpec as P

H = 32
HD = 128
KV_HEADS = 8
D = 4096
RPR = 2


def swapped(block, axis, distance):
    count = lax.axis_size(axis)
    route = []
    for low in range(count):
        high = low | 1 << distance
        if high != low and high < count:
            route += [(low, high), (high, low)]
    return lax.ppermute(block, axis, route)


def passed_along(value, axis, steps):
    count = lax.axis_size(axis)
    pairs = [(source, (source + steps) % count) for source in range(count)]
    return lax.ppermute(value, axis, pairs)


def doc_of(positions, ends):
    return jnp.sum((positions[:, None] >= ends[None, :]).astype(jnp.int32), axis=1)


def attend_row(query_rows, key_rows, value_rows, query_pos, key_pos, ends, length):
    seg_len = query_rows.shape[0]
    key_len = key_rows.shape[0]
    group_size = H // KV_HEADS
    query_doc = doc_of(query_pos, ends)
    key_doc = doc_of(key_pos, ends)
    allowed = (key_pos[None, :] <= query_pos[:, None]) & (key_doc[None, :] == query_doc[:, None])
    queries = query_rows.reshape(seg_len, KV_HEADS, group_size, HD)
    keys = key_rows.reshape(key_len, KV_HEADS, HD)
    values = value_rows.reshape(key_len, KV_HEADS, HD)
    scores = (
        jnp.einsum("qkgd,skd->kgqs", queries, keys, preferred_element_type=jnp.float32)
        * HD ** (-0.5)
    )
    row_top = jnp.max(jnp.where(allowed, scores, -jnp.inf), axis=-1, keepdims=True)
    weights = jnp.where(allowed, jnp.exp(scores - row_top), 0.0)
    row_total = jnp.sum(weights, axis=-1)
    rounded = weights.astype(jnp.bfloat16)
    summed = jnp.einsum("kgqs,skd->qkgd", rounded, values, preferred_element_type=jnp.float32)
    result = summed / jnp.transpose(row_total, (2, 0, 1))[..., None]
    valid = (query_pos < length).astype(jnp.float32)
    result = result * valid[:, None, None, None]
    return result.reshape(seg_len, D).astype(jnp.bfloat16)


def gathered(block, seq_index, seq_count, reach, hold=None):
    if seq_count == 4 and reach == 2:
        over_y = lax.ppermute(block, "seq", [(j, j ^ 2) for j in range(4)])
        odd = seq_index % 2 == 1
        onward = jnp.where(odd, over_y, block)
        if hold is not None:
            onward = lax.optimization_barrier((onward, hold))[0]
        over_x = lax.ppermute(onward, "seq", [(j, j ^ 1) for j in range(4)])
        return [
            (over_y, jnp.bitwise_xor(seq_index, 2)),
            (over_x, jnp.where(odd, seq_index - 1, jnp.bitwise_xor(seq_index, 3))),
        ]
    pieces = []
    for shift in range(1, reach + 1):
        pairs = [(source, source + shift) for source in range(seq_count - shift)]
        pieces.append((lax.ppermute(block, "seq", pairs), seq_index - shift))
    return pieces


def shards(qkv, stream_lengths, doc_lengths, hand_over):
    seq_count = lax.axis_size("seq")
    seq_index = lax.axis_index("seq")
    replica = lax.axis_index("dp")
    partner = jnp.bitwise_xor(replica, 1)
    own_rows = qkv[0]
    seg_len = own_rows.shape[1]
    length_all = seg_len * seq_count
    doc_ends = jnp.cumsum(doc_lengths[0], axis=1)
    lengths_all = stream_lengths[0]
    reach = min(seq_count - 1, -(-(length_all // 2 - 1) // seg_len))
    local = jnp.arange(seg_len, dtype=jnp.int32)
    query_pos = seq_index * seg_len + local
    key_value_width = KV_HEADS * HD
    far = jnp.int32(4 * length_all)

    def attend_own(row, kv_local, pieces_and_chunks, own_index):
        pieces = [kv_local]
        key_pos = [query_pos]
        for piece, chunk in pieces_and_chunks:
            pieces.append(piece)
            key_pos.append(jnp.where(chunk >= 0, chunk * seg_len + local, far))
        kv_all = jnp.concatenate(pieces, axis=0)
        key_pos = jnp.concatenate(key_pos)
        row_id = 2 * replica + own_index
        ends = lax.dynamic_index_in_dim(doc_ends, row_id, 0, keepdims=False)
        length = lax.dynamic_index_in_dim(lengths_all, row_id, 0, keepdims=False)
        return attend_row(
            row[:, :D],
            kv_all[:, :key_value_width],
            kv_all[:, key_value_width:],
            query_pos,
            key_pos,
            ends,
            length,
        )

    first_row, second_row = own_rows[0], own_rows[1]
    first_kv = first_row[:, D:]
    first_pieces = gathered(first_kv, seq_index, seq_count, reach)
    first_out = attend_own(first_row, first_kv, first_pieces, 0)
    second_kv = lax.optimization_barrier((second_row[:, D:], first_pieces[0][0]))[0]
    second_pieces = gathered(second_kv, seq_index, seq_count, reach, hold=first_out)
    first_next = passed_along(first_out, "section", 1)
    previous_hand = passed_along(hand_over[0], "section", 1)
    second_row, _, previous_hand = lax.optimization_barrier((second_row, first_out, previous_hand))
    second_out = attend_own(second_row, second_kv, second_pieces, 1)
    second_next = passed_along(second_out, "section", 1)

    own_hand = lax.dynamic_index_in_dim(previous_hand, replica, 0, keepdims=False)
    partner_hand = lax.dynamic_index_in_dim(previous_hand, partner, 0, keepdims=False)
    partner_first = swapped(first_next, "dp", 0)
    partner_second = swapped(second_next, "dp", 0)
    sent = [
        jnp.where(own_hand == 1, first_next, second_next),
        jnp.where(partner_hand == 0, partner_first, partner_second),
    ]
    out = jnp.stack(sent, axis=0)
    return out.reshape(1, RPR, seg_len, D)


def solution(mesh):
    return jax.shard_map(
        shards,
        mesh=mesh,
        in_specs=(
            P("section", "dp", "seq", None),
            P("section", None),
            P("section", None, None),
            P("section", None),
        ),
        out_specs=P("section", "dp", "seq", None),
        check_vma=False,
    )
```

```python
import jax
import jax.numpy as jnp
from jax import lax
from jax.sharding import PartitionSpec as P

H = 32
HD = 128
KV_HEADS = 8
D = 4096
RPR = 2


def swapped(block, axis, distance):
    count = lax.axis_size(axis)
    route = []
    for low in range(count):
        high = low | 1 << distance
        if high != low and high < count:
            route += [(low, high), (high, low)]
    return lax.ppermute(block, axis, route)


def passed_along(value, axis, steps):
    count = lax.axis_size(axis)
    pairs = [(source, (source + steps) % count) for source in range(count)]
    return lax.ppermute(value, axis, pairs)


def doc_of(positions, ends):
    return jnp.sum((positions[:, None] >= ends[None, :]).astype(jnp.int32), axis=1)


def attend_row(query_rows, key_rows, value_rows, query_pos, key_pos, ends, length):
    seg_len = query_rows.shape[0]
    key_len = key_rows.shape[0]
    group_size = H // KV_HEADS
    query_doc = doc_of(query_pos, ends)
    key_doc = doc_of(key_pos, ends)
    allowed = (key_pos[None, :] <= query_pos[:, None]) & (key_doc[None, :] == query_doc[:, None])
    queries = query_rows.reshape(seg_len, KV_HEADS, group_size, HD)
    keys = key_rows.reshape(key_len, KV_HEADS, HD)
    values = value_rows.reshape(key_len, KV_HEADS, HD)
    scores = (
        jnp.einsum("qkgd,skd->kgqs", queries, keys, preferred_element_type=jnp.float32)
        * HD ** (-0.5)
    )
    row_top = jnp.max(jnp.where(allowed, scores, -jnp.inf), axis=-1, keepdims=True)
    weights = jnp.where(allowed, jnp.exp(scores - row_top), 0.0)
    row_total = jnp.sum(weights, axis=-1)
    rounded = weights.astype(jnp.bfloat16)
    summed = jnp.einsum("kgqs,skd->qkgd", rounded, values, preferred_element_type=jnp.float32)
    result = summed / jnp.transpose(row_total, (2, 0, 1))[..., None]
    valid = (query_pos < length).astype(jnp.float32)
    result = result * valid[:, None, None, None]
    return result.reshape(seg_len, D).astype(jnp.bfloat16)


def gathered(block, seq_index, seq_count, reach, hold=None):
    if seq_count == 4 and reach == 2:
        over_y = lax.ppermute(block, "seq", [(j, j ^ 2) for j in range(4)])
        odd = seq_index % 2 == 1
        onward = jnp.where(odd, over_y, block)
        if hold is not None:
            onward = lax.optimization_barrier((onward, hold))[0]
        over_x = lax.ppermute(onward, "seq", [(j, j ^ 1) for j in range(4)])
        return [
            (over_y, jnp.bitwise_xor(seq_index, 2)),
            (over_x, jnp.where(odd, seq_index - 1, jnp.bitwise_xor(seq_index, 3))),
        ]
    pieces = []
    for shift in range(1, reach + 1):
        pairs = [(source, source + shift) for source in range(seq_count - shift)]
        pieces.append((lax.ppermute(block, "seq", pairs), seq_index - shift))
    return pieces


def shards(qkv, stream_lengths, doc_lengths, hand_over):
    seq_count = lax.axis_size("seq")
    seq_index = lax.axis_index("seq")
    replica = lax.axis_index("dp")
    partner = jnp.bitwise_xor(replica, 1)
    own_rows = qkv[0]
    seg_len = own_rows.shape[1]
    length_all = seg_len * seq_count
    doc_ends = jnp.cumsum(doc_lengths[0], axis=1)
    lengths_all = stream_lengths[0]
    reach = min(seq_count - 1, -(-(length_all // 2 - 1) // seg_len))
    local = jnp.arange(seg_len, dtype=jnp.int32)
    query_pos = seq_index * seg_len + local
    key_value_width = KV_HEADS * HD
    far = jnp.int32(4 * length_all)

    def attend_own(row, kv_local, pieces_and_chunks, own_index):
        pieces = [kv_local]
        key_pos = [query_pos]
        for piece, chunk in pieces_and_chunks:
            pieces.append(piece)
            key_pos.append(jnp.where(chunk >= 0, chunk * seg_len + local, far))
        kv_all = jnp.concatenate(pieces, axis=0)
        key_pos = jnp.concatenate(key_pos)
        row_id = 2 * replica + own_index
        ends = lax.dynamic_index_in_dim(doc_ends, row_id, 0, keepdims=False)
        length = lax.dynamic_index_in_dim(lengths_all, row_id, 0, keepdims=False)
        return attend_row(
            row[:, :D],
            kv_all[:, :key_value_width],
            kv_all[:, key_value_width:],
            query_pos,
            key_pos,
            ends,
            length,
        )

    first_row, second_row = own_rows[0], own_rows[1]
    first_kv = first_row[:, D:]
    first_pieces = gathered(first_kv, seq_index, seq_count, reach)
    first_out = attend_own(first_row, first_kv, first_pieces, 0)
    second_kv = lax.optimization_barrier((second_row[:, D:], first_pieces[0][0]))[0]
    second_pieces = gathered(second_kv, seq_index, seq_count, reach, hold=first_out)
    replicas = lax.axis_size("dp")
    own_hand = jnp.sum(jnp.where(jnp.arange(replicas) == replica, hand_over[0], 0))
    hand_block = jnp.full((seg_len, HD), own_hand, dtype=jnp.bfloat16)
    first_next = passed_along(jnp.concatenate([first_out, hand_block], axis=1), "section", 1)
    second_row = lax.optimization_barrier((second_row, first_out))[0]
    second_out = attend_own(second_row, second_kv, second_pieces, 1)
    second_next = passed_along(second_out, "section", 1)

    partner_first = swapped(first_next, "dp", 0)
    partner_second = swapped(second_next, "dp", 0)
    sent = [
        jnp.where(first_next[0:1, D:D + 1] == 1, first_next[:, :D], second_next),
        jnp.where(partner_first[0:1, D:D + 1] == 0, partner_first[:, :D], partner_second),
    ]
    out = jnp.stack(sent, axis=0)
    return out.reshape(1, RPR, seg_len, D)


def solution(mesh):
    return jax.shard_map(
        shards,
        mesh=mesh,
        in_specs=(
            P("section", "dp", "seq", None),
            P("section", None),
            P("section", None, None),
            P("section", None),
        ),
        out_specs=P("section", "dp", "seq", None),
        check_vma=False,
    )
```

```python
import jax
import jax.numpy as jnp
from jax import lax
from jax.sharding import PartitionSpec as P

H = 32
HD = 128
KV_HEADS = 8
D = 4096
RPR = 2


def swapped(block, axis, distance):
    count = lax.axis_size(axis)
    route = []
    for low in range(count):
        high = low | 1 << distance
        if high != low and high < count:
            route += [(low, high), (high, low)]
    return lax.ppermute(block, axis, route)


def passed_along(value, axis, steps):
    count = lax.axis_size(axis)
    pairs = [(source, (source + steps) % count) for source in range(count)]
    return lax.ppermute(value, axis, pairs)


def doc_of(positions, ends):
    return jnp.sum((positions[:, None] >= ends[None, :]).astype(jnp.int32), axis=1)


def attend_row(query_rows, key_rows, value_rows, query_pos, key_pos, ends, length):
    seg_len = query_rows.shape[0]
    key_len = key_rows.shape[0]
    group_size = H // KV_HEADS
    query_doc = doc_of(query_pos, ends)
    key_doc = doc_of(key_pos, ends)
    allowed = (key_pos[None, :] <= query_pos[:, None]) & (key_doc[None, :] == query_doc[:, None])
    queries = query_rows.reshape(seg_len, KV_HEADS, group_size, HD)
    keys = key_rows.reshape(key_len, KV_HEADS, HD)
    values = value_rows.reshape(key_len, KV_HEADS, HD)
    scores = (
        jnp.einsum("qkgd,skd->kgqs", queries, keys, preferred_element_type=jnp.float32)
        * HD ** (-0.5)
    )
    row_top = jnp.max(jnp.where(allowed, scores, -jnp.inf), axis=-1, keepdims=True)
    weights = jnp.where(allowed, jnp.exp(scores - row_top), 0.0)
    row_total = jnp.sum(weights, axis=-1)
    rounded = weights.astype(jnp.bfloat16)
    summed = jnp.einsum("kgqs,skd->qkgd", rounded, values, preferred_element_type=jnp.float32)
    result = summed / jnp.transpose(row_total, (2, 0, 1))[..., None]
    valid = (query_pos < length).astype(jnp.float32)
    result = result * valid[:, None, None, None]
    return result.reshape(seg_len, D).astype(jnp.bfloat16)


def gathered(block, seq_index, seq_count, reach, hold=None):
    if seq_count == 4 and reach == 2:
        over_y = lax.ppermute(block, "seq", [(j, j ^ 2) for j in range(4)])
        odd = seq_index % 2 == 1
        onward = jnp.where(odd, over_y, block)
        if hold is not None:
            onward = lax.optimization_barrier((onward, hold))[0]
        over_x = lax.ppermute(onward, "seq", [(j, j ^ 1) for j in range(4)])
        return [
            (over_y, jnp.bitwise_xor(seq_index, 2)),
            (over_x, jnp.where(odd, seq_index - 1, jnp.bitwise_xor(seq_index, 3))),
        ]
    pieces = []
    for shift in range(1, reach + 1):
        pairs = [(source, source + shift) for source in range(seq_count - shift)]
        pieces.append((lax.ppermute(block, "seq", pairs), seq_index - shift))
    return pieces


def shards(qkv, stream_lengths, doc_lengths, hand_over):
    seq_count = lax.axis_size("seq")
    seq_index = lax.axis_index("seq")
    replica = lax.axis_index("dp")
    partner = jnp.bitwise_xor(replica, 1)
    own_rows = qkv[0]
    seg_len = own_rows.shape[1]
    length_all = seg_len * seq_count
    doc_ends = jnp.cumsum(doc_lengths[0], axis=1)
    lengths_all = stream_lengths[0]
    reach = min(seq_count - 1, -(-(length_all // 2 - 1) // seg_len))
    local = jnp.arange(seg_len, dtype=jnp.int32)
    query_pos = seq_index * seg_len + local
    key_value_width = KV_HEADS * HD
    far = jnp.int32(4 * length_all)

    replicas = lax.axis_size("dp")
    handed = jnp.sum(jnp.where(jnp.arange(replicas) == replica, hand_over[0], 0)) == 1
    own_ends = lax.dynamic_slice_in_dim(doc_ends, 2 * replica, 2, 0)
    own_lengths = lax.dynamic_slice_in_dim(lengths_all, 2 * replica, 2, 0)

    def attend_own(query_rows, kv_local, pieces_and_chunks, first_is_kept):
        pieces = [kv_local]
        key_pos = [query_pos]
        for piece, chunk in pieces_and_chunks:
            pieces.append(piece)
            key_pos.append(jnp.where(chunk >= 0, chunk * seg_len + local, far))
        kv_all = jnp.concatenate(pieces, axis=0)
        key_pos = jnp.concatenate(key_pos)
        ends = jnp.where(first_is_kept, own_ends[0], own_ends[1])
        length = jnp.where(first_is_kept, own_lengths[0], own_lengths[1])
        return attend_row(
            query_rows,
            kv_all[:, :key_value_width],
            kv_all[:, key_value_width:],
            query_pos,
            key_pos,
            ends,
            length,
        )

    kept_kv = jnp.where(handed, own_rows[0, :, D:], own_rows[1, :, D:])
    kept_pieces = gathered(kept_kv, seq_index, seq_count, reach)
    kept_queries = jnp.where(handed, own_rows[0, :, :D], own_rows[1, :, :D])
    kept_out = attend_own(kept_queries, kept_kv, kept_pieces, handed)
    given_kv = jnp.where(handed, own_rows[1, :, D:], own_rows[0, :, D:])
    given_kv = lax.optimization_barrier((given_kv, kept_pieces[0][0]))[0]
    given_pieces = gathered(given_kv, seq_index, seq_count, reach, hold=kept_out)
    sent = [passed_along(kept_out, "section", 1)]
    given_queries = jnp.where(handed, own_rows[1, :, :D], own_rows[0, :, :D])
    given_queries = lax.optimization_barrier((given_queries, kept_out))[0]
    given_out = attend_own(given_queries, given_kv, given_pieces, jnp.logical_not(handed))
    sections = lax.axis_size("section")
    pairs = []
    for section in range(sections):
        for rep in range(replicas):
            pairs.append(
                (section * replicas + rep, (section + 1) % sections * replicas + (rep ^ 1))
            )
    sent.append(lax.ppermute(given_out, ("section", "dp"), pairs))
    out = jnp.stack(sent, axis=0)
    return out.reshape(1, RPR, seg_len, D)


def solution(mesh):
    return jax.shard_map(
        shards,
        mesh=mesh,
        in_specs=(
            P("section", "dp", "seq", None),
            P("section", None),
            P("section", None, None),
            P("section", None),
        ),
        out_specs=P("section", "dp", "seq", None),
        check_vma=False,
    )
```

```python
import jax
import jax.numpy as jnp
from jax import lax
from jax.sharding import PartitionSpec as P

H = 32
HD = 128
KV_HEADS = 8
D = 4096
RPR = 2


def swapped(block, axis, distance):
    count = lax.axis_size(axis)
    route = []
    for low in range(count):
        high = low | 1 << distance
        if high != low and high < count:
            route += [(low, high), (high, low)]
    return lax.ppermute(block, axis, route)


def passed_along(value, axis, steps):
    count = lax.axis_size(axis)
    pairs = [(source, (source + steps) % count) for source in range(count)]
    return lax.ppermute(value, axis, pairs)


def doc_of(positions, ends):
    return jnp.sum((positions[:, None] >= ends[None, :]).astype(jnp.int32), axis=1)


def attend_row(query_rows, key_rows, value_rows, query_pos, key_pos, ends, length):
    seg_len = query_rows.shape[0]
    key_len = key_rows.shape[0]
    group_size = H // KV_HEADS
    query_doc = doc_of(query_pos, ends)
    key_doc = doc_of(key_pos, ends)
    allowed = (key_pos[None, :] <= query_pos[:, None]) & (key_doc[None, :] == query_doc[:, None])
    queries = query_rows.reshape(seg_len, KV_HEADS, group_size, HD)
    keys = key_rows.reshape(key_len, KV_HEADS, HD)
    values = value_rows.reshape(key_len, KV_HEADS, HD)
    scores = (
        jnp.einsum("qkgd,skd->kgqs", queries, keys, preferred_element_type=jnp.float32)
        * HD ** (-0.5)
    )
    row_top = jnp.max(jnp.where(allowed, scores, -jnp.inf), axis=-1, keepdims=True)
    weights = jnp.where(allowed, jnp.exp(scores - row_top), 0.0)
    row_total = jnp.sum(weights, axis=-1)
    rounded = weights.astype(jnp.bfloat16)
    summed = jnp.einsum("kgqs,skd->qkgd", rounded, values, preferred_element_type=jnp.float32)
    result = summed / jnp.transpose(row_total, (2, 0, 1))[..., None]
    valid = (query_pos < length).astype(jnp.float32)
    result = result * valid[:, None, None, None]
    return result.reshape(seg_len, D).astype(jnp.bfloat16)


def gathered(block, seq_index, seq_count, reach, hold=None):
    if seq_count == 4 and reach == 2:
        over_y = lax.ppermute(block, "seq", [(j, j ^ 2) for j in range(4)])
        odd = seq_index % 2 == 1
        onward = jnp.where(odd, over_y, block)
        if hold is not None:
            onward = lax.optimization_barrier((onward, hold))[0]
        over_x = lax.ppermute(onward, "seq", [(j, j ^ 1) for j in range(4)])
        return [
            (over_y, jnp.bitwise_xor(seq_index, 2)),
            (over_x, jnp.where(odd, seq_index - 1, jnp.bitwise_xor(seq_index, 3))),
        ]
    pieces = []
    for shift in range(1, reach + 1):
        pairs = [(source, source + shift) for source in range(seq_count - shift)]
        pieces.append((lax.ppermute(block, "seq", pairs), seq_index - shift))
    return pieces


def shards(qkv, stream_lengths, doc_lengths, hand_over):
    seq_count = lax.axis_size("seq")
    seq_index = lax.axis_index("seq")
    replica = lax.axis_index("dp")
    partner = jnp.bitwise_xor(replica, 1)
    own_rows = qkv[0]
    seg_len = own_rows.shape[1]
    length_all = seg_len * seq_count
    doc_ends = jnp.cumsum(doc_lengths[0], axis=1)
    lengths_all = stream_lengths[0]
    reach = min(seq_count - 1, -(-(length_all // 2 - 1) // seg_len))
    local = jnp.arange(seg_len, dtype=jnp.int32)
    query_pos = seq_index * seg_len + local
    key_value_width = KV_HEADS * HD
    far = jnp.int32(4 * length_all)

    replicas = lax.axis_size("dp")
    handed = jnp.sum(jnp.where(jnp.arange(replicas) == replica, hand_over[0], 0)) == 1
    own_ends = lax.dynamic_slice_in_dim(doc_ends, 2 * replica, 2, 0)
    own_lengths = lax.dynamic_slice_in_dim(lengths_all, 2 * replica, 2, 0)

    def attend_own(query_rows, kv_local, pieces_and_chunks, first_is_kept):
        pieces = [kv_local]
        key_pos = [query_pos]
        for piece, chunk in pieces_and_chunks:
            pieces.append(piece)
            key_pos.append(jnp.where(chunk >= 0, chunk * seg_len + local, far))
        kv_all = jnp.concatenate(pieces, axis=0)
        key_pos = jnp.concatenate(key_pos)
        ends = jnp.where(first_is_kept, own_ends[0], own_ends[1])
        length = jnp.where(first_is_kept, own_lengths[0], own_lengths[1])
        return attend_row(
            query_rows,
            kv_all[:, :key_value_width],
            kv_all[:, key_value_width:],
            query_pos,
            key_pos,
            ends,
            length,
        )

    kept_kv = jnp.where(handed, own_rows[0, :, D:], own_rows[1, :, D:])
    kept_pieces = gathered(kept_kv, seq_index, seq_count, reach)
    kept_queries = jnp.where(handed, own_rows[0, :, :D], own_rows[1, :, :D])
    kept_out = attend_own(kept_queries, kept_kv, kept_pieces, handed)
    given_kv = jnp.where(handed, own_rows[1, :, D:], own_rows[0, :, D:])
    given_kv = lax.optimization_barrier((given_kv, kept_pieces[0][0]))[0]
    given_pieces = gathered(given_kv, seq_index, seq_count, reach, hold=kept_out)
    sent = [passed_along(kept_out, "section", 1)]
    given_queries = jnp.where(handed, own_rows[1, :, :D], own_rows[0, :, :D])
    given_queries = lax.optimization_barrier((given_queries, kept_out))[0]
    given_out = attend_own(given_queries, given_kv, given_pieces, jnp.logical_not(handed))
    sections = lax.axis_size("section")
    pairs = []
    for section in range(sections):
        for rep in range(replicas):
            pairs.append(
                (section * replicas + rep, (section + 1) % sections * replicas + (rep ^ 1))
            )
    sent.append(lax.ppermute(given_out, ("section", "dp"), pairs))
    out = lax.optimization_barrier(jnp.stack([sent[0], sent[0]], axis=0))
    out = lax.dynamic_update_slice_in_dim(out, sent[1][None], 1, 0)
    return out.reshape(1, RPR, seg_len, D)


def solution(mesh):
    return jax.shard_map(
        shards,
        mesh=mesh,
        in_specs=(
            P("section", "dp", "seq", None),
            P("section", None),
            P("section", None, None),
            P("section", None),
        ),
        out_specs=P("section", "dp", "seq", None),
        check_vma=False,
    )
```

```python
import jax
import jax.numpy as jnp
from jax import lax
from jax.sharding import PartitionSpec as P

H = 32
HD = 128
KV_HEADS = 8
D = 4096
RPR = 2


def swapped(block, axis, distance):
    count = lax.axis_size(axis)
    route = []
    for low in range(count):
        high = low | 1 << distance
        if high != low and high < count:
            route += [(low, high), (high, low)]
    return lax.ppermute(block, axis, route)


def passed_along(value, axis, steps):
    count = lax.axis_size(axis)
    pairs = [(source, (source + steps) % count) for source in range(count)]
    return lax.ppermute(value, axis, pairs)


def doc_of(positions, ends):
    return jnp.sum((positions[:, None] >= ends[None, :]).astype(jnp.int32), axis=1)


def attend_row(query_rows, key_rows, value_rows, query_pos, key_pos, ends, length):
    seg_len = query_rows.shape[0]
    key_len = key_rows.shape[0]
    group_size = H // KV_HEADS
    query_doc = doc_of(query_pos, ends)
    key_doc = doc_of(key_pos, ends)
    allowed = (key_pos[None, :] <= query_pos[:, None]) & (key_doc[None, :] == query_doc[:, None])
    kv_heads = key_rows.shape[1] // HD
    queries = query_rows.reshape(seg_len, kv_heads, group_size, HD)
    keys = key_rows.reshape(key_len, kv_heads, HD)
    values = value_rows.reshape(key_len, kv_heads, HD)
    scores = (
        jnp.einsum("qkgd,skd->kgqs", queries, keys, preferred_element_type=jnp.float32)
        * HD ** (-0.5)
    )
    row_top = jnp.max(jnp.where(allowed, scores, -jnp.inf), axis=-1, keepdims=True)
    weights = jnp.where(allowed, jnp.exp(scores - row_top), 0.0)
    row_total = jnp.sum(weights, axis=-1)
    rounded = weights.astype(jnp.bfloat16)
    summed = jnp.einsum("kgqs,skd->qkgd", rounded, values, preferred_element_type=jnp.float32)
    result = summed / jnp.transpose(row_total, (2, 0, 1))[..., None]
    valid = (query_pos < length).astype(jnp.float32)
    result = result * valid[:, None, None, None]
    return result.reshape(seg_len, kv_heads * group_size * HD).astype(jnp.bfloat16)


def gathered(block, seq_index, seq_count, reach, hold=None):
    if seq_count == 4 and reach == 2:
        over_y = lax.ppermute(block, "seq", [(j, j ^ 2) for j in range(4)])
        odd = seq_index % 2 == 1
        onward = jnp.where(odd, over_y, block)
        if hold is not None:
            onward = lax.optimization_barrier((onward, hold))[0]
        over_x = lax.ppermute(onward, "seq", [(j, j ^ 1) for j in range(4)])
        return [
            (over_y, jnp.bitwise_xor(seq_index, 2)),
            (over_x, jnp.where(odd, seq_index - 1, jnp.bitwise_xor(seq_index, 3))),
        ]
    pieces = []
    for shift in range(1, reach + 1):
        pairs = [(source, source + shift) for source in range(seq_count - shift)]
        pieces.append((lax.ppermute(block, "seq", pairs), seq_index - shift))
    return pieces


def shards(qkv, stream_lengths, doc_lengths, hand_over):
    seq_count = lax.axis_size("seq")
    seq_index = lax.axis_index("seq")
    replica = lax.axis_index("dp")
    partner = jnp.bitwise_xor(replica, 1)
    own_rows = qkv[0]
    seg_len = own_rows.shape[1]
    length_all = seg_len * seq_count
    doc_ends = jnp.cumsum(doc_lengths[0], axis=1)
    lengths_all = stream_lengths[0]
    reach = min(seq_count - 1, -(-(length_all // 2 - 1) // seg_len))
    local = jnp.arange(seg_len, dtype=jnp.int32)
    query_pos = seq_index * seg_len + local
    key_value_width = KV_HEADS * HD
    far = jnp.int32(4 * length_all)

    replicas = lax.axis_size("dp")
    handed = jnp.sum(jnp.where(jnp.arange(replicas) == replica, hand_over[0], 0)) == 1
    own_ends = lax.dynamic_slice_in_dim(doc_ends, 2 * replica, 2, 0)
    own_lengths = lax.dynamic_slice_in_dim(lengths_all, 2 * replica, 2, 0)

    def attend_own(query_rows, kv_local, pieces_and_chunks, first_is_kept):
        width = kv_local.shape[1] // 2
        pieces = [kv_local]
        key_pos = [query_pos]
        for piece, chunk in pieces_and_chunks:
            pieces.append(piece)
            key_pos.append(jnp.where(chunk >= 0, chunk * seg_len + local, far))
        kv_all = jnp.concatenate(pieces, axis=0)
        key_pos = jnp.concatenate(key_pos)
        ends = jnp.where(first_is_kept, own_ends[0], own_ends[1])
        length = jnp.where(first_is_kept, own_lengths[0], own_lengths[1])
        return attend_row(
            query_rows,
            kv_all[:, :width],
            kv_all[:, width:],
            query_pos,
            key_pos,
            ends,
            length,
        )

    def columns(kv_from, kv_to):
        per_kv = (H // KV_HEADS) * HD
        queries = own_rows[:, :, kv_from * per_kv : kv_to * per_kv]
        keys = own_rows[:, :, D + kv_from * HD : D + kv_to * HD]
        values = own_rows[:, :, D + key_value_width + kv_from * HD : D + key_value_width + kv_to * HD]
        return queries, jnp.concatenate([keys, values], axis=2)

    half = KV_HEADS // 2
    plan = [(True, 0, half), (True, half, KV_HEADS), (False, 0, KV_HEADS)]
    outs = []
    arrived = []
    last_first = None
    last_out = None
    for is_kept, kv_from, kv_to in plan:
        queries, kv_rows = columns(kv_from, kv_to)
        pick = handed if is_kept else jnp.logical_not(handed)
        kv_local = jnp.where(pick, kv_rows[0], kv_rows[1])
        if last_first is not None:
            kv_local = lax.optimization_barrier((kv_local, last_first))[0]
        pieces = gathered(kv_local, seq_index, seq_count, reach, hold=last_out)
        query_rows = jnp.where(pick, queries[0], queries[1])
        if len(arrived) == 1:
            query_rows = lax.optimization_barrier((query_rows, arrived[0]))[0]
        elif last_out is not None:
            query_rows = lax.optimization_barrier((query_rows, last_out))[0]
        out = attend_own(query_rows, kv_local, pieces, pick)
        if is_kept:
            arrived.append(passed_along(out, "section", 1))
        outs.append(out)
        last_first = pieces[0][0]
        last_out = out
    sent = arrived
    sections = lax.axis_size("section")
    pairs = []
    for section in range(sections):
        for rep in range(replicas):
            pairs.append(
                (section * replicas + rep, (section + 1) % sections * replicas + (rep ^ 1))
            )
    given_next = lax.ppermute(outs[2], ("section", "dp"), pairs)
    sent = [jnp.concatenate(sent, axis=1), given_next]
    out = lax.optimization_barrier(jnp.stack([sent[0], sent[0]], axis=0))
    out = lax.dynamic_update_slice_in_dim(out, sent[1][None], 1, 0)
    return out.reshape(1, RPR, seg_len, D)


def solution(mesh):
    return jax.shard_map(
        shards,
        mesh=mesh,
        in_specs=(
            P("section", "dp", "seq", None),
            P("section", None),
            P("section", None, None),
            P("section", None),
        ),
        out_specs=P("section", "dp", "seq", None),
        check_vma=False,
    )
```

```python
import jax
import jax.numpy as jnp
from jax import lax
from jax.sharding import PartitionSpec as P

H = 32
HD = 128
KV_HEADS = 8
D = 4096
RPR = 2


def swapped(block, axis, distance):
    count = lax.axis_size(axis)
    route = []
    for low in range(count):
        high = low | 1 << distance
        if high != low and high < count:
            route += [(low, high), (high, low)]
    return lax.ppermute(block, axis, route)


def passed_along(value, axis, steps):
    count = lax.axis_size(axis)
    pairs = [(source, (source + steps) % count) for source in range(count)]
    return lax.ppermute(value, axis, pairs)


def doc_of(positions, ends):
    return jnp.sum((positions[:, None] >= ends[None, :]).astype(jnp.int32), axis=1)


def attend_row(query_rows, key_rows, value_rows, query_pos, key_pos, ends, length):
    seg_len = query_rows.shape[0]
    key_len = key_rows.shape[0]
    group_size = H // KV_HEADS
    query_doc = doc_of(query_pos, ends)
    key_doc = doc_of(key_pos, ends)
    allowed = (key_pos[None, :] <= query_pos[:, None]) & (key_doc[None, :] == query_doc[:, None])
    queries = query_rows.reshape(seg_len, KV_HEADS, group_size, HD)
    keys = key_rows.reshape(key_len, KV_HEADS, HD)
    values = value_rows.reshape(key_len, KV_HEADS, HD)
    scores = (
        jnp.einsum("qkgd,skd->kgqs", queries, keys, preferred_element_type=jnp.float32)
        * HD ** (-0.5)
    )
    row_top = jnp.max(jnp.where(allowed, scores, -jnp.inf), axis=-1, keepdims=True)
    weights = jnp.where(allowed, jnp.exp(scores - row_top), 0.0)
    row_total = jnp.sum(weights, axis=-1)
    rounded = weights.astype(jnp.bfloat16)
    summed = jnp.einsum("kgqs,skd->qkgd", rounded, values, preferred_element_type=jnp.float32)
    result = summed / jnp.transpose(row_total, (2, 0, 1))[..., None]
    valid = (query_pos < length).astype(jnp.float32)
    result = result * valid[:, None, None, None]
    return result.reshape(seg_len, D).astype(jnp.bfloat16)


def gathered(block, seq_index, seq_count, reach, hold=None):
    if seq_count == 4 and reach == 2:
        over_y = lax.ppermute(block, "seq", [(j, j ^ 2) for j in range(4)])
        odd = seq_index % 2 == 1
        onward = jnp.where(odd, over_y, block)
        if hold is not None:
            onward = lax.optimization_barrier((onward, hold))[0]
        over_x = lax.ppermute(onward, "seq", [(j, j ^ 1) for j in range(4)])
        return [
            (over_y, jnp.bitwise_xor(seq_index, 2)),
            (over_x, jnp.where(odd, seq_index - 1, jnp.bitwise_xor(seq_index, 3))),
        ]
    pieces = []
    for shift in range(1, reach + 1):
        pairs = [(source, source + shift) for source in range(seq_count - shift)]
        pieces.append((lax.ppermute(block, "seq", pairs), seq_index - shift))
    return pieces


def shards(qkv, stream_lengths, doc_lengths, hand_over):
    seq_count = lax.axis_size("seq")
    seq_index = lax.axis_index("seq")
    replica = lax.axis_index("dp")
    partner = jnp.bitwise_xor(replica, 1)
    own_rows = qkv[0]
    seg_len = own_rows.shape[1]
    length_all = seg_len * seq_count
    doc_ends = jnp.cumsum(doc_lengths[0], axis=1)
    lengths_all = stream_lengths[0]
    reach = min(seq_count - 1, -(-(length_all // 2 - 1) // seg_len))
    local = jnp.arange(seg_len, dtype=jnp.int32)
    query_pos = seq_index * seg_len + local
    key_value_width = KV_HEADS * HD
    far = jnp.int32(4 * length_all)

    replicas = lax.axis_size("dp")
    handed = hand_over[0, 0] == 1
    for rep in range(1, replicas):
        handed = jnp.where(replica == rep, hand_over[0, rep] == 1, handed)
    own_ends = lax.dynamic_slice_in_dim(doc_ends, 2 * replica, 2, 0)
    own_lengths = lax.dynamic_slice_in_dim(lengths_all, 2 * replica, 2, 0)

    def attend_own(query_rows, kv_local, pieces_and_chunks, first_is_kept):
        pieces = [kv_local]
        key_pos = [query_pos]
        for piece, chunk in pieces_and_chunks:
            pieces.append(piece)
            key_pos.append(jnp.where(chunk >= 0, chunk * seg_len + local, far))
        kv_all = jnp.concatenate(pieces, axis=0)
        key_pos = jnp.concatenate(key_pos)
        ends = jnp.where(first_is_kept, own_ends[0], own_ends[1])
        length = jnp.where(first_is_kept, own_lengths[0], own_lengths[1])
        return attend_row(
            query_rows,
            kv_all[:, :key_value_width],
            kv_all[:, key_value_width:],
            query_pos,
            key_pos,
            ends,
            length,
        )

    kept_kv = jnp.where(handed, own_rows[0, :, D:], own_rows[1, :, D:])
    kept_pieces = gathered(kept_kv, seq_index, seq_count, reach)
    kept_queries = jnp.where(handed, own_rows[0, :, :D], own_rows[1, :, :D])
    kept_out = attend_own(kept_queries, kept_kv, kept_pieces, handed)
    given_kv = jnp.where(handed, own_rows[1, :, D:], own_rows[0, :, D:])
    given_kv = lax.optimization_barrier((given_kv, kept_pieces[0][0]))[0]
    given_pieces = gathered(given_kv, seq_index, seq_count, reach, hold=kept_out)
    sent = [passed_along(kept_out, "section", 1)]
    given_queries = jnp.where(handed, own_rows[1, :, :D], own_rows[0, :, :D])
    given_queries = lax.optimization_barrier((given_queries, kept_out))[0]
    given_out = attend_own(given_queries, given_kv, given_pieces, jnp.logical_not(handed))
    sections = lax.axis_size("section")
    pairs = []
    for section in range(sections):
        for rep in range(replicas):
            pairs.append(
                (section * replicas + rep, (section + 1) % sections * replicas + (rep ^ 1))
            )
    sent.append(lax.ppermute(given_out, ("section", "dp"), pairs))
    out = lax.optimization_barrier(jnp.stack([sent[0], sent[0]], axis=0))
    out = lax.dynamic_update_slice_in_dim(out, sent[1][None], 1, 0)
    return out.reshape(1, RPR, seg_len, D)


def solution(mesh):
    return jax.shard_map(
        shards,
        mesh=mesh,
        in_specs=(
            P("section", "dp", "seq", None),
            P("section", None),
            P("section", None, None),
            P("section", None),
        ),
        out_specs=P("section", "dp", "seq", None),
        check_vma=False,
    )
```

```python
import jax
import jax.numpy as jnp
from jax import lax
from jax.sharding import PartitionSpec as P

H = 32
HD = 128
KV_HEADS = 8
D = 4096
RPR = 2


def swapped(block, axis, distance):
    count = lax.axis_size(axis)
    route = []
    for low in range(count):
        high = low | 1 << distance
        if high != low and high < count:
            route += [(low, high), (high, low)]
    return lax.ppermute(block, axis, route)


def passed_along(value, axis, steps):
    count = lax.axis_size(axis)
    pairs = [(source, (source + steps) % count) for source in range(count)]
    return lax.ppermute(value, axis, pairs)


def doc_of(positions, ends):
    return jnp.sum((positions[:, None] >= ends[None, :]).astype(jnp.int32), axis=1)


def attend_row(query_rows, key_rows, value_rows, query_pos, key_pos, ends, length):
    seg_len = query_rows.shape[0]
    key_len = key_rows.shape[0]
    group_size = H // KV_HEADS
    query_doc = doc_of(query_pos, ends)
    key_doc = doc_of(key_pos, ends)
    allowed = (key_pos[None, :] <= query_pos[:, None]) & (key_doc[None, :] == query_doc[:, None])
    queries = query_rows.reshape(seg_len, KV_HEADS, group_size, HD)
    keys = key_rows.reshape(key_len, KV_HEADS, HD)
    values = value_rows.reshape(key_len, KV_HEADS, HD)
    scores = (
        jnp.einsum("qkgd,skd->kgqs", queries, keys, preferred_element_type=jnp.float32)
        * HD ** (-0.5)
    )
    row_top = jnp.max(jnp.where(allowed, scores, -jnp.inf), axis=-1, keepdims=True)
    weights = jnp.where(allowed, jnp.exp(scores - row_top), 0.0)
    row_total = jnp.sum(weights, axis=-1)
    rounded = weights.astype(jnp.bfloat16)
    summed = jnp.einsum("kgqs,skd->qkgd", rounded, values, preferred_element_type=jnp.float32)
    result = summed / jnp.transpose(row_total, (2, 0, 1))[..., None]
    valid = (query_pos < length).astype(jnp.float32)
    result = result * valid[:, None, None, None]
    return result.reshape(seg_len, D).astype(jnp.bfloat16)


def gathered(block, seq_index, seq_count, reach, hold=None):
    if seq_count == 4 and reach == 2:
        replicas = lax.axis_size("dp")
        axes = ("dp", "seq")
        replica = lax.axis_index("dp")

        def pairs(first):
            route = []
            for rep in range(replicas):
                step = 2 if (rep % 2 == 0) == first else 1
                route += [(rep * 4 + j, rep * 4 + (j ^ step)) for j in range(4)]
            return route

        over_first = lax.ppermute(block, axes, pairs(True))
        both = jnp.concatenate([block, over_first], axis=0)
        if hold is not None:
            both = lax.optimization_barrier((both, hold))[0]
        over_second = lax.ppermute(both, axes, pairs(False))
        even = replica % 2 == 0
        first_step = jnp.where(even, 2, 1)
        second_step = jnp.where(even, 1, 2)
        seg_len = block.shape[0]
        pieces = [
            (over_first, jnp.bitwise_xor(seq_index, first_step)),
            (over_second[:seg_len], jnp.bitwise_xor(seq_index, second_step)),
            (over_second[seg_len:], jnp.bitwise_xor(seq_index, 3)),
        ]
        return pieces, over_second
    pieces = []
    for shift in range(1, reach + 1):
        pairs = [(source, source + shift) for source in range(seq_count - shift)]
        pieces.append((lax.ppermute(block, "seq", pairs), seq_index - shift))
    return pieces, pieces[-1][0]


def shards(qkv, stream_lengths, doc_lengths, hand_over):
    seq_count = lax.axis_size("seq")
    seq_index = lax.axis_index("seq")
    replica = lax.axis_index("dp")
    partner = jnp.bitwise_xor(replica, 1)
    own_rows = qkv[0]
    seg_len = own_rows.shape[1]
    length_all = seg_len * seq_count
    doc_ends = jnp.cumsum(doc_lengths[0], axis=1)
    lengths_all = stream_lengths[0]
    reach = min(seq_count - 1, -(-(length_all // 2 - 1) // seg_len))
    local = jnp.arange(seg_len, dtype=jnp.int32)
    query_pos = seq_index * seg_len + local
    key_value_width = KV_HEADS * HD
    far = jnp.int32(4 * length_all)

    replicas = lax.axis_size("dp")
    handed = jnp.sum(jnp.where(jnp.arange(replicas) == replica, hand_over[0], 0)) == 1
    own_ends = lax.dynamic_slice_in_dim(doc_ends, 2 * replica, 2, 0)
    own_lengths = lax.dynamic_slice_in_dim(lengths_all, 2 * replica, 2, 0)

    def attend_own(query_rows, kv_local, pieces_and_chunks, first_is_kept):
        pieces = [kv_local]
        key_pos = [query_pos]
        for piece, chunk in pieces_and_chunks:
            pieces.append(piece)
            key_pos.append(jnp.where(chunk >= 0, chunk * seg_len + local, far))
        kv_all = jnp.concatenate(pieces, axis=0)
        key_pos = jnp.concatenate(key_pos)
        ends = jnp.where(first_is_kept, own_ends[0], own_ends[1])
        length = jnp.where(first_is_kept, own_lengths[0], own_lengths[1])
        return attend_row(
            query_rows,
            kv_all[:, :key_value_width],
            kv_all[:, key_value_width:],
            query_pos,
            key_pos,
            ends,
            length,
        )

    kept_kv = jnp.where(handed, own_rows[0, :, D:], own_rows[1, :, D:])
    kept_pieces, kept_last = gathered(kept_kv, seq_index, seq_count, reach)
    kept_queries = jnp.where(handed, own_rows[0, :, :D], own_rows[1, :, :D])
    kept_out = attend_own(kept_queries, kept_kv, kept_pieces, handed)
    given_kv = jnp.where(handed, own_rows[1, :, D:], own_rows[0, :, D:])
    given_kv = lax.optimization_barrier((given_kv, kept_last))[0]
    given_pieces, _ = gathered(given_kv, seq_index, seq_count, reach, hold=kept_out)
    sent = [passed_along(kept_out, "section", 1)]
    given_queries = jnp.where(handed, own_rows[1, :, :D], own_rows[0, :, :D])
    given_queries = lax.optimization_barrier((given_queries, kept_out))[0]
    given_out = attend_own(given_queries, given_kv, given_pieces, jnp.logical_not(handed))
    sections = lax.axis_size("section")
    pairs = []
    for section in range(sections):
        for rep in range(replicas):
            pairs.append(
                (section * replicas + rep, (section + 1) % sections * replicas + (rep ^ 1))
            )
    sent.append(lax.ppermute(given_out, ("section", "dp"), pairs))
    out = lax.optimization_barrier(jnp.stack([sent[0], sent[0]], axis=0))
    out = lax.dynamic_update_slice_in_dim(out, sent[1][None], 1, 0)
    return out.reshape(1, RPR, seg_len, D)


def solution(mesh):
    return jax.shard_map(
        shards,
        mesh=mesh,
        in_specs=(
            P("section", "dp", "seq", None),
            P("section", None),
            P("section", None, None),
            P("section", None),
        ),
        out_specs=P("section", "dp", "seq", None),
        check_vma=False,
    )
```

```python
import jax
import jax.numpy as jnp
from jax import lax
from jax.sharding import PartitionSpec as P

H = 32
HD = 128
KV_HEADS = 8
D = 4096
RPR = 2


def swapped(block, axis, distance):
    count = lax.axis_size(axis)
    route = []
    for low in range(count):
        high = low | 1 << distance
        if high != low and high < count:
            route += [(low, high), (high, low)]
    return lax.ppermute(block, axis, route)


def passed_along(value, axis, steps):
    count = lax.axis_size(axis)
    pairs = [(source, (source + steps) % count) for source in range(count)]
    return lax.ppermute(value, axis, pairs)


def doc_of(positions, ends):
    return jnp.sum((positions[:, None] >= ends[None, :]).astype(jnp.int32), axis=1)


def attend_row(query_rows, key_rows, value_rows, query_pos, key_pos, ends, length):
    seg_len = query_rows.shape[0]
    key_len = key_rows.shape[0]
    group_size = H // KV_HEADS
    query_doc = doc_of(query_pos, ends)
    key_doc = doc_of(key_pos, ends)
    allowed = (key_pos[None, :] <= query_pos[:, None]) & (key_doc[None, :] == query_doc[:, None])
    queries = query_rows.reshape(seg_len, KV_HEADS, group_size, HD)
    keys = key_rows.reshape(key_len, KV_HEADS, HD)
    values = value_rows.reshape(key_len, KV_HEADS, HD)
    scores = (
        jnp.einsum("qkgd,skd->kgqs", queries, keys, preferred_element_type=jnp.float32)
        * HD ** (-0.5)
    )
    row_top = jnp.max(jnp.where(allowed, scores, -jnp.inf), axis=-1, keepdims=True)
    weights = jnp.where(allowed, jnp.exp(scores - row_top), 0.0)
    row_total = jnp.sum(weights, axis=-1)
    rounded = weights.astype(jnp.bfloat16)
    summed = jnp.einsum("kgqs,skd->qkgd", rounded, values, preferred_element_type=jnp.float32)
    result = summed / jnp.transpose(row_total, (2, 0, 1))[..., None]
    valid = (query_pos < length).astype(jnp.float32)
    result = result * valid[:, None, None, None]
    return result.reshape(seg_len, D).astype(jnp.bfloat16)


def gathered(block, seq_index, seq_count, reach, hold=None):
    if seq_count == 4 and reach == 2:
        over_y = lax.ppermute(block, "seq", [(j, j ^ 2) for j in range(4)])
        odd = seq_index % 2 == 1
        onward = jnp.where(odd, over_y, block)
        if hold is not None:
            onward = lax.optimization_barrier((onward, hold))[0]
        over_x = lax.ppermute(onward, "seq", [(j, j ^ 1) for j in range(4)])
        return [
            (over_y, jnp.bitwise_xor(seq_index, 2)),
            (over_x, jnp.where(odd, seq_index - 1, jnp.bitwise_xor(seq_index, 3))),
        ]
    pieces = []
    for shift in range(1, reach + 1):
        pairs = [(source, source + shift) for source in range(seq_count - shift)]
        pieces.append((lax.ppermute(block, "seq", pairs), seq_index - shift))
    return pieces


def gathered_mirrored(block, seq_index, seq_count, reach):
    if seq_count == 4 and reach == 2:
        over_x = lax.ppermute(block, "seq", [(j, j ^ 1) for j in range(4)])
        both = jnp.concatenate([block, over_x], axis=0)
        over_y = lax.ppermute(both, "seq", [(j, j ^ 2) for j in range(4)])
        seg_len = block.shape[0]
        return [
            (over_x, jnp.bitwise_xor(seq_index, 1)),
            (over_y[:seg_len], jnp.bitwise_xor(seq_index, 2)),
            (over_y[seg_len:], jnp.bitwise_xor(seq_index, 3)),
        ]
    return gathered(block, seq_index, seq_count, reach)


def shards(qkv, stream_lengths, doc_lengths, hand_over):
    seq_count = lax.axis_size("seq")
    seq_index = lax.axis_index("seq")
    replica = lax.axis_index("dp")
    partner = jnp.bitwise_xor(replica, 1)
    own_rows = qkv[0]
    seg_len = own_rows.shape[1]
    length_all = seg_len * seq_count
    doc_ends = jnp.cumsum(doc_lengths[0], axis=1)
    lengths_all = stream_lengths[0]
    reach = min(seq_count - 1, -(-(length_all // 2 - 1) // seg_len))
    local = jnp.arange(seg_len, dtype=jnp.int32)
    query_pos = seq_index * seg_len + local
    key_value_width = KV_HEADS * HD
    far = jnp.int32(4 * length_all)

    replicas = lax.axis_size("dp")
    handed = jnp.sum(jnp.where(jnp.arange(replicas) == replica, hand_over[0], 0)) == 1
    own_ends = lax.dynamic_slice_in_dim(doc_ends, 2 * replica, 2, 0)
    own_lengths = lax.dynamic_slice_in_dim(lengths_all, 2 * replica, 2, 0)

    def attend_own(query_rows, kv_local, pieces_and_chunks, first_is_kept):
        pieces = [kv_local]
        key_pos = [query_pos]
        for piece, chunk in pieces_and_chunks:
            pieces.append(piece)
            key_pos.append(jnp.where(chunk >= 0, chunk * seg_len + local, far))
        kv_all = jnp.concatenate(pieces, axis=0)
        key_pos = jnp.concatenate(key_pos)
        ends = jnp.where(first_is_kept, own_ends[0], own_ends[1])
        length = jnp.where(first_is_kept, own_lengths[0], own_lengths[1])
        return attend_row(
            query_rows,
            kv_all[:, :key_value_width],
            kv_all[:, key_value_width:],
            query_pos,
            key_pos,
            ends,
            length,
        )

    kept_kv = jnp.where(handed, own_rows[0, :, D:], own_rows[1, :, D:])
    kept_pieces = gathered(kept_kv, seq_index, seq_count, reach)
    kept_queries = jnp.where(handed, own_rows[0, :, :D], own_rows[1, :, :D])
    kept_out = attend_own(kept_queries, kept_kv, kept_pieces, handed)
    given_kv = jnp.where(handed, own_rows[1, :, D:], own_rows[0, :, D:])
    given_pieces = gathered_mirrored(given_kv, seq_index, seq_count, reach)
    sent = [passed_along(kept_out, "section", 1)]
    given_queries = jnp.where(handed, own_rows[1, :, :D], own_rows[0, :, :D])
    given_queries = lax.optimization_barrier((given_queries, kept_out))[0]
    given_out = attend_own(given_queries, given_kv, given_pieces, jnp.logical_not(handed))
    sections = lax.axis_size("section")
    pairs = []
    for section in range(sections):
        for rep in range(replicas):
            pairs.append(
                (section * replicas + rep, (section + 1) % sections * replicas + (rep ^ 1))
            )
    sent.append(lax.ppermute(given_out, ("section", "dp"), pairs))
    out = lax.optimization_barrier(jnp.stack([sent[0], sent[0]], axis=0))
    out = lax.dynamic_update_slice_in_dim(out, sent[1][None], 1, 0)
    return out.reshape(1, RPR, seg_len, D)


def solution(mesh):
    return jax.shard_map(
        shards,
        mesh=mesh,
        in_specs=(
            P("section", "dp", "seq", None),
            P("section", None),
            P("section", None, None),
            P("section", None),
        ),
        out_specs=P("section", "dp", "seq", None),
        check_vma=False,
    )
```

```python
import jax
import jax.numpy as jnp
from jax import lax
from jax.sharding import PartitionSpec as P

H = 32
HD = 128
KV_HEADS = 8
D = 4096
RPR = 2


def swapped(block, axis, distance):
    count = lax.axis_size(axis)
    route = []
    for low in range(count):
        high = low | 1 << distance
        if high != low and high < count:
            route += [(low, high), (high, low)]
    return lax.ppermute(block, axis, route)


def passed_along(value, axis, steps):
    count = lax.axis_size(axis)
    pairs = [(source, (source + steps) % count) for source in range(count)]
    return lax.ppermute(value, axis, pairs)


def doc_of(positions, ends):
    return jnp.sum((positions[:, None] >= ends[None, :]).astype(jnp.int32), axis=1)


def attend_row(query_rows, key_rows, value_rows, query_pos, key_pos, ends, length):
    seg_len = query_rows.shape[0]
    key_len = key_rows.shape[0]
    group_size = H // KV_HEADS
    query_doc = doc_of(query_pos, ends)
    key_doc = doc_of(key_pos, ends)
    allowed = (key_pos[None, :] <= query_pos[:, None]) & (key_doc[None, :] == query_doc[:, None])
    queries = query_rows.reshape(seg_len, KV_HEADS, group_size, HD)
    keys = key_rows.reshape(key_len, KV_HEADS, HD)
    values = value_rows.reshape(key_len, KV_HEADS, HD)
    scores = (
        jnp.einsum("qkgd,skd->kgqs", queries, keys, preferred_element_type=jnp.float32)
        * HD ** (-0.5)
    )
    row_top = jnp.max(jnp.where(allowed, scores, -jnp.inf), axis=-1, keepdims=True)
    weights = jnp.where(allowed, jnp.exp(scores - row_top), 0.0)
    row_total = jnp.sum(weights, axis=-1)
    rounded = weights.astype(jnp.bfloat16)
    summed = jnp.einsum("kgqs,skd->qkgd", rounded, values, preferred_element_type=jnp.float32)
    result = summed / jnp.transpose(row_total, (2, 0, 1))[..., None]
    valid = (query_pos < length).astype(jnp.float32)
    result = result * valid[:, None, None, None]
    return result.reshape(seg_len, D).astype(jnp.bfloat16)


def gathered(block, seq_index, seq_count, reach, hold=None):
    if seq_count == 4 and reach == 2:
        over_y = lax.ppermute(block, "seq", [(j, j ^ 2) for j in range(4)])
        odd = seq_index % 2 == 1
        onward = jnp.where(odd, over_y, block)
        if hold is not None:
            onward = lax.optimization_barrier((onward, hold))[0]
        over_x = lax.ppermute(onward, "seq", [(j, j ^ 1) for j in range(4)])
        return [
            (over_y, jnp.bitwise_xor(seq_index, 2)),
            (over_x, jnp.where(odd, seq_index - 1, jnp.bitwise_xor(seq_index, 3))),
        ]
    pieces = []
    for shift in range(1, reach + 1):
        pairs = [(source, source + shift) for source in range(seq_count - shift)]
        pieces.append((lax.ppermute(block, "seq", pairs), seq_index - shift))
    return pieces


def shards(qkv, stream_lengths, doc_lengths, hand_over):
    seq_count = lax.axis_size("seq")
    seq_index = lax.axis_index("seq")
    replica = lax.axis_index("dp")
    partner = jnp.bitwise_xor(replica, 1)
    own_rows = qkv[0]
    seg_len = own_rows.shape[1]
    length_all = seg_len * seq_count
    doc_ends = jnp.cumsum(doc_lengths[0], axis=1)
    lengths_all = stream_lengths[0]
    reach = min(seq_count - 1, -(-(length_all // 2 - 1) // seg_len))
    local = jnp.arange(seg_len, dtype=jnp.int32)
    query_pos = seq_index * seg_len + local
    key_value_width = KV_HEADS * HD
    far = jnp.int32(4 * length_all)

    replicas = lax.axis_size("dp")
    handed = jnp.sum(jnp.where(jnp.arange(replicas) == replica, hand_over[0], 0)) == 1
    own_ends = lax.dynamic_slice_in_dim(doc_ends, 2 * replica, 2, 0)
    own_lengths = lax.dynamic_slice_in_dim(lengths_all, 2 * replica, 2, 0)

    def positions_of(pieces_and_chunks):
        key_pos = [query_pos]
        for _, chunk in pieces_and_chunks:
            key_pos.append(jnp.where(chunk >= 0, chunk * seg_len + local, far))
        return jnp.concatenate(key_pos)

    def attend_own(query_rows, key_pieces, value_pieces, key_pos, first_is_kept):
        ends = jnp.where(first_is_kept, own_ends[0], own_ends[1])
        length = jnp.where(first_is_kept, own_lengths[0], own_lengths[1])
        return attend_row(
            query_rows,
            jnp.concatenate(key_pieces, axis=0),
            jnp.concatenate(value_pieces, axis=0),
            query_pos,
            key_pos,
            ends,
            length,
        )

    kept_k = jnp.where(handed, own_rows[0, :, D:D + key_value_width], own_rows[1, :, D:D + key_value_width])
    kept_v = jnp.where(handed, own_rows[0, :, D + key_value_width:], own_rows[1, :, D + key_value_width:])
    k_pieces = gathered(kept_k, seq_index, seq_count, reach)
    kept_v = lax.optimization_barrier((kept_v, k_pieces[0][0]))[0]
    v_pieces = gathered(kept_v, seq_index, seq_count, reach)
    kept_queries = jnp.where(handed, own_rows[0, :, :D], own_rows[1, :, :D])
    kept_out = attend_own(
        kept_queries,
        [kept_k] + [piece for piece, _ in k_pieces],
        [kept_v] + [piece for piece, _ in v_pieces],
        positions_of(k_pieces),
        handed,
    )
    given_kv = jnp.where(handed, own_rows[1, :, D:], own_rows[0, :, D:])
    given_kv = lax.optimization_barrier((given_kv, v_pieces[0][0]))[0]
    given_pieces = gathered(given_kv, seq_index, seq_count, reach, hold=kept_out)
    sent = [passed_along(kept_out, "section", 1)]
    given_queries = jnp.where(handed, own_rows[1, :, :D], own_rows[0, :, :D])
    given_queries = lax.optimization_barrier((given_queries, kept_out))[0]
    given_out = attend_own(
        given_queries,
        [given_kv[:, :key_value_width]] + [piece[:, :key_value_width] for piece, _ in given_pieces],
        [given_kv[:, key_value_width:]] + [piece[:, key_value_width:] for piece, _ in given_pieces],
        positions_of(given_pieces),
        jnp.logical_not(handed),
    )
    sections = lax.axis_size("section")
    pairs = []
    for section in range(sections):
        for rep in range(replicas):
            pairs.append(
                (section * replicas + rep, (section + 1) % sections * replicas + (rep ^ 1))
            )
    sent.append(lax.ppermute(given_out, ("section", "dp"), pairs))
    out = lax.optimization_barrier(jnp.stack([sent[0], sent[0]], axis=0))
    out = lax.dynamic_update_slice_in_dim(out, sent[1][None], 1, 0)
    return out.reshape(1, RPR, seg_len, D)


def solution(mesh):
    return jax.shard_map(
        shards,
        mesh=mesh,
        in_specs=(
            P("section", "dp", "seq", None),
            P("section", None),
            P("section", None, None),
            P("section", None),
        ),
        out_specs=P("section", "dp", "seq", None),
        check_vma=False,
    )
```

```python
import jax
import jax.numpy as jnp
from jax import lax
from jax.sharding import PartitionSpec as P

H = 32
HD = 128
KV_HEADS = 8
D = 4096
RPR = 2


def swapped(block, axis, distance):
    count = lax.axis_size(axis)
    route = []
    for low in range(count):
        high = low | 1 << distance
        if high != low and high < count:
            route += [(low, high), (high, low)]
    return lax.ppermute(block, axis, route)


def passed_along(value, axis, steps):
    count = lax.axis_size(axis)
    pairs = [(source, (source + steps) % count) for source in range(count)]
    return lax.ppermute(value, axis, pairs)


def doc_of(positions, ends):
    return jnp.sum((positions[:, None] >= ends[None, :]).astype(jnp.int32), axis=1)


def attend_row(query_rows, key_rows, value_rows, query_pos, key_pos, ends, length):
    seg_len = query_rows.shape[0]
    key_len = key_rows.shape[0]
    group_size = H // KV_HEADS
    query_doc = doc_of(query_pos, ends)
    key_doc = doc_of(key_pos, ends)
    allowed = (key_pos[None, :] <= query_pos[:, None]) & (key_doc[None, :] == query_doc[:, None])
    queries = query_rows.reshape(seg_len, KV_HEADS, group_size, HD)
    keys = key_rows.reshape(key_len, KV_HEADS, HD)
    values = value_rows.reshape(key_len, KV_HEADS, HD)
    scores = (
        jnp.einsum("qkgd,skd->kgqs", queries, keys, preferred_element_type=jnp.float32)
        * HD ** (-0.5)
    )
    row_top = jnp.max(jnp.where(allowed, scores, -jnp.inf), axis=-1, keepdims=True)
    weights = jnp.where(allowed, jnp.exp(scores - row_top), 0.0)
    row_total = jnp.sum(weights, axis=-1)
    rounded = weights.astype(jnp.bfloat16)
    summed = jnp.einsum("kgqs,skd->qkgd", rounded, values, preferred_element_type=jnp.float32)
    result = summed / jnp.transpose(row_total, (2, 0, 1))[..., None]
    valid = (query_pos < length).astype(jnp.float32)
    result = result * valid[:, None, None, None]
    return result.reshape(seg_len, D).astype(jnp.bfloat16)


def gathered(block, seq_index, seq_count, reach, hold=None):
    if seq_count == 4 and reach == 2:
        over_y = lax.ppermute(block, "seq", [(j, j ^ 2) for j in range(4)])
        odd = seq_index % 2 == 1
        onward = jnp.where(odd, over_y, block)
        if hold is not None:
            onward = lax.optimization_barrier((onward, hold))[0]
        over_x = lax.ppermute(onward, "seq", [(j, j ^ 1) for j in range(4)])
        return [
            (over_y, jnp.bitwise_xor(seq_index, 2)),
            (over_x, jnp.where(odd, seq_index - 1, jnp.bitwise_xor(seq_index, 3))),
        ]
    pieces = []
    for shift in range(1, reach + 1):
        pairs = [(source, source + shift) for source in range(seq_count - shift)]
        pieces.append((lax.ppermute(block, "seq", pairs), seq_index - shift))
    return pieces


def dense_shards(qkv, stream_lengths, doc_lengths, hand_over):
    seq_count = lax.axis_size("seq")
    seq_index = lax.axis_index("seq")
    replica = lax.axis_index("dp")
    partner = jnp.bitwise_xor(replica, 1)
    own_rows = qkv[0]
    seg_len = own_rows.shape[1]
    length_all = seg_len * seq_count
    doc_ends = jnp.cumsum(doc_lengths[0], axis=1)
    lengths_all = stream_lengths[0]
    reach = min(seq_count - 1, -(-(length_all // 2 - 1) // seg_len))
    local = jnp.arange(seg_len, dtype=jnp.int32)
    query_pos = seq_index * seg_len + local
    key_value_width = KV_HEADS * HD
    far = jnp.int32(4 * length_all)

    replicas = lax.axis_size("dp")
    handed = jnp.sum(jnp.where(jnp.arange(replicas) == replica, hand_over[0], 0)) == 1
    own_ends = lax.dynamic_slice_in_dim(doc_ends, 2 * replica, 2, 0)
    own_lengths = lax.dynamic_slice_in_dim(lengths_all, 2 * replica, 2, 0)

    def attend_own(query_rows, kv_local, pieces_and_chunks, first_is_kept):
        pieces = [kv_local]
        key_pos = [query_pos]
        for piece, chunk in pieces_and_chunks:
            pieces.append(piece)
            key_pos.append(jnp.where(chunk >= 0, chunk * seg_len + local, far))
        kv_all = jnp.concatenate(pieces, axis=0)
        key_pos = jnp.concatenate(key_pos)
        ends = jnp.where(first_is_kept, own_ends[0], own_ends[1])
        length = jnp.where(first_is_kept, own_lengths[0], own_lengths[1])
        return attend_row(
            query_rows,
            kv_all[:, :key_value_width],
            kv_all[:, key_value_width:],
            query_pos,
            key_pos,
            ends,
            length,
        )

    kept_kv = jnp.where(handed, own_rows[0, :, D:], own_rows[1, :, D:])
    kept_pieces = gathered(kept_kv, seq_index, seq_count, reach)
    kept_queries = jnp.where(handed, own_rows[0, :, :D], own_rows[1, :, :D])
    kept_out = attend_own(kept_queries, kept_kv, kept_pieces, handed)
    given_kv = jnp.where(handed, own_rows[1, :, D:], own_rows[0, :, D:])
    given_kv = lax.optimization_barrier((given_kv, kept_pieces[0][0]))[0]
    given_pieces = gathered(given_kv, seq_index, seq_count, reach, hold=kept_out)
    sent = [passed_along(kept_out, "section", 1)]
    given_queries = jnp.where(handed, own_rows[1, :, :D], own_rows[0, :, :D])
    given_queries = lax.optimization_barrier((given_queries, kept_out))[0]
    given_out = attend_own(given_queries, given_kv, given_pieces, jnp.logical_not(handed))
    sections = lax.axis_size("section")
    pairs = []
    for section in range(sections):
        for rep in range(replicas):
            pairs.append(
                (section * replicas + rep, (section + 1) % sections * replicas + (rep ^ 1))
            )
    sent.append(lax.ppermute(given_out, ("section", "dp"), pairs))
    out = lax.optimization_barrier(jnp.stack([sent[0], sent[0]], axis=0))
    out = lax.dynamic_update_slice_in_dim(out, sent[1][None], 1, 0)
    return out.reshape(1, RPR, seg_len, D)


def shards(qkv, stream_lengths, doc_lengths, hand_over):
    seq_count = lax.axis_size("seq")
    seg_len = qkv.shape[2]
    length_all = seg_len * seq_count
    rows = stream_lengths.shape[1]
    reach = min(seq_count - 1, -(-(length_all // 2 - 1) // seg_len))
    short_most = rows * length_all // 4 - 3 * length_all // 4 - (rows - 2)
    if not (seq_count == 4 and reach == 2 and 0 < short_most < seg_len):
        return dense_shards(qkv, stream_lengths, doc_lengths, hand_over)

    seq_index = lax.axis_index("seq")
    replica = lax.axis_index("dp")
    partner = jnp.bitwise_xor(replica, 1)
    own_rows = qkv[0]
    doc_ends = jnp.cumsum(doc_lengths[0], axis=1)
    lengths_all = stream_lengths[0]
    local = jnp.arange(seg_len, dtype=jnp.int32)
    query_pos = seq_index * seg_len + local
    key_value_width = KV_HEADS * HD
    far = jnp.int32(4 * length_all)
    own_ends = lax.dynamic_slice_in_dim(doc_ends, 2 * replica, 2, 0)
    own_lengths = lax.dynamic_slice_in_dim(lengths_all, 2 * replica, 2, 0)
    swap_second = own_lengths[1] >= own_lengths[0]

    def pick(first_if, a, b):
        return jnp.where(first_if, a, b)

    short_rows = pick(swap_second, own_rows[0], own_rows[1])
    short_out = attend_row(
        short_rows[:, :D],
        short_rows[:, D:D + key_value_width],
        short_rows[:, D + key_value_width:],
        query_pos,
        query_pos,
        pick(swap_second, own_ends[0], own_ends[1]),
        pick(swap_second, own_lengths[0], own_lengths[1]),
    )
    short_next = passed_along(short_out, "section", 1)

    long_rows = pick(swap_second, own_rows[1], own_rows[0])
    long_kv = long_rows[:, D:]
    long_pieces = gathered(long_kv, seq_index, seq_count, reach)
    previous = passed_along(jnp.concatenate([lengths_all, hand_over[0]]), "section", 1)
    long_queries, _, previous = lax.optimization_barrier((long_rows[:, :D], short_out, previous))
    pieces = [long_kv]
    key_pos = [query_pos]
    for piece, chunk in long_pieces:
        pieces.append(piece)
        key_pos.append(jnp.where(chunk >= 0, chunk * seg_len + local, far))
    kv_all = jnp.concatenate(pieces, axis=0)
    long_out = attend_row(
        long_queries,
        kv_all[:, :key_value_width],
        kv_all[:, key_value_width:],
        query_pos,
        jnp.concatenate(key_pos),
        pick(swap_second, own_ends[1], own_ends[0]),
        pick(swap_second, own_lengths[1], own_lengths[0]),
    )
    long_next = passed_along(long_out, "section", 1)

    previous_lengths = previous[:rows]
    previous_hand = previous[rows:]

    def short_index(rep):
        first = lax.dynamic_index_in_dim(previous_lengths, 2 * rep, 0, keepdims=False)
        second = lax.dynamic_index_in_dim(previous_lengths, 2 * rep + 1, 0, keepdims=False)
        return jnp.where(second >= first, 0, 1)

    own_hand = lax.dynamic_index_in_dim(previous_hand, replica, 0, keepdims=False)
    partner_hand = lax.dynamic_index_in_dim(previous_hand, partner, 0, keepdims=False)
    partner_short = swapped(short_next, "dp", 0)
    partner_long = swapped(long_next, "dp", 0)
    sent = [
        jnp.where(short_index(replica) == 1 - own_hand, short_next, long_next),
        jnp.where(short_index(partner) == partner_hand, partner_short, partner_long),
    ]
    out = jnp.stack(sent, axis=0)
    return out.reshape(1, RPR, seg_len, D)


def solution(mesh):
    return jax.shard_map(
        shards,
        mesh=mesh,
        in_specs=(
            P("section", "dp", "seq", None),
            P("section", None),
            P("section", None, None),
            P("section", None),
        ),
        out_specs=P("section", "dp", "seq", None),
        check_vma=False,
    )
```

```python
import jax
import jax.numpy as jnp
from jax import lax
from jax.sharding import PartitionSpec as P

H = 32
HD = 128
KV_HEADS = 8
D = 4096
RPR = 2


def swapped(block, axis, distance):
    count = lax.axis_size(axis)
    route = []
    for low in range(count):
        high = low | 1 << distance
        if high != low and high < count:
            route += [(low, high), (high, low)]
    return lax.ppermute(block, axis, route)


def passed_along(value, axis, steps):
    count = lax.axis_size(axis)
    pairs = [(source, (source + steps) % count) for source in range(count)]
    return lax.ppermute(value, axis, pairs)


def doc_of(positions, ends):
    return jnp.sum((positions[:, None] >= ends[None, :]).astype(jnp.int32), axis=1)


def attend_row(query_rows, key_rows, value_rows, query_pos, key_pos, ends, length):
    seg_len = query_rows.shape[0]
    key_len = key_rows.shape[0]
    group_size = H // KV_HEADS
    query_doc = doc_of(query_pos, ends)
    key_doc = doc_of(key_pos, ends)
    allowed = (key_pos[None, :] <= query_pos[:, None]) & (key_doc[None, :] == query_doc[:, None])
    queries = query_rows.reshape(seg_len, KV_HEADS, group_size, HD)
    keys = key_rows.reshape(key_len, KV_HEADS, HD)
    values = value_rows.reshape(key_len, KV_HEADS, HD)
    scores = (
        jnp.einsum("qkgd,skd->kgqs", queries, keys, preferred_element_type=jnp.float32)
        * HD ** (-0.5)
    )
    row_top = jnp.max(jnp.where(allowed, scores, -jnp.inf), axis=-1, keepdims=True)
    weights = jnp.where(allowed, jnp.exp(scores - row_top), 0.0)
    row_total = jnp.sum(weights, axis=-1)
    rounded = weights.astype(jnp.bfloat16)
    summed = jnp.einsum("kgqs,skd->qkgd", rounded, values, preferred_element_type=jnp.float32)
    result = summed / jnp.transpose(row_total, (2, 0, 1))[..., None]
    valid = (query_pos < length).astype(jnp.float32)
    result = result * valid[:, None, None, None]
    return result.reshape(seg_len, D).astype(jnp.bfloat16)


def gathered(block, seq_index, seq_count, reach, hold=None):
    if seq_count == 4 and reach == 2:
        over_y = lax.ppermute(block, "seq", [(j, j ^ 2) for j in range(4)])
        odd = seq_index % 2 == 1
        onward = jnp.where(odd, over_y, block)
        if hold is not None:
            onward = lax.optimization_barrier((onward, hold))[0]
        over_x = lax.ppermute(onward, "seq", [(j, j ^ 1) for j in range(4)])
        return [
            (over_y, jnp.bitwise_xor(seq_index, 2)),
            (over_x, jnp.where(odd, seq_index - 1, jnp.bitwise_xor(seq_index, 3))),
        ]
    pieces = []
    for shift in range(1, reach + 1):
        pairs = [(source, source + shift) for source in range(seq_count - shift)]
        pieces.append((lax.ppermute(block, "seq", pairs), seq_index - shift))
    return pieces


def dense_shards(qkv, stream_lengths, doc_lengths, hand_over):
    seq_count = lax.axis_size("seq")
    seq_index = lax.axis_index("seq")
    replica = lax.axis_index("dp")
    partner = jnp.bitwise_xor(replica, 1)
    own_rows = qkv[0]
    seg_len = own_rows.shape[1]
    length_all = seg_len * seq_count
    doc_ends = jnp.cumsum(doc_lengths[0], axis=1)
    lengths_all = stream_lengths[0]
    reach = min(seq_count - 1, -(-(length_all // 2 - 1) // seg_len))
    local = jnp.arange(seg_len, dtype=jnp.int32)
    query_pos = seq_index * seg_len + local
    key_value_width = KV_HEADS * HD
    far = jnp.int32(4 * length_all)

    replicas = lax.axis_size("dp")
    handed = jnp.sum(jnp.where(jnp.arange(replicas) == replica, hand_over[0], 0)) == 1
    own_ends = lax.dynamic_slice_in_dim(doc_ends, 2 * replica, 2, 0)
    own_lengths = lax.dynamic_slice_in_dim(lengths_all, 2 * replica, 2, 0)

    def attend_own(query_rows, kv_local, pieces_and_chunks, first_is_kept):
        pieces = [kv_local]
        key_pos = [query_pos]
        for piece, chunk in pieces_and_chunks:
            pieces.append(piece)
            key_pos.append(jnp.where(chunk >= 0, chunk * seg_len + local, far))
        kv_all = jnp.concatenate(pieces, axis=0)
        key_pos = jnp.concatenate(key_pos)
        ends = jnp.where(first_is_kept, own_ends[0], own_ends[1])
        length = jnp.where(first_is_kept, own_lengths[0], own_lengths[1])
        return attend_row(
            query_rows,
            kv_all[:, :key_value_width],
            kv_all[:, key_value_width:],
            query_pos,
            key_pos,
            ends,
            length,
        )

    kept_kv = jnp.where(handed, own_rows[0, :, D:], own_rows[1, :, D:])
    kept_pieces = gathered(kept_kv, seq_index, seq_count, reach)
    kept_queries = jnp.where(handed, own_rows[0, :, :D], own_rows[1, :, :D])
    kept_out = attend_own(kept_queries, kept_kv, kept_pieces, handed)
    given_kv = jnp.where(handed, own_rows[1, :, D:], own_rows[0, :, D:])
    given_kv = lax.optimization_barrier((given_kv, kept_pieces[0][0]))[0]
    given_pieces = gathered(given_kv, seq_index, seq_count, reach, hold=kept_out)
    sent = [passed_along(kept_out, "section", 1)]
    given_queries = jnp.where(handed, own_rows[1, :, :D], own_rows[0, :, :D])
    given_queries = lax.optimization_barrier((given_queries, kept_out))[0]
    given_out = attend_own(given_queries, given_kv, given_pieces, jnp.logical_not(handed))
    sections = lax.axis_size("section")
    pairs = []
    for section in range(sections):
        for rep in range(replicas):
            pairs.append(
                (section * replicas + rep, (section + 1) % sections * replicas + (rep ^ 1))
            )
    sent.append(lax.ppermute(given_out, ("section", "dp"), pairs))
    out = lax.optimization_barrier(jnp.stack([sent[0], sent[0]], axis=0))
    out = lax.dynamic_update_slice_in_dim(out, sent[1][None], 1, 0)
    return out.reshape(1, RPR, seg_len, D)


def shards(qkv, stream_lengths, doc_lengths, hand_over):
    seq_count = lax.axis_size("seq")
    seg_len = qkv.shape[2]
    length_all = seg_len * seq_count
    rows = stream_lengths.shape[1]
    reach = min(seq_count - 1, -(-(length_all // 2 - 1) // seg_len))
    short_most = rows * length_all // 4 - 3 * length_all // 4 - (rows - 2)
    if not (seq_count == 4 and reach == 2 and 0 < short_most < seg_len):
        return dense_shards(qkv, stream_lengths, doc_lengths, hand_over)

    seq_index = lax.axis_index("seq")
    replica = lax.axis_index("dp")
    partner = jnp.bitwise_xor(replica, 1)
    own_rows = qkv[0]
    doc_ends = jnp.cumsum(doc_lengths[0], axis=1)
    lengths_all = stream_lengths[0]
    local = jnp.arange(seg_len, dtype=jnp.int32)
    query_pos = seq_index * seg_len + local
    key_value_width = KV_HEADS * HD
    far = jnp.int32(4 * length_all)
    own_ends = lax.dynamic_slice_in_dim(doc_ends, 2 * replica, 2, 0)
    own_lengths = lax.dynamic_slice_in_dim(lengths_all, 2 * replica, 2, 0)
    swap_second = own_lengths[1] >= own_lengths[0]

    def pick(first_if, a, b):
        return jnp.where(first_if, a, b)

    short_rows = pick(swap_second, own_rows[0], own_rows[1])
    short_out = attend_row(
        short_rows[:, :D],
        short_rows[:, D:D + key_value_width],
        short_rows[:, D + key_value_width:],
        query_pos,
        query_pos,
        pick(swap_second, own_ends[0], own_ends[1]),
        pick(swap_second, own_lengths[0], own_lengths[1]),
    )
    replicas = lax.axis_size("dp")
    own_hand = jnp.sum(jnp.where(jnp.arange(replicas) == replica, hand_over[0], 0))
    short_index = jnp.where(swap_second, 0, 1)
    lane = jnp.arange(D)[None, :]
    tag = jnp.where(lane == 0, short_index, jnp.where(lane == 1, own_hand, 0))
    last_event = (local == seg_len - 1)[:, None]
    short_out = jnp.where(last_event, tag.astype(jnp.bfloat16), short_out)
    short_next = passed_along(short_out, "section", 1)

    long_rows = pick(swap_second, own_rows[1], own_rows[0])
    long_kv = long_rows[:, D:]
    long_pieces = gathered(long_kv, seq_index, seq_count, reach)
    long_queries = lax.optimization_barrier((long_rows[:, :D], short_out))[0]
    pieces = [long_kv]
    key_pos = [query_pos]
    for piece, chunk in long_pieces:
        pieces.append(piece)
        key_pos.append(jnp.where(chunk >= 0, chunk * seg_len + local, far))
    kv_all = jnp.concatenate(pieces, axis=0)
    long_out = attend_row(
        long_queries,
        kv_all[:, :key_value_width],
        kv_all[:, key_value_width:],
        query_pos,
        jnp.concatenate(key_pos),
        pick(swap_second, own_ends[1], own_ends[0]),
        pick(swap_second, own_lengths[1], own_lengths[0]),
    )
    long_next = passed_along(long_out, "section", 1)

    partner_short = swapped(short_next, "dp", 0)
    partner_long = swapped(long_next, "dp", 0)

    def placed(short_block, long_block, own_index_of):
        tag = short_block[seg_len - 1, :2].astype(jnp.int32)
        cleared = jnp.where(last_event, jnp.zeros_like(short_block), short_block)
        return jnp.where(tag[0] == own_index_of(tag[1]), cleared, long_block)

    sent = [
        placed(short_next, long_next, lambda hand: 1 - hand),
        placed(partner_short, partner_long, lambda hand: hand),
    ]
    out = jnp.stack(sent, axis=0)
    return out.reshape(1, RPR, seg_len, D)


def solution(mesh):
    return jax.shard_map(
        shards,
        mesh=mesh,
        in_specs=(
            P("section", "dp", "seq", None),
            P("section", None),
            P("section", None, None),
            P("section", None),
        ),
        out_specs=P("section", "dp", "seq", None),
        check_vma=False,
    )
```

```python
import jax
import jax.numpy as jnp
from jax import lax
from jax.sharding import PartitionSpec as P

H = 32
HD = 128
KV_HEADS = 8
D = 4096
RPR = 2


def swapped(block, axis, distance):
    count = lax.axis_size(axis)
    route = []
    for low in range(count):
        high = low | 1 << distance
        if high != low and high < count:
            route += [(low, high), (high, low)]
    return lax.ppermute(block, axis, route)


def passed_along(value, axis, steps):
    count = lax.axis_size(axis)
    pairs = [(source, (source + steps) % count) for source in range(count)]
    return lax.ppermute(value, axis, pairs)


def doc_of(positions, ends):
    return jnp.sum((positions[:, None] >= ends[None, :]).astype(jnp.int32), axis=1)


def attend_row(query_rows, key_rows, value_rows, query_pos, key_pos, ends, length):
    seg_len = query_rows.shape[0]
    key_len = key_rows.shape[0]
    group_size = H // KV_HEADS
    query_doc = doc_of(query_pos, ends)
    key_doc = doc_of(key_pos, ends)
    allowed = (key_pos[None, :] <= query_pos[:, None]) & (key_doc[None, :] == query_doc[:, None])
    queries = query_rows.reshape(seg_len, KV_HEADS, group_size, HD)
    keys = key_rows.reshape(key_len, KV_HEADS, HD)
    values = value_rows.reshape(key_len, KV_HEADS, HD)
    scores = (
        jnp.einsum("qkgd,skd->kgqs", queries, keys, preferred_element_type=jnp.float32)
        * HD ** (-0.5)
    )
    row_top = jnp.max(jnp.where(allowed, scores, -jnp.inf), axis=-1, keepdims=True)
    weights = jnp.where(allowed, jnp.exp(scores - row_top), 0.0)
    row_total = jnp.sum(weights, axis=-1)
    rounded = weights.astype(jnp.bfloat16)
    summed = jnp.einsum("kgqs,skd->qkgd", rounded, values, preferred_element_type=jnp.float32)
    result = summed / jnp.transpose(row_total, (2, 0, 1))[..., None]
    valid = (query_pos < length).astype(jnp.float32)
    result = result * valid[:, None, None, None]
    return result.reshape(seg_len, D).astype(jnp.bfloat16)


def gathered(block, seq_index, seq_count, reach, hold=None):
    if seq_count == 4 and reach == 2:
        over_y = lax.ppermute(block, "seq", [(j, j ^ 2) for j in range(4)])
        odd = seq_index % 2 == 1
        onward = jnp.where(odd, over_y, block)
        if hold is not None:
            onward = lax.optimization_barrier((onward, hold))[0]
        over_x = lax.ppermute(onward, "seq", [(j, j ^ 1) for j in range(4)])
        return [
            (over_y, jnp.bitwise_xor(seq_index, 2)),
            (over_x, jnp.where(odd, seq_index - 1, jnp.bitwise_xor(seq_index, 3))),
        ]
    pieces = []
    for shift in range(1, reach + 1):
        pairs = [(source, source + shift) for source in range(seq_count - shift)]
        pieces.append((lax.ppermute(block, "seq", pairs), seq_index - shift))
    return pieces


def dense_shards(qkv, stream_lengths, doc_lengths, hand_over):
    seq_count = lax.axis_size("seq")
    seq_index = lax.axis_index("seq")
    replica = lax.axis_index("dp")
    partner = jnp.bitwise_xor(replica, 1)
    own_rows = qkv[0]
    seg_len = own_rows.shape[1]
    length_all = seg_len * seq_count
    doc_ends = jnp.cumsum(doc_lengths[0], axis=1)
    lengths_all = stream_lengths[0]
    reach = min(seq_count - 1, -(-(length_all // 2 - 1) // seg_len))
    local = jnp.arange(seg_len, dtype=jnp.int32)
    query_pos = seq_index * seg_len + local
    key_value_width = KV_HEADS * HD
    far = jnp.int32(4 * length_all)

    replicas = lax.axis_size("dp")
    handed = jnp.sum(jnp.where(jnp.arange(replicas) == replica, hand_over[0], 0)) == 1
    own_ends = lax.dynamic_slice_in_dim(doc_ends, 2 * replica, 2, 0)
    own_lengths = lax.dynamic_slice_in_dim(lengths_all, 2 * replica, 2, 0)

    def attend_own(query_rows, kv_local, pieces_and_chunks, first_is_kept):
        pieces = [kv_local]
        key_pos = [query_pos]
        for piece, chunk in pieces_and_chunks:
            pieces.append(piece)
            key_pos.append(jnp.where(chunk >= 0, chunk * seg_len + local, far))
        kv_all = jnp.concatenate(pieces, axis=0)
        key_pos = jnp.concatenate(key_pos)
        ends = jnp.where(first_is_kept, own_ends[0], own_ends[1])
        length = jnp.where(first_is_kept, own_lengths[0], own_lengths[1])
        return attend_row(
            query_rows,
            kv_all[:, :key_value_width],
            kv_all[:, key_value_width:],
            query_pos,
            key_pos,
            ends,
            length,
        )

    kept_kv = jnp.where(handed, own_rows[0, :, D:], own_rows[1, :, D:])
    kept_pieces = gathered(kept_kv, seq_index, seq_count, reach)
    kept_queries = jnp.where(handed, own_rows[0, :, :D], own_rows[1, :, :D])
    kept_out = attend_own(kept_queries, kept_kv, kept_pieces, handed)
    given_kv = jnp.where(handed, own_rows[1, :, D:], own_rows[0, :, D:])
    given_kv = lax.optimization_barrier((given_kv, kept_pieces[0][0]))[0]
    given_pieces = gathered(given_kv, seq_index, seq_count, reach, hold=kept_out)
    sent = [passed_along(kept_out, "section", 1)]
    given_queries = jnp.where(handed, own_rows[1, :, :D], own_rows[0, :, :D])
    given_queries = lax.optimization_barrier((given_queries, kept_out))[0]
    given_out = attend_own(given_queries, given_kv, given_pieces, jnp.logical_not(handed))
    sections = lax.axis_size("section")
    pairs = []
    for section in range(sections):
        for rep in range(replicas):
            pairs.append(
                (section * replicas + rep, (section + 1) % sections * replicas + (rep ^ 1))
            )
    sent.append(lax.ppermute(given_out, ("section", "dp"), pairs))
    out = lax.optimization_barrier(jnp.stack([sent[0], sent[0]], axis=0))
    out = lax.dynamic_update_slice_in_dim(out, sent[1][None], 1, 0)
    return out.reshape(1, RPR, seg_len, D)


def shards(qkv, stream_lengths, doc_lengths, hand_over):
    seq_count = lax.axis_size("seq")
    seg_len = qkv.shape[2]
    length_all = seg_len * seq_count
    rows = stream_lengths.shape[1]
    reach = min(seq_count - 1, -(-(length_all // 2 - 1) // seg_len))
    short_most = rows * length_all // 4 - 3 * length_all // 4 - (rows - 2)
    if not (seq_count == 4 and reach == 2 and 0 < short_most < seg_len):
        return dense_shards(qkv, stream_lengths, doc_lengths, hand_over)

    seq_index = lax.axis_index("seq")
    replica = lax.axis_index("dp")
    partner = jnp.bitwise_xor(replica, 1)
    own_rows = qkv[0]
    doc_ends = jnp.cumsum(doc_lengths[0], axis=1)
    lengths_all = stream_lengths[0]
    local = jnp.arange(seg_len, dtype=jnp.int32)
    query_pos = seq_index * seg_len + local
    key_value_width = KV_HEADS * HD
    far = jnp.int32(4 * length_all)
    own_ends = lax.dynamic_slice_in_dim(doc_ends, 2 * replica, 2, 0)
    own_lengths = lax.dynamic_slice_in_dim(lengths_all, 2 * replica, 2, 0)
    swap_second = own_lengths[1] >= own_lengths[0]

    def pick(first_if, a, b):
        return jnp.where(first_if, a, b)

    short_rows = pick(swap_second, own_rows[0], own_rows[1])
    short_out = attend_row(
        short_rows[:, :D],
        short_rows[:, D:D + key_value_width],
        short_rows[:, D + key_value_width:],
        query_pos,
        query_pos,
        pick(swap_second, own_ends[0], own_ends[1]),
        pick(swap_second, own_lengths[0], own_lengths[1]),
    )
    short_next = passed_along(short_out, "section", 1)

    long_rows = pick(swap_second, own_rows[1], own_rows[0])
    long_kv = long_rows[:, D:]
    long_pieces = gathered(long_kv, seq_index, seq_count, reach)
    meta = lax.optimization_barrier((jnp.concatenate([lengths_all, hand_over[0]]), long_pieces[0][0]))[0]
    previous = passed_along(meta, "section", 1)
    long_queries = lax.optimization_barrier((long_rows[:, :D], short_out))[0]
    pieces = [long_kv]
    key_pos = [query_pos]
    for piece, chunk in long_pieces:
        pieces.append(piece)
        key_pos.append(jnp.where(chunk >= 0, chunk * seg_len + local, far))
    kv_all = jnp.concatenate(pieces, axis=0)
    long_out = attend_row(
        long_queries,
        kv_all[:, :key_value_width],
        kv_all[:, key_value_width:],
        query_pos,
        jnp.concatenate(key_pos),
        pick(swap_second, own_ends[1], own_ends[0]),
        pick(swap_second, own_lengths[1], own_lengths[0]),
    )
    long_out, previous = lax.optimization_barrier((long_out, previous))
    long_next = passed_along(long_out, "section", 1)

    previous_lengths = previous[:rows]
    previous_hand = previous[rows:]

    def short_index(rep):
        first = lax.dynamic_index_in_dim(previous_lengths, 2 * rep, 0, keepdims=False)
        second = lax.dynamic_index_in_dim(previous_lengths, 2 * rep + 1, 0, keepdims=False)
        return jnp.where(second >= first, 0, 1)

    own_hand = lax.dynamic_index_in_dim(previous_hand, replica, 0, keepdims=False)
    partner_hand = lax.dynamic_index_in_dim(previous_hand, partner, 0, keepdims=False)
    partner_short = swapped(short_next, "dp", 0)
    partner_long = swapped(long_next, "dp", 0)
    sent = [
        jnp.where(short_index(replica) == 1 - own_hand, short_next, long_next),
        jnp.where(short_index(partner) == partner_hand, partner_short, partner_long),
    ]
    out = jnp.stack(sent, axis=0)
    return out.reshape(1, RPR, seg_len, D)


def solution(mesh):
    return jax.shard_map(
        shards,
        mesh=mesh,
        in_specs=(
            P("section", "dp", "seq", None),
            P("section", None),
            P("section", None, None),
            P("section", None),
        ),
        out_specs=P("section", "dp", "seq", None),
        check_vma=False,
    )
```

```python
import jax
import jax.numpy as jnp
from jax import lax
from jax.sharding import PartitionSpec as P

H = 32
HD = 128
KV_HEADS = 8
D = 4096
RPR = 2


def swapped(block, axis, distance):
    count = lax.axis_size(axis)
    route = []
    for low in range(count):
        high = low | 1 << distance
        if high != low and high < count:
            route += [(low, high), (high, low)]
    return lax.ppermute(block, axis, route)


def passed_along(value, axis, steps):
    count = lax.axis_size(axis)
    pairs = [(source, (source + steps) % count) for source in range(count)]
    return lax.ppermute(value, axis, pairs)


def doc_of(positions, ends):
    return jnp.sum((positions[:, None] >= ends[None, :]).astype(jnp.int32), axis=1)


def attend_row(query_rows, key_rows, value_rows, query_pos, key_pos, ends, length):
    seg_len = query_rows.shape[0]
    key_len = key_rows.shape[0]
    group_size = H // KV_HEADS
    query_doc = doc_of(query_pos, ends)
    key_doc = doc_of(key_pos, ends)
    allowed = (key_pos[None, :] <= query_pos[:, None]) & (key_doc[None, :] == query_doc[:, None])
    queries = query_rows.reshape(seg_len, KV_HEADS, group_size, HD)
    keys = key_rows.reshape(key_len, KV_HEADS, HD)
    values = value_rows.reshape(key_len, KV_HEADS, HD)
    scores = (
        jnp.einsum("qkgd,skd->kgqs", queries, keys, preferred_element_type=jnp.float32)
        * HD ** (-0.5)
    )
    row_top = jnp.max(jnp.where(allowed, scores, -jnp.inf), axis=-1, keepdims=True)
    weights = jnp.where(allowed, jnp.exp(scores - row_top), 0.0)
    row_total = jnp.sum(weights, axis=-1)
    rounded = weights.astype(jnp.bfloat16)
    summed = jnp.einsum("kgqs,skd->qkgd", rounded, values, preferred_element_type=jnp.float32)
    result = summed / jnp.transpose(row_total, (2, 0, 1))[..., None]
    valid = (query_pos < length).astype(jnp.float32)
    result = result * valid[:, None, None, None]
    return result.reshape(seg_len, D).astype(jnp.bfloat16)


def gathered(block, seq_index, seq_count, reach, hold=None):
    if seq_count == 4 and reach == 2:
        over_y = lax.ppermute(block, "seq", [(j, j ^ 2) for j in range(4)])
        odd = seq_index % 2 == 1
        onward = jnp.where(odd, over_y, block)
        if hold is not None:
            onward = lax.optimization_barrier((onward, hold))[0]
        over_x = lax.ppermute(onward, "seq", [(j, j ^ 1) for j in range(4)])
        return [
            (over_y, jnp.bitwise_xor(seq_index, 2)),
            (over_x, jnp.where(odd, seq_index - 1, jnp.bitwise_xor(seq_index, 3))),
        ]
    pieces = []
    for shift in range(1, reach + 1):
        pairs = [(source, source + shift) for source in range(seq_count - shift)]
        pieces.append((lax.ppermute(block, "seq", pairs), seq_index - shift))
    return pieces


def dense_shards(qkv, stream_lengths, doc_lengths, hand_over):
    seq_count = lax.axis_size("seq")
    seq_index = lax.axis_index("seq")
    replica = lax.axis_index("dp")
    partner = jnp.bitwise_xor(replica, 1)
    own_rows = qkv[0]
    seg_len = own_rows.shape[1]
    length_all = seg_len * seq_count
    doc_ends = jnp.cumsum(doc_lengths[0], axis=1)
    lengths_all = stream_lengths[0]
    reach = min(seq_count - 1, -(-(length_all // 2 - 1) // seg_len))
    local = jnp.arange(seg_len, dtype=jnp.int32)
    query_pos = seq_index * seg_len + local
    key_value_width = KV_HEADS * HD
    far = jnp.int32(4 * length_all)

    replicas = lax.axis_size("dp")
    handed = jnp.sum(jnp.where(jnp.arange(replicas) == replica, hand_over[0], 0)) == 1
    own_ends = lax.dynamic_slice_in_dim(doc_ends, 2 * replica, 2, 0)
    own_lengths = lax.dynamic_slice_in_dim(lengths_all, 2 * replica, 2, 0)

    def attend_own(query_rows, kv_local, pieces_and_chunks, first_is_kept):
        pieces = [kv_local]
        key_pos = [query_pos]
        for piece, chunk in pieces_and_chunks:
            pieces.append(piece)
            key_pos.append(jnp.where(chunk >= 0, chunk * seg_len + local, far))
        kv_all = jnp.concatenate(pieces, axis=0)
        key_pos = jnp.concatenate(key_pos)
        ends = jnp.where(first_is_kept, own_ends[0], own_ends[1])
        length = jnp.where(first_is_kept, own_lengths[0], own_lengths[1])
        return attend_row(
            query_rows,
            kv_all[:, :key_value_width],
            kv_all[:, key_value_width:],
            query_pos,
            key_pos,
            ends,
            length,
        )

    kept_kv = jnp.where(handed, own_rows[0, :, D:], own_rows[1, :, D:])
    kept_pieces = gathered(kept_kv, seq_index, seq_count, reach)
    kept_queries = jnp.where(handed, own_rows[0, :, :D], own_rows[1, :, :D])
    kept_out = attend_own(kept_queries, kept_kv, kept_pieces, handed)
    given_kv = jnp.where(handed, own_rows[1, :, D:], own_rows[0, :, D:])
    given_kv = lax.optimization_barrier((given_kv, kept_pieces[0][0]))[0]
    given_pieces = gathered(given_kv, seq_index, seq_count, reach, hold=kept_out)
    sent = [passed_along(kept_out, "section", 1)]
    given_queries = jnp.where(handed, own_rows[1, :, :D], own_rows[0, :, :D])
    given_queries = lax.optimization_barrier((given_queries, kept_out))[0]
    given_out = attend_own(given_queries, given_kv, given_pieces, jnp.logical_not(handed))
    sections = lax.axis_size("section")
    pairs = []
    for section in range(sections):
        for rep in range(replicas):
            pairs.append(
                (section * replicas + rep, (section + 1) % sections * replicas + (rep ^ 1))
            )
    sent.append(lax.ppermute(given_out, ("section", "dp"), pairs))
    out = lax.optimization_barrier(jnp.stack([sent[0], sent[0]], axis=0))
    out = lax.dynamic_update_slice_in_dim(out, sent[1][None], 1, 0)
    return out.reshape(1, RPR, seg_len, D)


def shards(qkv, stream_lengths, doc_lengths, hand_over):
    seq_count = lax.axis_size("seq")
    seg_len = qkv.shape[2]
    length_all = seg_len * seq_count
    rows = stream_lengths.shape[1]
    reach = min(seq_count - 1, -(-(length_all // 2 - 1) // seg_len))
    short_most = rows * length_all // 4 - 3 * length_all // 4 - (rows - 2)
    if not (seq_count == 4 and reach == 2 and 0 < short_most < seg_len):
        return dense_shards(qkv, stream_lengths, doc_lengths, hand_over)

    seq_index = lax.axis_index("seq")
    replica = lax.axis_index("dp")
    partner = jnp.bitwise_xor(replica, 1)
    own_rows = qkv[0]
    doc_ends = jnp.cumsum(doc_lengths[0], axis=1)
    lengths_all = stream_lengths[0]
    local = jnp.arange(seg_len, dtype=jnp.int32)
    query_pos = seq_index * seg_len + local
    key_value_width = KV_HEADS * HD
    far = jnp.int32(4 * length_all)
    own_ends = lax.dynamic_slice_in_dim(doc_ends, 2 * replica, 2, 0)
    own_lengths = lax.dynamic_slice_in_dim(lengths_all, 2 * replica, 2, 0)
    swap_second = own_lengths[1] >= own_lengths[0]

    def pick(first_if, a, b):
        return jnp.where(first_if, a, b)

    long_rows = pick(swap_second, own_rows[1], own_rows[0])
    long_kv = long_rows[:, D:]
    long_pieces = gathered(long_kv, seq_index, seq_count, reach)
    meta = lax.optimization_barrier((jnp.concatenate([lengths_all, hand_over[0]]), long_kv))[0]
    previous = passed_along(meta, "section", 1)
    short_rows = pick(swap_second, own_rows[0], own_rows[1])
    short_rows, previous = lax.optimization_barrier((short_rows, previous))
    short_out = attend_row(
        short_rows[:, :D],
        short_rows[:, D:D + key_value_width],
        short_rows[:, D + key_value_width:],
        query_pos,
        query_pos,
        pick(swap_second, own_ends[0], own_ends[1]),
        pick(swap_second, own_lengths[0], own_lengths[1]),
    )
    short_next = passed_along(short_out, "section", 1)

    long_queries = lax.optimization_barrier((long_rows[:, :D], short_out))[0]
    pieces = [long_kv]
    key_pos = [query_pos]
    for piece, chunk in long_pieces:
        pieces.append(piece)
        key_pos.append(jnp.where(chunk >= 0, chunk * seg_len + local, far))
    kv_all = jnp.concatenate(pieces, axis=0)
    long_out = attend_row(
        long_queries,
        kv_all[:, :key_value_width],
        kv_all[:, key_value_width:],
        query_pos,
        jnp.concatenate(key_pos),
        pick(swap_second, own_ends[1], own_ends[0]),
        pick(swap_second, own_lengths[1], own_lengths[0]),
    )
    long_next = passed_along(long_out, "section", 1)

    previous_lengths = previous[:rows]
    previous_hand = previous[rows:]

    def short_index(rep):
        first = lax.dynamic_index_in_dim(previous_lengths, 2 * rep, 0, keepdims=False)
        second = lax.dynamic_index_in_dim(previous_lengths, 2 * rep + 1, 0, keepdims=False)
        return jnp.where(second >= first, 0, 1)

    own_hand = lax.dynamic_index_in_dim(previous_hand, replica, 0, keepdims=False)
    partner_hand = lax.dynamic_index_in_dim(previous_hand, partner, 0, keepdims=False)
    partner_short = swapped(short_next, "dp", 0)
    partner_long = swapped(long_next, "dp", 0)
    sent = [
        jnp.where(short_index(replica) == 1 - own_hand, short_next, long_next),
        jnp.where(short_index(partner) == partner_hand, partner_short, partner_long),
    ]
    out = jnp.stack(sent, axis=0)
    return out.reshape(1, RPR, seg_len, D)


def solution(mesh):
    return jax.shard_map(
        shards,
        mesh=mesh,
        in_specs=(
            P("section", "dp", "seq", None),
            P("section", None),
            P("section", None, None),
            P("section", None),
        ),
        out_specs=P("section", "dp", "seq", None),
        check_vma=False,
    )
```

```python
import jax
import jax.numpy as jnp
from jax import lax
from jax.sharding import PartitionSpec as P

H = 32
HD = 128
KV_HEADS = 8
D = 4096
RPR = 2


def swapped(block, axis, distance):
    count = lax.axis_size(axis)
    route = []
    for low in range(count):
        high = low | 1 << distance
        if high != low and high < count:
            route += [(low, high), (high, low)]
    return lax.ppermute(block, axis, route)


def passed_along(value, axis, steps):
    count = lax.axis_size(axis)
    pairs = [(source, (source + steps) % count) for source in range(count)]
    return lax.ppermute(value, axis, pairs)


def doc_of(positions, ends):
    return jnp.sum((positions[:, None] >= ends[None, :]).astype(jnp.int32), axis=1)


def attend_row(query_rows, key_rows, value_rows, query_pos, key_pos, ends, length):
    seg_len = query_rows.shape[0]
    key_len = key_rows.shape[0]
    group_size = H // KV_HEADS
    query_doc = doc_of(query_pos, ends)
    key_doc = doc_of(key_pos, ends)
    allowed = (key_pos[None, :] <= query_pos[:, None]) & (key_doc[None, :] == query_doc[:, None])
    queries = query_rows.reshape(seg_len, KV_HEADS, group_size, HD)
    keys = key_rows.reshape(key_len, KV_HEADS, HD)
    values = value_rows.reshape(key_len, KV_HEADS, HD)
    scores = (
        jnp.einsum("qkgd,skd->kgqs", queries, keys, preferred_element_type=jnp.float32)
        * HD ** (-0.5)
    )
    row_top = jnp.max(jnp.where(allowed, scores, -jnp.inf), axis=-1, keepdims=True)
    weights = jnp.where(allowed, jnp.exp(scores - row_top), 0.0)
    row_total = jnp.sum(weights, axis=-1)
    rounded = weights.astype(jnp.bfloat16)
    summed = jnp.einsum("kgqs,skd->qkgd", rounded, values, preferred_element_type=jnp.float32)
    result = summed / jnp.transpose(row_total, (2, 0, 1))[..., None]
    valid = (query_pos < length).astype(jnp.float32)
    result = result * valid[:, None, None, None]
    return result.reshape(seg_len, D).astype(jnp.bfloat16)


def gathered(block, seq_index, seq_count, reach, hold=None):
    if seq_count == 4 and reach == 2:
        over_y = lax.ppermute(block, "seq", [(j, j ^ 2) for j in range(4)])
        odd = seq_index % 2 == 1
        onward = jnp.where(odd, over_y, block)
        if hold is not None:
            onward = lax.optimization_barrier((onward, hold))[0]
        over_x = lax.ppermute(onward, "seq", [(j, j ^ 1) for j in range(4)])
        return [
            (over_y, jnp.bitwise_xor(seq_index, 2)),
            (over_x, jnp.where(odd, seq_index - 1, jnp.bitwise_xor(seq_index, 3))),
        ]
    pieces = []
    for shift in range(1, reach + 1):
        pairs = [(source, source + shift) for source in range(seq_count - shift)]
        pieces.append((lax.ppermute(block, "seq", pairs), seq_index - shift))
    return pieces


def dense_shards(qkv, stream_lengths, doc_lengths, hand_over):
    seq_count = lax.axis_size("seq")
    seq_index = lax.axis_index("seq")
    replica = lax.axis_index("dp")
    partner = jnp.bitwise_xor(replica, 1)
    own_rows = qkv[0]
    seg_len = own_rows.shape[1]
    length_all = seg_len * seq_count
    doc_ends = jnp.cumsum(doc_lengths[0], axis=1)
    lengths_all = stream_lengths[0]
    reach = min(seq_count - 1, -(-(length_all // 2 - 1) // seg_len))
    local = jnp.arange(seg_len, dtype=jnp.int32)
    query_pos = seq_index * seg_len + local
    key_value_width = KV_HEADS * HD
    far = jnp.int32(4 * length_all)

    replicas = lax.axis_size("dp")
    handed = jnp.sum(jnp.where(jnp.arange(replicas) == replica, hand_over[0], 0)) == 1
    own_ends = lax.dynamic_slice_in_dim(doc_ends, 2 * replica, 2, 0)
    own_lengths = lax.dynamic_slice_in_dim(lengths_all, 2 * replica, 2, 0)

    def attend_own(query_rows, kv_local, pieces_and_chunks, first_is_kept):
        pieces = [kv_local]
        key_pos = [query_pos]
        for piece, chunk in pieces_and_chunks:
            pieces.append(piece)
            key_pos.append(jnp.where(chunk >= 0, chunk * seg_len + local, far))
        kv_all = jnp.concatenate(pieces, axis=0)
        key_pos = jnp.concatenate(key_pos)
        ends = jnp.where(first_is_kept, own_ends[0], own_ends[1])
        length = jnp.where(first_is_kept, own_lengths[0], own_lengths[1])
        return attend_row(
            query_rows,
            kv_all[:, :key_value_width],
            kv_all[:, key_value_width:],
            query_pos,
            key_pos,
            ends,
            length,
        )

    kept_kv = jnp.where(handed, own_rows[0, :, D:], own_rows[1, :, D:])
    kept_pieces = gathered(kept_kv, seq_index, seq_count, reach)
    kept_queries = jnp.where(handed, own_rows[0, :, :D], own_rows[1, :, :D])
    kept_out = attend_own(kept_queries, kept_kv, kept_pieces, handed)
    given_kv = jnp.where(handed, own_rows[1, :, D:], own_rows[0, :, D:])
    given_kv = lax.optimization_barrier((given_kv, kept_pieces[0][0]))[0]
    given_pieces = gathered(given_kv, seq_index, seq_count, reach, hold=kept_out)
    sent = [passed_along(kept_out, "section", 1)]
    given_queries = jnp.where(handed, own_rows[1, :, :D], own_rows[0, :, :D])
    given_queries = lax.optimization_barrier((given_queries, kept_out))[0]
    given_out = attend_own(given_queries, given_kv, given_pieces, jnp.logical_not(handed))
    sections = lax.axis_size("section")
    pairs = []
    for section in range(sections):
        for rep in range(replicas):
            pairs.append(
                (section * replicas + rep, (section + 1) % sections * replicas + (rep ^ 1))
            )
    sent.append(lax.ppermute(given_out, ("section", "dp"), pairs))
    out = lax.optimization_barrier(jnp.stack([sent[0], sent[0]], axis=0))
    out = lax.dynamic_update_slice_in_dim(out, sent[1][None], 1, 0)
    return out.reshape(1, RPR, seg_len, D)


def shards(qkv, stream_lengths, doc_lengths, hand_over):
    seq_count = lax.axis_size("seq")
    seg_len = qkv.shape[2]
    length_all = seg_len * seq_count
    rows = stream_lengths.shape[1]
    reach = min(seq_count - 1, -(-(length_all // 2 - 1) // seg_len))
    short_most = rows * length_all // 4 - 3 * length_all // 4 - (rows - 2)
    if not (seq_count == 4 and reach == 2 and 0 < short_most < seg_len):
        return dense_shards(qkv, stream_lengths, doc_lengths, hand_over)

    seq_index = lax.axis_index("seq")
    replica = lax.axis_index("dp")
    partner = jnp.bitwise_xor(replica, 1)
    own_rows = qkv[0]
    doc_ends = jnp.cumsum(doc_lengths[0], axis=1)
    lengths_all = stream_lengths[0]
    local = jnp.arange(seg_len, dtype=jnp.int32)
    query_pos = seq_index * seg_len + local
    key_value_width = KV_HEADS * HD
    far = jnp.int32(4 * length_all)
    own_ends = lax.dynamic_slice_in_dim(doc_ends, 2 * replica, 2, 0)
    own_lengths = lax.dynamic_slice_in_dim(lengths_all, 2 * replica, 2, 0)
    swap_second = own_lengths[1] >= own_lengths[0]

    def pick(first_if, a, b):
        return jnp.where(first_if, a, b)

    short_rows = pick(swap_second, own_rows[0], own_rows[1])
    short_out = attend_row(
        short_rows[:, :D],
        short_rows[:, D:D + key_value_width],
        short_rows[:, D + key_value_width:],
        query_pos,
        query_pos,
        pick(swap_second, own_ends[0], own_ends[1]),
        pick(swap_second, own_lengths[0], own_lengths[1]),
    )
    short_next = passed_along(short_out, "section", 1)

    long_rows = pick(swap_second, own_rows[1], own_rows[0])
    long_kv = long_rows[:, D:]
    long_pieces = gathered(long_kv, seq_index, seq_count, reach)
    meta = lax.optimization_barrier((jnp.concatenate([lengths_all, hand_over[0]]), long_kv))[0]
    previous = passed_along(meta, "section", 1)
    long_queries = lax.optimization_barrier((long_rows[:, :D], short_out))[0]
    pieces = [long_kv]
    key_pos = [query_pos]
    for piece, chunk in long_pieces:
        pieces.append(piece)
        key_pos.append(jnp.where(chunk >= 0, chunk * seg_len + local, far))
    kv_all = jnp.concatenate(pieces, axis=0)
    long_out = attend_row(
        long_queries,
        kv_all[:, :key_value_width],
        kv_all[:, key_value_width:],
        query_pos,
        jnp.concatenate(key_pos),
        pick(swap_second, own_ends[1], own_ends[0]),
        pick(swap_second, own_lengths[1], own_lengths[0]),
    )
    long_out, previous = lax.optimization_barrier((long_out, previous))
    long_next = passed_along(long_out, "section", 1)

    previous_lengths = previous[:rows]
    previous_hand = previous[rows:]

    def short_index(rep):
        first = lax.dynamic_index_in_dim(previous_lengths, 2 * rep, 0, keepdims=False)
        second = lax.dynamic_index_in_dim(previous_lengths, 2 * rep + 1, 0, keepdims=False)
        return jnp.where(second >= first, 0, 1)

    own_hand = lax.dynamic_index_in_dim(previous_hand, replica, 0, keepdims=False)
    partner_hand = lax.dynamic_index_in_dim(previous_hand, partner, 0, keepdims=False)
    partner_short = swapped(short_next, "dp", 0)
    partner_long = swapped(long_next, "dp", 0)
    sent = [
        jnp.where(short_index(replica) == 1 - own_hand, short_next, long_next),
        jnp.where(short_index(partner) == partner_hand, partner_short, partner_long),
    ]
    out = jnp.stack(sent, axis=0)
    return out.reshape(1, RPR, seg_len, D)


def solution(mesh):
    return jax.shard_map(
        shards,
        mesh=mesh,
        in_specs=(
            P("section", "dp", "seq", None),
            P("section", None),
            P("section", None, None),
            P("section", None),
        ),
        out_specs=P("section", "dp", "seq", None),
        check_vma=False,
    )
```

```python
import jax
import jax.numpy as jnp
from jax import lax
from jax.sharding import PartitionSpec as P

H = 32
HD = 128
KV_HEADS = 8
D = 4096
RPR = 2


def swapped(block, axis, distance):
    count = lax.axis_size(axis)
    route = []
    for low in range(count):
        high = low | 1 << distance
        if high != low and high < count:
            route += [(low, high), (high, low)]
    return lax.ppermute(block, axis, route)


def passed_along(value, axis, steps):
    count = lax.axis_size(axis)
    pairs = [(source, (source + steps) % count) for source in range(count)]
    return lax.ppermute(value, axis, pairs)


def doc_of(positions, ends):
    return jnp.sum((positions[:, None] >= ends[None, :]).astype(jnp.int32), axis=1)


def attend_row(query_rows, key_rows, value_rows, query_pos, key_pos, ends, length):
    seg_len = query_rows.shape[0]
    key_len = key_rows.shape[0]
    group_size = H // KV_HEADS
    query_doc = doc_of(query_pos, ends)
    key_doc = doc_of(key_pos, ends)
    allowed = (key_pos[None, :] <= query_pos[:, None]) & (key_doc[None, :] == query_doc[:, None])
    queries = query_rows.reshape(seg_len, KV_HEADS, group_size, HD)
    keys = key_rows.reshape(key_len, KV_HEADS, HD)
    values = value_rows.reshape(key_len, KV_HEADS, HD)
    scores = (
        jnp.einsum("qkgd,skd->kgqs", queries, keys, preferred_element_type=jnp.float32)
        * HD ** (-0.5)
    )
    row_top = jnp.max(jnp.where(allowed, scores, -jnp.inf), axis=-1, keepdims=True)
    weights = jnp.where(allowed, jnp.exp(scores - row_top), 0.0)
    row_total = jnp.sum(weights, axis=-1)
    rounded = weights.astype(jnp.bfloat16)
    summed = jnp.einsum("kgqs,skd->qkgd", rounded, values, preferred_element_type=jnp.float32)
    result = summed / jnp.transpose(row_total, (2, 0, 1))[..., None]
    valid = (query_pos < length).astype(jnp.float32)
    result = result * valid[:, None, None, None]
    return result.reshape(seg_len, D).astype(jnp.bfloat16)


def gathered(block, seq_index, seq_count, reach, hold=None):
    if seq_count == 4 and reach == 2:
        over_y = lax.ppermute(block, "seq", [(j, j ^ 2) for j in range(4)])
        odd = seq_index % 2 == 1
        onward = jnp.where(odd, over_y, block)
        if hold is not None:
            onward = lax.optimization_barrier((onward, hold))[0]
        over_x = lax.ppermute(onward, "seq", [(j, j ^ 1) for j in range(4)])
        return [
            (over_y, jnp.bitwise_xor(seq_index, 2)),
            (over_x, jnp.where(odd, seq_index - 1, jnp.bitwise_xor(seq_index, 3))),
        ]
    pieces = []
    for shift in range(1, reach + 1):
        pairs = [(source, source + shift) for source in range(seq_count - shift)]
        pieces.append((lax.ppermute(block, "seq", pairs), seq_index - shift))
    return pieces


def dense_shards(qkv, stream_lengths, doc_lengths, hand_over):
    seq_count = lax.axis_size("seq")
    seq_index = lax.axis_index("seq")
    replica = lax.axis_index("dp")
    partner = jnp.bitwise_xor(replica, 1)
    own_rows = qkv[0]
    seg_len = own_rows.shape[1]
    length_all = seg_len * seq_count
    doc_ends = jnp.cumsum(doc_lengths[0], axis=1)
    lengths_all = stream_lengths[0]
    reach = min(seq_count - 1, -(-(length_all // 2 - 1) // seg_len))
    local = jnp.arange(seg_len, dtype=jnp.int32)
    query_pos = seq_index * seg_len + local
    key_value_width = KV_HEADS * HD
    far = jnp.int32(4 * length_all)

    replicas = lax.axis_size("dp")
    handed = jnp.sum(jnp.where(jnp.arange(replicas) == replica, hand_over[0], 0)) == 1
    own_ends = lax.dynamic_slice_in_dim(doc_ends, 2 * replica, 2, 0)
    own_lengths = lax.dynamic_slice_in_dim(lengths_all, 2 * replica, 2, 0)

    def attend_own(query_rows, kv_local, pieces_and_chunks, first_is_kept):
        pieces = [kv_local]
        key_pos = [query_pos]
        for piece, chunk in pieces_and_chunks:
            pieces.append(piece)
            key_pos.append(jnp.where(chunk >= 0, chunk * seg_len + local, far))
        kv_all = jnp.concatenate(pieces, axis=0)
        key_pos = jnp.concatenate(key_pos)
        ends = jnp.where(first_is_kept, own_ends[0], own_ends[1])
        length = jnp.where(first_is_kept, own_lengths[0], own_lengths[1])
        return attend_row(
            query_rows,
            kv_all[:, :key_value_width],
            kv_all[:, key_value_width:],
            query_pos,
            key_pos,
            ends,
            length,
        )

    kept_kv = jnp.where(handed, own_rows[0, :, D:], own_rows[1, :, D:])
    kept_pieces = gathered(kept_kv, seq_index, seq_count, reach)
    kept_queries = jnp.where(handed, own_rows[0, :, :D], own_rows[1, :, :D])
    kept_out = attend_own(kept_queries, kept_kv, kept_pieces, handed)
    given_kv = jnp.where(handed, own_rows[1, :, D:], own_rows[0, :, D:])
    given_kv = lax.optimization_barrier((given_kv, kept_pieces[0][0]))[0]
    given_pieces = gathered(given_kv, seq_index, seq_count, reach, hold=kept_out)
    sent = [passed_along(kept_out, "section", 1)]
    given_queries = jnp.where(handed, own_rows[1, :, :D], own_rows[0, :, :D])
    given_queries = lax.optimization_barrier((given_queries, kept_out))[0]
    given_out = attend_own(given_queries, given_kv, given_pieces, jnp.logical_not(handed))
    sections = lax.axis_size("section")
    pairs = []
    for section in range(sections):
        for rep in range(replicas):
            pairs.append(
                (section * replicas + rep, (section + 1) % sections * replicas + (rep ^ 1))
            )
    sent.append(lax.ppermute(given_out, ("section", "dp"), pairs))
    out = lax.optimization_barrier(jnp.stack([sent[0], sent[0]], axis=0))
    out = lax.dynamic_update_slice_in_dim(out, sent[1][None], 1, 0)
    return out.reshape(1, RPR, seg_len, D)


def shards(qkv, stream_lengths, doc_lengths, hand_over):
    seq_count = lax.axis_size("seq")
    seg_len = qkv.shape[2]
    length_all = seg_len * seq_count
    rows = stream_lengths.shape[1]
    reach = min(seq_count - 1, -(-(length_all // 2 - 1) // seg_len))
    short_most = rows * length_all // 4 - 3 * length_all // 4 - (rows - 2)
    if not (seq_count == 4 and reach == 2 and 0 < short_most < seg_len):
        return dense_shards(qkv, stream_lengths, doc_lengths, hand_over)

    seq_index = lax.axis_index("seq")
    replica = lax.axis_index("dp")
    partner = jnp.bitwise_xor(replica, 1)
    own_rows = qkv[0]
    doc_ends = jnp.cumsum(doc_lengths[0], axis=1)
    lengths_all = stream_lengths[0]
    local = jnp.arange(seg_len, dtype=jnp.int32)
    query_pos = seq_index * seg_len + local
    key_value_width = KV_HEADS * HD
    far = jnp.int32(4 * length_all)
    own_ends = lax.dynamic_slice_in_dim(doc_ends, 2 * replica, 2, 0)
    own_lengths = lax.dynamic_slice_in_dim(lengths_all, 2 * replica, 2, 0)
    swap_second = own_lengths[1] >= own_lengths[0]

    def pick(first_if, a, b):
        return jnp.where(first_if, a, b)

    short_rows = pick(swap_second, own_rows[0], own_rows[1])
    short_out = attend_row(
        short_rows[:, :D],
        short_rows[:, D:D + key_value_width],
        short_rows[:, D + key_value_width:],
        query_pos,
        query_pos,
        pick(swap_second, own_ends[0], own_ends[1]),
        pick(swap_second, own_lengths[0], own_lengths[1]),
    )
    short_next = passed_along(short_out, "section", 1)

    long_rows = pick(swap_second, own_rows[1], own_rows[0])
    long_kv = long_rows[:, D:]
    long_pieces = gathered(long_kv, seq_index, seq_count, reach)
    meta = lax.optimization_barrier((jnp.concatenate([lengths_all, hand_over[0]]), short_out))[0]
    previous = passed_along(meta, "section", 1)
    long_queries = lax.optimization_barrier((long_rows[:, :D], short_out))[0]
    pieces = [long_kv]
    key_pos = [query_pos]
    for piece, chunk in long_pieces:
        pieces.append(piece)
        key_pos.append(jnp.where(chunk >= 0, chunk * seg_len + local, far))
    kv_all = jnp.concatenate(pieces, axis=0)
    long_out = attend_row(
        long_queries,
        kv_all[:, :key_value_width],
        kv_all[:, key_value_width:],
        query_pos,
        jnp.concatenate(key_pos),
        pick(swap_second, own_ends[1], own_ends[0]),
        pick(swap_second, own_lengths[1], own_lengths[0]),
    )
    long_out, previous = lax.optimization_barrier((long_out, previous))
    long_next = passed_along(long_out, "section", 1)

    previous_lengths = previous[:rows]
    previous_hand = previous[rows:]

    def short_index(rep):
        first = lax.dynamic_index_in_dim(previous_lengths, 2 * rep, 0, keepdims=False)
        second = lax.dynamic_index_in_dim(previous_lengths, 2 * rep + 1, 0, keepdims=False)
        return jnp.where(second >= first, 0, 1)

    own_hand = lax.dynamic_index_in_dim(previous_hand, replica, 0, keepdims=False)
    partner_hand = lax.dynamic_index_in_dim(previous_hand, partner, 0, keepdims=False)
    partner_short = swapped(short_next, "dp", 0)
    partner_long = swapped(long_next, "dp", 0)
    sent = [
        jnp.where(short_index(replica) == 1 - own_hand, short_next, long_next),
        jnp.where(short_index(partner) == partner_hand, partner_short, partner_long),
    ]
    out = jnp.stack(sent, axis=0)
    return out.reshape(1, RPR, seg_len, D)


def solution(mesh):
    return jax.shard_map(
        shards,
        mesh=mesh,
        in_specs=(
            P("section", "dp", "seq", None),
            P("section", None),
            P("section", None, None),
            P("section", None),
        ),
        out_specs=P("section", "dp", "seq", None),
        check_vma=False,
    )
```

```python
import jax
import jax.numpy as jnp
from jax import lax
from jax.sharding import PartitionSpec as P

H = 32
HD = 128
KV_HEADS = 8
D = 4096
RPR = 2


def swapped(block, axis, distance):
    count = lax.axis_size(axis)
    route = []
    for low in range(count):
        high = low | 1 << distance
        if high != low and high < count:
            route += [(low, high), (high, low)]
    return lax.ppermute(block, axis, route)


def passed_along(value, axis, steps):
    count = lax.axis_size(axis)
    pairs = [(source, (source + steps) % count) for source in range(count)]
    return lax.ppermute(value, axis, pairs)


def doc_of(positions, ends):
    return jnp.sum((positions[:, None] >= ends[None, :]).astype(jnp.int32), axis=1)


def attend_row(query_rows, key_rows, value_rows, query_pos, key_pos, ends, length):
    seg_len = query_rows.shape[0]
    key_len = key_rows.shape[0]
    group_size = H // KV_HEADS
    query_doc = doc_of(query_pos, ends)
    key_doc = doc_of(key_pos, ends)
    allowed = (key_pos[None, :] <= query_pos[:, None]) & (key_doc[None, :] == query_doc[:, None])
    queries = query_rows.reshape(seg_len, KV_HEADS, group_size, HD)
    keys = key_rows.reshape(key_len, KV_HEADS, HD)
    values = value_rows.reshape(key_len, KV_HEADS, HD)
    scores = (
        jnp.einsum("qkgd,skd->kgqs", queries, keys, preferred_element_type=jnp.float32)
        * HD ** (-0.5)
    )
    row_top = jnp.max(jnp.where(allowed, scores, -jnp.inf), axis=-1, keepdims=True)
    weights = jnp.where(allowed, jnp.exp(scores - row_top), 0.0)
    row_total = jnp.sum(weights, axis=-1)
    rounded = weights.astype(jnp.bfloat16)
    summed = jnp.einsum("kgqs,skd->qkgd", rounded, values, preferred_element_type=jnp.float32)
    result = summed / jnp.transpose(row_total, (2, 0, 1))[..., None]
    valid = (query_pos < length).astype(jnp.float32)
    result = result * valid[:, None, None, None]
    return result.reshape(seg_len, D).astype(jnp.bfloat16)


def gathered(block, seq_index, seq_count, reach, hold=None):
    if seq_count == 4 and reach == 2:
        over_y = lax.ppermute(block, "seq", [(j, j ^ 2) for j in range(4)])
        odd = seq_index % 2 == 1
        onward = jnp.where(odd, over_y, block)
        if hold is not None:
            onward = lax.optimization_barrier((onward, hold))[0]
        over_x = lax.ppermute(onward, "seq", [(j, j ^ 1) for j in range(4)])
        return [
            (over_y, jnp.bitwise_xor(seq_index, 2)),
            (over_x, jnp.where(odd, seq_index - 1, jnp.bitwise_xor(seq_index, 3))),
        ]
    pieces = []
    for shift in range(1, reach + 1):
        pairs = [(source, source + shift) for source in range(seq_count - shift)]
        pieces.append((lax.ppermute(block, "seq", pairs), seq_index - shift))
    return pieces


def dense_shards(qkv, stream_lengths, doc_lengths, hand_over):
    seq_count = lax.axis_size("seq")
    seq_index = lax.axis_index("seq")
    replica = lax.axis_index("dp")
    partner = jnp.bitwise_xor(replica, 1)
    own_rows = qkv[0]
    seg_len = own_rows.shape[1]
    length_all = seg_len * seq_count
    doc_ends = jnp.cumsum(doc_lengths[0], axis=1)
    lengths_all = stream_lengths[0]
    reach = min(seq_count - 1, -(-(length_all // 2 - 1) // seg_len))
    local = jnp.arange(seg_len, dtype=jnp.int32)
    query_pos = seq_index * seg_len + local
    key_value_width = KV_HEADS * HD
    far = jnp.int32(4 * length_all)

    replicas = lax.axis_size("dp")
    handed = jnp.sum(jnp.where(jnp.arange(replicas) == replica, hand_over[0], 0)) == 1
    own_ends = lax.dynamic_slice_in_dim(doc_ends, 2 * replica, 2, 0)
    own_lengths = lax.dynamic_slice_in_dim(lengths_all, 2 * replica, 2, 0)

    def attend_own(query_rows, kv_local, pieces_and_chunks, first_is_kept):
        pieces = [kv_local]
        key_pos = [query_pos]
        for piece, chunk in pieces_and_chunks:
            pieces.append(piece)
            key_pos.append(jnp.where(chunk >= 0, chunk * seg_len + local, far))
        kv_all = jnp.concatenate(pieces, axis=0)
        key_pos = jnp.concatenate(key_pos)
        ends = jnp.where(first_is_kept, own_ends[0], own_ends[1])
        length = jnp.where(first_is_kept, own_lengths[0], own_lengths[1])
        return attend_row(
            query_rows,
            kv_all[:, :key_value_width],
            kv_all[:, key_value_width:],
            query_pos,
            key_pos,
            ends,
            length,
        )

    kept_kv = jnp.where(handed, own_rows[0, :, D:], own_rows[1, :, D:])
    kept_pieces = gathered(kept_kv, seq_index, seq_count, reach)
    kept_queries = jnp.where(handed, own_rows[0, :, :D], own_rows[1, :, :D])
    kept_out = attend_own(kept_queries, kept_kv, kept_pieces, handed)
    given_kv = jnp.where(handed, own_rows[1, :, D:], own_rows[0, :, D:])
    given_kv = lax.optimization_barrier((given_kv, kept_pieces[0][0]))[0]
    given_pieces = gathered(given_kv, seq_index, seq_count, reach, hold=kept_out)
    sent = [passed_along(kept_out, "section", 1)]
    given_queries = jnp.where(handed, own_rows[1, :, :D], own_rows[0, :, :D])
    given_queries = lax.optimization_barrier((given_queries, kept_out))[0]
    given_out = attend_own(given_queries, given_kv, given_pieces, jnp.logical_not(handed))
    sections = lax.axis_size("section")
    pairs = []
    for section in range(sections):
        for rep in range(replicas):
            pairs.append(
                (section * replicas + rep, (section + 1) % sections * replicas + (rep ^ 1))
            )
    sent.append(lax.ppermute(given_out, ("section", "dp"), pairs))
    out = lax.optimization_barrier(jnp.stack([sent[0], sent[0]], axis=0))
    out = lax.dynamic_update_slice_in_dim(out, sent[1][None], 1, 0)
    return out.reshape(1, RPR, seg_len, D)


def shards(qkv, stream_lengths, doc_lengths, hand_over):
    seq_count = lax.axis_size("seq")
    seg_len = qkv.shape[2]
    length_all = seg_len * seq_count
    rows = stream_lengths.shape[1]
    reach = min(seq_count - 1, -(-(length_all // 2 - 1) // seg_len))
    short_most = rows * length_all // 4 - 3 * length_all // 4 - (rows - 2)
    if not (seq_count == 4 and reach == 2 and 0 < short_most < seg_len):
        return dense_shards(qkv, stream_lengths, doc_lengths, hand_over)

    seq_index = lax.axis_index("seq")
    replica = lax.axis_index("dp")
    partner = jnp.bitwise_xor(replica, 1)
    own_rows = qkv[0]
    doc_ends = jnp.cumsum(doc_lengths[0], axis=1)
    lengths_all = stream_lengths[0]
    local = jnp.arange(seg_len, dtype=jnp.int32)
    query_pos = seq_index * seg_len + local
    key_value_width = KV_HEADS * HD
    far = jnp.int32(4 * length_all)
    row_ids = jnp.arange(rows)
    own_ends = jnp.stack(
        [jnp.sum(jnp.where((row_ids == 2 * replica + k)[:, None], doc_ends, 0), axis=0) for k in range(2)]
    )
    own_lengths = jnp.stack(
        [jnp.sum(jnp.where(row_ids == 2 * replica + k, lengths_all, 0)) for k in range(2)]
    )
    swap_second = own_lengths[1] >= own_lengths[0]

    def pick(first_if, a, b):
        return jnp.where(first_if, a, b)

    short_rows = pick(swap_second, own_rows[0], own_rows[1])
    short_out = attend_row(
        short_rows[:, :D],
        short_rows[:, D:D + key_value_width],
        short_rows[:, D + key_value_width:],
        query_pos,
        query_pos,
        pick(swap_second, own_ends[0], own_ends[1]),
        pick(swap_second, own_lengths[0], own_lengths[1]),
    )
    short_next = passed_along(short_out, "section", 1)

    long_rows = pick(swap_second, own_rows[1], own_rows[0])
    long_kv = long_rows[:, D:]
    long_pieces = gathered(long_kv, seq_index, seq_count, reach)
    meta = lax.optimization_barrier((jnp.concatenate([lengths_all, hand_over[0]]), long_kv))[0]
    previous = passed_along(meta, "section", 1)
    long_queries = lax.optimization_barrier((long_rows[:, :D], short_out))[0]
    pieces = [long_kv]
    key_pos = [query_pos]
    for piece, chunk in long_pieces:
        pieces.append(piece)
        key_pos.append(jnp.where(chunk >= 0, chunk * seg_len + local, far))
    kv_all = jnp.concatenate(pieces, axis=0)
    long_out = attend_row(
        long_queries,
        kv_all[:, :key_value_width],
        kv_all[:, key_value_width:],
        query_pos,
        jnp.concatenate(key_pos),
        pick(swap_second, own_ends[1], own_ends[0]),
        pick(swap_second, own_lengths[1], own_lengths[0]),
    )
    long_out, previous = lax.optimization_barrier((long_out, previous))
    long_next = passed_along(long_out, "section", 1)

    previous_lengths = previous[:rows]
    previous_hand = previous[rows:]

    def short_index(rep):
        first = lax.dynamic_index_in_dim(previous_lengths, 2 * rep, 0, keepdims=False)
        second = lax.dynamic_index_in_dim(previous_lengths, 2 * rep + 1, 0, keepdims=False)
        return jnp.where(second >= first, 0, 1)

    own_hand = lax.dynamic_index_in_dim(previous_hand, replica, 0, keepdims=False)
    partner_hand = lax.dynamic_index_in_dim(previous_hand, partner, 0, keepdims=False)
    partner_short = swapped(short_next, "dp", 0)
    partner_long = swapped(long_next, "dp", 0)
    sent = [
        jnp.where(short_index(replica) == 1 - own_hand, short_next, long_next),
        jnp.where(short_index(partner) == partner_hand, partner_short, partner_long),
    ]
    out = jnp.stack(sent, axis=0)
    return out.reshape(1, RPR, seg_len, D)


def solution(mesh):
    return jax.shard_map(
        shards,
        mesh=mesh,
        in_specs=(
            P("section", "dp", "seq", None),
            P("section", None),
            P("section", None, None),
            P("section", None),
        ),
        out_specs=P("section", "dp", "seq", None),
        check_vma=False,
    )
```

```python
import jax
import jax.numpy as jnp
from jax import lax
from jax.sharding import PartitionSpec as P

H = 32
HD = 128
KV_HEADS = 8
D = 4096
RPR = 2


def swapped(block, axis, distance):
    count = lax.axis_size(axis)
    route = []
    for low in range(count):
        high = low | 1 << distance
        if high != low and high < count:
            route += [(low, high), (high, low)]
    return lax.ppermute(block, axis, route)


def passed_along(value, axis, steps):
    count = lax.axis_size(axis)
    pairs = [(source, (source + steps) % count) for source in range(count)]
    return lax.ppermute(value, axis, pairs)


def doc_of(positions, ends):
    return jnp.sum((positions[:, None] >= ends[None, :]).astype(jnp.int32), axis=1)


def attend_row(query_rows, key_rows, value_rows, query_pos, key_pos, ends, length):
    seg_len = query_rows.shape[0]
    key_len = key_rows.shape[0]
    group_size = H // KV_HEADS
    query_doc = doc_of(query_pos, ends)
    key_doc = doc_of(key_pos, ends)
    allowed = (key_pos[None, :] <= query_pos[:, None]) & (key_doc[None, :] == query_doc[:, None])
    queries = query_rows.reshape(seg_len, KV_HEADS, group_size, HD)
    keys = key_rows.reshape(key_len, KV_HEADS, HD)
    values = value_rows.reshape(key_len, KV_HEADS, HD)
    scores = (
        jnp.einsum("qkgd,skd->kgqs", queries, keys, preferred_element_type=jnp.float32)
        * HD ** (-0.5)
    )
    row_top = jnp.max(jnp.where(allowed, scores, -jnp.inf), axis=-1, keepdims=True)
    weights = jnp.where(allowed, jnp.exp(scores - row_top), 0.0)
    row_total = jnp.sum(weights, axis=-1)
    rounded = weights.astype(jnp.bfloat16)
    summed = jnp.einsum("kgqs,skd->qkgd", rounded, values, preferred_element_type=jnp.float32)
    result = summed / jnp.transpose(row_total, (2, 0, 1))[..., None]
    valid = (query_pos < length).astype(jnp.float32)
    result = result * valid[:, None, None, None]
    return result.reshape(seg_len, D).astype(jnp.bfloat16)


def gathered(block, seq_index, seq_count, reach, hold=None):
    if seq_count == 4 and reach == 2:
        over_y = lax.ppermute(block, "seq", [(j, j ^ 2) for j in range(4)])
        odd = seq_index % 2 == 1
        onward = jnp.where(odd, over_y, block)
        if hold is not None:
            onward = lax.optimization_barrier((onward, hold))[0]
        over_x = lax.ppermute(onward, "seq", [(j, j ^ 1) for j in range(4)])
        return [
            (over_y, jnp.bitwise_xor(seq_index, 2)),
            (over_x, jnp.where(odd, seq_index - 1, jnp.bitwise_xor(seq_index, 3))),
        ]
    pieces = []
    for shift in range(1, reach + 1):
        pairs = [(source, source + shift) for source in range(seq_count - shift)]
        pieces.append((lax.ppermute(block, "seq", pairs), seq_index - shift))
    return pieces


def dense_shards(qkv, stream_lengths, doc_lengths, hand_over):
    seq_count = lax.axis_size("seq")
    seq_index = lax.axis_index("seq")
    replica = lax.axis_index("dp")
    partner = jnp.bitwise_xor(replica, 1)
    own_rows = qkv[0]
    seg_len = own_rows.shape[1]
    length_all = seg_len * seq_count
    doc_ends = jnp.cumsum(doc_lengths[0], axis=1)
    lengths_all = stream_lengths[0]
    reach = min(seq_count - 1, -(-(length_all // 2 - 1) // seg_len))
    local = jnp.arange(seg_len, dtype=jnp.int32)
    query_pos = seq_index * seg_len + local
    key_value_width = KV_HEADS * HD
    far = jnp.int32(4 * length_all)

    replicas = lax.axis_size("dp")
    handed = jnp.sum(jnp.where(jnp.arange(replicas) == replica, hand_over[0], 0)) == 1
    own_ends = lax.dynamic_slice_in_dim(doc_ends, 2 * replica, 2, 0)
    own_lengths = lax.dynamic_slice_in_dim(lengths_all, 2 * replica, 2, 0)

    def attend_own(query_rows, kv_local, pieces_and_chunks, first_is_kept):
        pieces = [kv_local]
        key_pos = [query_pos]
        for piece, chunk in pieces_and_chunks:
            pieces.append(piece)
            key_pos.append(jnp.where(chunk >= 0, chunk * seg_len + local, far))
        kv_all = jnp.concatenate(pieces, axis=0)
        key_pos = jnp.concatenate(key_pos)
        ends = jnp.where(first_is_kept, own_ends[0], own_ends[1])
        length = jnp.where(first_is_kept, own_lengths[0], own_lengths[1])
        return attend_row(
            query_rows,
            kv_all[:, :key_value_width],
            kv_all[:, key_value_width:],
            query_pos,
            key_pos,
            ends,
            length,
        )

    kept_kv = jnp.where(handed, own_rows[0, :, D:], own_rows[1, :, D:])
    kept_pieces = gathered(kept_kv, seq_index, seq_count, reach)
    kept_queries = jnp.where(handed, own_rows[0, :, :D], own_rows[1, :, :D])
    kept_out = attend_own(kept_queries, kept_kv, kept_pieces, handed)
    given_kv = jnp.where(handed, own_rows[1, :, D:], own_rows[0, :, D:])
    given_kv = lax.optimization_barrier((given_kv, kept_pieces[0][0]))[0]
    given_pieces = gathered(given_kv, seq_index, seq_count, reach, hold=kept_out)
    sent = [passed_along(kept_out, "section", 1)]
    given_queries = jnp.where(handed, own_rows[1, :, :D], own_rows[0, :, :D])
    given_queries = lax.optimization_barrier((given_queries, kept_out))[0]
    given_out = attend_own(given_queries, given_kv, given_pieces, jnp.logical_not(handed))
    sections = lax.axis_size("section")
    pairs = []
    for section in range(sections):
        for rep in range(replicas):
            pairs.append(
                (section * replicas + rep, (section + 1) % sections * replicas + (rep ^ 1))
            )
    sent.append(lax.ppermute(given_out, ("section", "dp"), pairs))
    out = lax.optimization_barrier(jnp.stack([sent[0], sent[0]], axis=0))
    out = lax.dynamic_update_slice_in_dim(out, sent[1][None], 1, 0)
    return out.reshape(1, RPR, seg_len, D)


def shards(qkv, stream_lengths, doc_lengths, hand_over):
    seq_count = lax.axis_size("seq")
    seg_len = qkv.shape[2]
    length_all = seg_len * seq_count
    rows = stream_lengths.shape[1]
    reach = min(seq_count - 1, -(-(length_all // 2 - 1) // seg_len))
    short_most = rows * length_all // 4 - 3 * length_all // 4 - (rows - 2)
    if not (seq_count == 4 and reach == 2 and 0 < short_most < seg_len):
        return dense_shards(qkv, stream_lengths, doc_lengths, hand_over)

    seq_index = lax.axis_index("seq")
    replica = lax.axis_index("dp")
    partner = jnp.bitwise_xor(replica, 1)
    own_rows = qkv[0]
    doc_ends = jnp.cumsum(doc_lengths[0], axis=1)
    lengths_all = stream_lengths[0]
    local = jnp.arange(seg_len, dtype=jnp.int32)
    query_pos = seq_index * seg_len + local
    key_value_width = KV_HEADS * HD
    far = jnp.int32(4 * length_all)
    own_ends = lax.dynamic_slice_in_dim(doc_ends, 2 * replica, 2, 0)
    own_lengths = lax.dynamic_slice_in_dim(lengths_all, 2 * replica, 2, 0)
    swap_second = own_lengths[1] >= own_lengths[0]

    def pick(first_if, a, b):
        return jnp.where(first_if, a, b)

    short_rows = pick(swap_second, own_rows[0], own_rows[1])
    short_out = attend_row(
        short_rows[:, :D],
        short_rows[:, D:D + key_value_width],
        short_rows[:, D + key_value_width:],
        query_pos,
        query_pos,
        pick(swap_second, own_ends[0], own_ends[1]),
        pick(swap_second, own_lengths[0], own_lengths[1]),
    )
    short_next = passed_along(short_out, "section", 1)

    long_rows = pick(swap_second, own_rows[1], own_rows[0])
    long_kv = long_rows[:, D:]
    long_pieces = gathered(long_kv, seq_index, seq_count, reach)
    meta = lax.optimization_barrier((jnp.concatenate([lengths_all, hand_over[0]]), long_kv))[0]
    previous = passed_along(meta, "section", 1)
    long_queries = lax.optimization_barrier((long_rows[:, :D], short_out))[0]
    pieces = [long_kv]
    key_pos = [query_pos]
    for piece, chunk in long_pieces:
        pieces.append(piece)
        key_pos.append(jnp.where(chunk >= 0, chunk * seg_len + local, far))
    kv_all = jnp.concatenate(pieces, axis=0)
    long_out = attend_row(
        long_queries,
        kv_all[:, :key_value_width],
        kv_all[:, key_value_width:],
        query_pos,
        jnp.concatenate(key_pos),
        pick(swap_second, own_ends[1], own_ends[0]),
        pick(swap_second, own_lengths[1], own_lengths[0]),
    )
    long_out, previous = lax.optimization_barrier((long_out, previous))
    long_next = passed_along(long_out, "section", 1)

    previous_lengths = previous[:rows]
    previous_hand = previous[rows:]

    def short_index(rep):
        first = lax.dynamic_index_in_dim(previous_lengths, 2 * rep, 0, keepdims=False)
        second = lax.dynamic_index_in_dim(previous_lengths, 2 * rep + 1, 0, keepdims=False)
        return jnp.where(second >= first, 0, 1)

    own_hand = lax.dynamic_index_in_dim(previous_hand, replica, 0, keepdims=False)
    partner_hand = lax.dynamic_index_in_dim(previous_hand, partner, 0, keepdims=False)
    partner_short = swapped(short_next, "dp", 0)
    partner_long = swapped(long_next, "dp", 0)
    sent = [
        jnp.where(short_index(replica) == 1 - own_hand, short_next, long_next),
        jnp.where(short_index(partner) == partner_hand, partner_short, partner_long),
    ]
    out = lax.optimization_barrier(jnp.stack([sent[0], sent[0]], axis=0))
    out = lax.dynamic_update_slice_in_dim(out, sent[1][None], 1, 0)
    return out.reshape(1, RPR, seg_len, D)


def solution(mesh):
    return jax.shard_map(
        shards,
        mesh=mesh,
        in_specs=(
            P("section", "dp", "seq", None),
            P("section", None),
            P("section", None, None),
            P("section", None),
        ),
        out_specs=P("section", "dp", "seq", None),
        check_vma=False,
    )
```

```python
import jax
import jax.numpy as jnp
from jax import lax
from jax.sharding import PartitionSpec as P

H = 32
HD = 128
KV_HEADS = 8
D = 4096
RPR = 2


def swapped(block, axis, distance):
    count = lax.axis_size(axis)
    route = []
    for low in range(count):
        high = low | 1 << distance
        if high != low and high < count:
            route += [(low, high), (high, low)]
    return lax.ppermute(block, axis, route)


def passed_along(value, axis, steps):
    count = lax.axis_size(axis)
    pairs = [(source, (source + steps) % count) for source in range(count)]
    return lax.ppermute(value, axis, pairs)


def doc_of(positions, ends):
    return jnp.sum((positions[:, None] >= ends[None, :]).astype(jnp.int32), axis=1)


def attend_row(query_rows, key_rows, value_rows, query_pos, key_pos, ends, length):
    seg_len = query_rows.shape[0]
    key_len = key_rows.shape[0]
    group_size = H // KV_HEADS
    query_doc = doc_of(query_pos, ends)
    key_doc = doc_of(key_pos, ends)
    allowed = (key_pos[None, :] <= query_pos[:, None]) & (key_doc[None, :] == query_doc[:, None])
    queries = query_rows.reshape(seg_len, KV_HEADS, group_size, HD)
    keys = key_rows.reshape(key_len, KV_HEADS, HD)
    values = value_rows.reshape(key_len, KV_HEADS, HD)
    scores = (
        jnp.einsum("qkgd,skd->kgqs", queries, keys, preferred_element_type=jnp.float32)
        * HD ** (-0.5)
    )
    row_top = jnp.max(jnp.where(allowed, scores, -jnp.inf), axis=-1, keepdims=True)
    weights = jnp.where(allowed, jnp.exp(scores - row_top), 0.0)
    row_total = jnp.sum(weights, axis=-1)
    rounded = weights.astype(jnp.bfloat16)
    summed = jnp.einsum("kgqs,skd->qkgd", rounded, values, preferred_element_type=jnp.float32)
    result = summed / jnp.transpose(row_total, (2, 0, 1))[..., None]
    valid = (query_pos < length).astype(jnp.float32)
    result = result * valid[:, None, None, None]
    return result.reshape(seg_len, D).astype(jnp.bfloat16)


def gathered(block, seq_index, seq_count, reach, hold=None):
    if seq_count == 4 and reach == 2:
        over_y = lax.ppermute(block, "seq", [(j, j ^ 2) for j in range(4)])
        odd = seq_index % 2 == 1
        onward = jnp.where(odd, over_y, block)
        if hold is not None:
            onward = lax.optimization_barrier((onward, hold))[0]
        over_x = lax.ppermute(onward, "seq", [(j, j ^ 1) for j in range(4)])
        return [
            (over_y, jnp.bitwise_xor(seq_index, 2)),
            (over_x, jnp.where(odd, seq_index - 1, jnp.bitwise_xor(seq_index, 3))),
        ]
    pieces = []
    for shift in range(1, reach + 1):
        pairs = [(source, source + shift) for source in range(seq_count - shift)]
        pieces.append((lax.ppermute(block, "seq", pairs), seq_index - shift))
    return pieces


def dense_shards(qkv, stream_lengths, doc_lengths, hand_over):
    seq_count = lax.axis_size("seq")
    seq_index = lax.axis_index("seq")
    replica = lax.axis_index("dp")
    partner = jnp.bitwise_xor(replica, 1)
    own_rows = qkv[0]
    seg_len = own_rows.shape[1]
    length_all = seg_len * seq_count
    doc_ends = jnp.cumsum(doc_lengths[0], axis=1)
    lengths_all = stream_lengths[0]
    reach = min(seq_count - 1, -(-(length_all // 2 - 1) // seg_len))
    local = jnp.arange(seg_len, dtype=jnp.int32)
    query_pos = seq_index * seg_len + local
    key_value_width = KV_HEADS * HD
    far = jnp.int32(4 * length_all)

    replicas = lax.axis_size("dp")
    handed = jnp.sum(jnp.where(jnp.arange(replicas) == replica, hand_over[0], 0)) == 1
    own_ends = lax.dynamic_slice_in_dim(doc_ends, 2 * replica, 2, 0)
    own_lengths = lax.dynamic_slice_in_dim(lengths_all, 2 * replica, 2, 0)

    def attend_own(query_rows, kv_local, pieces_and_chunks, first_is_kept):
        pieces = [kv_local]
        key_pos = [query_pos]
        for piece, chunk in pieces_and_chunks:
            pieces.append(piece)
            key_pos.append(jnp.where(chunk >= 0, chunk * seg_len + local, far))
        kv_all = jnp.concatenate(pieces, axis=0)
        key_pos = jnp.concatenate(key_pos)
        ends = jnp.where(first_is_kept, own_ends[0], own_ends[1])
        length = jnp.where(first_is_kept, own_lengths[0], own_lengths[1])
        return attend_row(
            query_rows,
            kv_all[:, :key_value_width],
            kv_all[:, key_value_width:],
            query_pos,
            key_pos,
            ends,
            length,
        )

    kept_kv = jnp.where(handed, own_rows[0, :, D:], own_rows[1, :, D:])
    kept_pieces = gathered(kept_kv, seq_index, seq_count, reach)
    kept_queries = jnp.where(handed, own_rows[0, :, :D], own_rows[1, :, :D])
    kept_out = attend_own(kept_queries, kept_kv, kept_pieces, handed)
    given_kv = jnp.where(handed, own_rows[1, :, D:], own_rows[0, :, D:])
    given_kv = lax.optimization_barrier((given_kv, kept_pieces[0][0]))[0]
    given_pieces = gathered(given_kv, seq_index, seq_count, reach, hold=kept_out)
    sent = [passed_along(kept_out, "section", 1)]
    given_queries = jnp.where(handed, own_rows[1, :, :D], own_rows[0, :, :D])
    given_queries = lax.optimization_barrier((given_queries, kept_out))[0]
    given_out = attend_own(given_queries, given_kv, given_pieces, jnp.logical_not(handed))
    sections = lax.axis_size("section")
    pairs = []
    for section in range(sections):
        for rep in range(replicas):
            pairs.append(
                (section * replicas + rep, (section + 1) % sections * replicas + (rep ^ 1))
            )
    sent.append(lax.ppermute(given_out, ("section", "dp"), pairs))
    out = lax.optimization_barrier(jnp.stack([sent[0], sent[0]], axis=0))
    out = lax.dynamic_update_slice_in_dim(out, sent[1][None], 1, 0)
    return out.reshape(1, RPR, seg_len, D)


def shards(qkv, stream_lengths, doc_lengths, hand_over):
    seq_count = lax.axis_size("seq")
    seg_len = qkv.shape[2]
    length_all = seg_len * seq_count
    rows = stream_lengths.shape[1]
    reach = min(seq_count - 1, -(-(length_all // 2 - 1) // seg_len))
    short_most = rows * length_all // 4 - 3 * length_all // 4 - (rows - 2)
    if not (seq_count == 4 and reach == 2 and 0 < short_most < seg_len):
        return dense_shards(qkv, stream_lengths, doc_lengths, hand_over)

    seq_index = lax.axis_index("seq")
    replica = lax.axis_index("dp")
    partner = jnp.bitwise_xor(replica, 1)
    own_rows = qkv[0]
    doc_ends = jnp.cumsum(doc_lengths[0], axis=1)
    lengths_all = stream_lengths[0]
    local = jnp.arange(seg_len, dtype=jnp.int32)
    query_pos = seq_index * seg_len + local
    key_value_width = KV_HEADS * HD
    far = jnp.int32(4 * length_all)
    own_ends = lax.dynamic_slice_in_dim(doc_ends, 2 * replica, 2, 0)
    own_lengths = lax.dynamic_slice_in_dim(lengths_all, 2 * replica, 2, 0)
    swap_second = own_lengths[1] >= own_lengths[0]

    def pick(first_if, a, b):
        return jnp.where(first_if, a, b)

    def short_part(lo, hi):
        return pick(swap_second, own_rows[0, :, lo:hi], own_rows[1, :, lo:hi])

    short_out = attend_row(
        short_part(0, D),
        short_part(D, D + key_value_width),
        short_part(D + key_value_width, D + 2 * key_value_width),
        query_pos,
        query_pos,
        pick(swap_second, own_ends[0], own_ends[1]),
        pick(swap_second, own_lengths[0], own_lengths[1]),
    )
    short_next = passed_along(short_out, "section", 1)

    long_rows = pick(swap_second, own_rows[1], own_rows[0])
    long_kv = long_rows[:, D:]
    long_pieces = gathered(long_kv, seq_index, seq_count, reach)
    meta = lax.optimization_barrier((jnp.concatenate([lengths_all, hand_over[0]]), long_kv))[0]
    previous = passed_along(meta, "section", 1)
    long_queries = lax.optimization_barrier((long_rows[:, :D], short_out))[0]
    pieces = [long_kv]
    key_pos = [query_pos]
    for piece, chunk in long_pieces:
        pieces.append(piece)
        key_pos.append(jnp.where(chunk >= 0, chunk * seg_len + local, far))
    kv_all = jnp.concatenate(pieces, axis=0)
    long_out = attend_row(
        long_queries,
        kv_all[:, :key_value_width],
        kv_all[:, key_value_width:],
        query_pos,
        jnp.concatenate(key_pos),
        pick(swap_second, own_ends[1], own_ends[0]),
        pick(swap_second, own_lengths[1], own_lengths[0]),
    )
    long_out, previous = lax.optimization_barrier((long_out, previous))
    long_next = passed_along(long_out, "section", 1)

    previous_lengths = previous[:rows]
    previous_hand = previous[rows:]

    def short_index(rep):
        first = lax.dynamic_index_in_dim(previous_lengths, 2 * rep, 0, keepdims=False)
        second = lax.dynamic_index_in_dim(previous_lengths, 2 * rep + 1, 0, keepdims=False)
        return jnp.where(second >= first, 0, 1)

    own_hand = lax.dynamic_index_in_dim(previous_hand, replica, 0, keepdims=False)
    partner_hand = lax.dynamic_index_in_dim(previous_hand, partner, 0, keepdims=False)
    partner_short = swapped(short_next, "dp", 0)
    partner_long = swapped(long_next, "dp", 0)
    sent = [
        jnp.where(short_index(replica) == 1 - own_hand, short_next, long_next),
        jnp.where(short_index(partner) == partner_hand, partner_short, partner_long),
    ]
    out = lax.optimization_barrier(jnp.stack([sent[0], sent[0]], axis=0))
    out = lax.dynamic_update_slice_in_dim(out, sent[1][None], 1, 0)
    return out.reshape(1, RPR, seg_len, D)


def solution(mesh):
    return jax.shard_map(
        shards,
        mesh=mesh,
        in_specs=(
            P("section", "dp", "seq", None),
            P("section", None),
            P("section", None, None),
            P("section", None),
        ),
        out_specs=P("section", "dp", "seq", None),
        check_vma=False,
    )
```
